32 devices in a mesh: groups: 2 (over y), space: 8 (over z, x), tm: 2 (over core).
Axes of the slice: x: 2, y: 2, z: 4, core: 2. Of those that a mesh axis runs over, the one named last changes fastest.
Arguments:
- latents: bfloat16 [4, 16, 4, 256, 256], P('groups', 'space', 'tm'), parts along dimension 0, may hold values from -6 to 6
- cotangent: bfloat16 [4, 16, 4, 256, 256], P('groups', 'space', 'tm'), parts along dimension 0, may hold values from -6 to 6
- valid_frames: int32 [4], P('groups'), parts along dimension 0, may hold values from 1 to 16, as said below
- spatial_weight: bfloat16 [9, 256, 256], replicated, may hold values from -0.125 to 0.125
- temporal_weight: bfloat16 [3, 256, 256], replicated, may hold values from -0.21875 to 0.21875
- cond_weight: bfloat16 [256, 256], replicated, may hold values from -0.375 to 0.375
Outputs:
- output: bfloat16 [4, 16, 4, 256, 256], P('groups', 'space', 'tm'), parts along dimension 0
- grad_latents: bfloat16 [4, 16, 4, 256, 256], P('groups', 'space', 'tm'), parts along dimension 0
- grad_spatial: bfloat16 [18, 256, 256], P('groups'), parts along dimension 0
- grad_temporal: bfloat16 [6, 256, 256], P('groups'), parts along dimension 0
- grad_cond: bfloat16 [512, 256], P('groups'), parts along dimension 0
The draws below stay inside these ranges and needn't reach their ends.
There are 2 independent parts, one for each index of `groups`. The reference program is written for one: setup_inputs(seed, part) draws one part's arguments, and reference() takes and returns one part's arrays. A program takes and returns all parts, laid end to end along the dimension named above; an argument that names none is the same for every part. Nothing has to cross between parts.
Inputs may be any that keep to these rules, and one draw needn't show every extreme that they name: `valid_frames`: the first clip has all 16 frames valid; the others have 1 to 16.
All inputs are finite; a program needn't handle non-finite values.
Results may differ from the reference program's by a relative error of at most 0.0055.
Values may be sent and summed in bfloat16 or wider, within the bound.
No kernel may reach another device: no remote copies, remote signals or barrier semaphores. Data moves between devices by JAX's collectives and lax.ppermute only.
A program may use at most 128 MiB of HBM per device.

```python
import jax
import jax.numpy as jnp
from jax import lax

C = 256
CLIPS = 2
WIDTH = 256
FRAMES = 16
HEIGHT = 4


def draw_valid_frames(key, part):
    lengths = jax.random.randint(key, (CLIPS,), 1, FRAMES + 1)
    return jnp.where(jnp.arange(CLIPS) == 0, FRAMES, lengths).astype(jnp.int32)


def levels(own_key, shape, split, low, high):
    def one(dim, shards_of):
        draws = jax.random.uniform(jax.random.fold_in(jax.random.fold_in(own_key, 6), dim), (shards_of,), jnp.float32, low / len(split), high / len(split))
        return jnp.repeat(jnp.exp(draws), shape[dim] // shards_of).reshape((-1,) + (1,) * (len(shape) - dim - 1))

    factor_of = one(*split[0])
    for cut in split[1:]:
        factor_of = factor_of * one(*cut)
    return factor_of


def bell_draw(key, extent, scale, bound, cuts=(), kind=jnp.bfloat16):
    drawn = jax.random.normal(key, extent, jnp.float32) * scale
    if len(cuts) > 0:
        drawn = levels(key, extent, cuts, -0.22, 0.18) * drawn
    return jnp.clip(drawn, min=-bound, max=bound).astype(kind)


def setup_inputs(seed: int = 0, part: int = 0) -> dict:
    key_list = jax.random.split(jax.random.key(seed), 7)
    part_keys = jax.random.split(jax.random.fold_in(key_list[6], part), 7)
    return {
        "latents": bell_draw(part_keys[0], (CLIPS, FRAMES, HEIGHT, WIDTH, C), 1.0, 6.0, ((1, 8), (2, 2))),
        "cotangent": bell_draw(part_keys[1], (CLIPS, FRAMES, HEIGHT, WIDTH, C), 1.0, 6.0, ((1, 8), (2, 2))),
        "valid_frames": draw_valid_frames(jax.random.fold_in(jax.random.fold_in(key_list[6], part), 71), part),
        "spatial_weight": bell_draw(key_list[3], (9, C, C), (9 * C) ** -0.5, 0.125),
        "temporal_weight": bell_draw(key_list[4], (3, C, C), (3 * C) ** -0.5, 0.21875),
        "cond_weight": bell_draw(key_list[5], (C, C), C ** -0.5, 0.375),
    }


def spatial_sum(padded, weights, flip):
    rows = padded.shape[2] - 2
    cols = padded.shape[3] - 2
    total = jnp.zeros(padded.shape[:2] + (rows, cols, weights.shape[2]), jnp.float32)
    for row_off in range(3):
        for col_off in range(3):
            if flip:
                piece = padded[:, :, 2 - row_off:2 - row_off + rows, 2 - col_off:2 - col_off + cols]
                kernel = weights[3 * row_off + col_off].T
            else:
                piece = padded[:, :, row_off:row_off + rows, col_off:col_off + cols]
                kernel = weights[3 * row_off + col_off]
            total = total + jnp.dot(piece, kernel, preferred_element_type=jnp.float32)
    return total


def reference(latents, cotangent, valid_frames, spatial_weight, temporal_weight, cond_weight):
    frame_ids = jnp.arange(FRAMES, dtype=jnp.int32)
    mask = (frame_ids[None, :] < valid_frames[:, None]).astype(jnp.bfloat16)[:, :, None, None, None]
    masked = latents * mask
    padded = jnp.pad(masked, ((0, 0), (0, 0), (1, 1), (1, 1), (0, 0)))
    pre = spatial_sum(padded, spatial_weight, False)
    act = jax.nn.silu(pre).astype(jnp.bfloat16)
    act_pad = jnp.pad(act, ((0, 0), (2, 0), (0, 0), (0, 0), (0, 0)))
    mixed = jnp.zeros(pre.shape, jnp.float32)
    for lag in range(3):
        mixed = mixed + jnp.dot(act_pad[:, 2 - lag:2 - lag + FRAMES], temporal_weight[lag], preferred_element_type=jnp.float32)
    cond = jnp.dot(masked[:, 0], cond_weight, preferred_element_type=jnp.float32)
    output = ((masked.astype(jnp.float32) + mixed + cond[:, None]) * mask.astype(jnp.float32)).astype(jnp.bfloat16)

    cot = cotangent * mask
    cot_pad = jnp.pad(cot, ((0, 0), (0, 2), (0, 0), (0, 0), (0, 0)))
    dact = jnp.zeros(pre.shape, jnp.float32)
    for lag in range(3):
        dact = dact + jnp.dot(cot_pad[:, lag:lag + FRAMES], temporal_weight[lag].T, preferred_element_type=jnp.float32)
    sig = jax.nn.sigmoid(pre)
    dpre = (dact * sig * (1.0 + pre * (1.0 - sig))).astype(jnp.bfloat16)
    cot_sum = jnp.sum(cot.astype(jnp.float32), axis=1)
    cond_back = jnp.dot(cot_sum, cond_weight.astype(jnp.float32).T, precision=lax.Precision.HIGHEST)
    dpre_pad = jnp.pad(dpre, ((0, 0), (0, 0), (1, 1), (1, 1), (0, 0)))
    dmasked = spatial_sum(dpre_pad, spatial_weight, True)
    first = (frame_ids == 0).astype(jnp.float32)[None, :, None, None, None]
    grad_latents = ((cot.astype(jnp.float32) + dmasked + first * cond_back[:, None]) * mask.astype(jnp.float32)).astype(jnp.bfloat16)

    scale = (CLIPS * FRAMES * HEIGHT * WIDTH) ** -0.5
    dims = (((0, 1, 2, 3), (0, 1, 2, 3)), ((), ()))
    spatial_terms = []
    for row_off in range(3):
        for col_off in range(3):
            piece = padded[:, :, row_off:row_off + HEIGHT, col_off:col_off + WIDTH]
            spatial_terms.append(lax.dot_general(piece, dpre, dims, preferred_element_type=jnp.float32))
    grad_spatial = (jnp.stack(spatial_terms) * scale).astype(jnp.bfloat16)
    temporal_terms = []
    for lag in range(3):
        temporal_terms.append(lax.dot_general(act_pad[:, 2 - lag:2 - lag + FRAMES], cot, dims, preferred_element_type=jnp.float32))
    grad_temporal = (jnp.stack(temporal_terms) * scale).astype(jnp.bfloat16)
    grad_cond = lax.dot_general(masked[:, 0].astype(jnp.float32), cot_sum, (((0, 1, 2), (0, 1, 2)), ((), ())), precision=lax.Precision.HIGHEST)
    grad_cond = (grad_cond * scale).astype(jnp.bfloat16)
    return output, grad_latents, grad_spatial, grad_temporal, grad_cond
```

```python
import jax
import jax.numpy as jnp
from jax import lax
from jax.sharding import PartitionSpec as P


def shifted(value, axis, by):
    count = lax.axis_size(axis)
    pairs = [(i, i + by) for i in range(count) if 0 <= i + by < count]
    return lax.ppermute(value, axis, pairs)


def tree_broadcast(value, axis):
    count = lax.axis_size(axis)
    me = lax.axis_index(axis)
    step = 1
    while step * 2 < count:
        step *= 2
    while step >= 1 and count > 1:
        pairs = [(i, i + step) for i in range(0, count, 2 * step) if i + step < count]
        got = lax.ppermute(value, axis, pairs)
        value = jnp.where(me % (2 * step) == step, got, value)
        step //= 2
    return value


def tree_reduce(value, axis):
    count = lax.axis_size(axis)
    step = 1
    while step < count:
        pairs = [(i + step, i) for i in range(0, count, 2 * step) if i + step < count]
        value = value + lax.ppermute(value, axis, pairs)
        step *= 2
    return value


def halving_sum(flat, axis):
    count = lax.axis_size(axis)
    me = lax.axis_index(axis)
    step = count // 2
    while step >= 1:
        half = flat.shape[0] // 2
        upper = (me // step) % 2
        keep = lax.dynamic_slice_in_dim(flat, upper * half, half, 0)
        send = lax.dynamic_slice_in_dim(flat, (1 - upper) * half, half, 0)
        pairs = [(i, i ^ step) for i in range(count)]
        flat = keep + lax.ppermute(send, axis, pairs)
        step //= 2
    return flat


def doubling_gather(piece, axis):
    count = lax.axis_size(axis)
    me = lax.axis_index(axis)
    step = 1
    while step < count:
        got = lax.ppermute(piece, axis, [(i, i ^ step) for i in range(count)])
        upper = (me // step) % 2 == 1
        piece = jnp.where(
            upper, jnp.concatenate([got, piece], 0), jnp.concatenate([piece, got], 0)
        )
        step *= 2
    return piece


def is_pow2(n):
    return n >= 1 and (n & (n - 1)) == 0


def all_sum_rounded(flat, axes, scale):
    sizes = [lax.axis_size(a) for a in axes]
    if not all(is_pow2(s) for s in sizes):
        return (lax.psum(flat, tuple(axes)) * scale).astype(jnp.bfloat16)
    parts = 1
    for s in sizes:
        parts *= s
    rows = flat.shape[0]
    unit = parts * 8
    padded_rows = -(-rows // unit) * unit
    if padded_rows != rows:
        flat = jnp.pad(flat, ((0, padded_rows - rows), (0, 0)))
    for a in axes:
        flat = halving_sum(flat, a)
    piece = (flat * scale).astype(jnp.bfloat16)
    for a in reversed(axes):
        piece = doubling_gather(piece, a)
    return piece[:rows]


def spatial_sum(padded, weights, flip):
    rows = padded.shape[2] - 2
    cols = padded.shape[3] - 2
    total = jnp.zeros(padded.shape[:2] + (rows, cols, weights.shape[2]), jnp.float32)
    for row_off in range(3):
        for col_off in range(3):
            if flip:
                piece = padded[
                    :, :, 2 - row_off : 2 - row_off + rows, 2 - col_off : 2 - col_off + cols
                ]
                kernel = weights[3 * row_off + col_off].T
            else:
                piece = padded[:, :, row_off : row_off + rows, col_off : col_off + cols]
                kernel = weights[3 * row_off + col_off]
            total = total + jnp.dot(piece, kernel, preferred_element_type=jnp.float32)
    return total


def lag_forward(padded_act, weights, count):
    total = 0.0
    for lag in range(3):
        total = total + jnp.dot(
            padded_act[:, 2 - lag : 2 - lag + count],
            weights[lag],
            preferred_element_type=jnp.float32,
        )
    return total


def lag_backward(padded_cot, weights, count):
    total = 0.0
    for lag in range(3):
        total = total + jnp.dot(
            padded_cot[:, lag : lag + count], weights[lag].T, preferred_element_type=jnp.float32
        )
    return total


def lag_grads(padded_act, cot, count):
    dims = (((0, 1, 2, 3), (0, 1, 2, 3)), ((), ()))
    terms = []
    for lag in range(3):
        terms.append(
            lax.dot_general(
                padded_act[:, 2 - lag : 2 - lag + count],
                cot,
                dims,
                preferred_element_type=jnp.float32,
            )
        )
    return jnp.stack(terms)


def row_halo(x):
    above = shifted(x[:, :, -1:], "tm", 1)
    below = shifted(x[:, :, :1], "tm", -1)
    return jnp.concatenate([above, x, below], axis=2)


def on_device(latents, cotangent, valid_frames, spatial_weight, temporal_weight, cond_weight):
    clips, frames, rows, cols, chans = latents.shape
    slab = lax.axis_index("space")
    frame_ids = slab * frames + jnp.arange(frames, dtype=jnp.int32)
    mask = (frame_ids[None, :] < valid_frames[:, None]).astype(jnp.bfloat16)[:, :, None, None, None]
    mask_f = mask.astype(jnp.float32)
    masked = latents * mask
    cot = cotangent * mask
    first = tree_broadcast(masked[:, 0], "space")
    cot_local = jnp.sum(cot, axis=1, dtype=jnp.float32)
    cot_sum = tree_reduce(cot_local, "space")
    later = shifted(cot, "space", -1)
    rows_pad = row_halo(masked)
    padded = jnp.pad(rows_pad, ((0, 0), (0, 0), (0, 0), (1, 1), (0, 0)))
    pre = spatial_sum(padded, spatial_weight, False)
    act = jax.nn.silu(pre).astype(jnp.bfloat16)
    earlier = shifted(act, "space", 1)
    act_pad = jnp.concatenate([earlier, act], axis=1)
    mixed = lag_forward(act_pad, temporal_weight, frames)
    cot_pad = jnp.concatenate([cot, later], axis=1)
    dact = lag_backward(cot_pad, temporal_weight, frames)
    temporal_terms = lag_grads(act_pad, cot, frames)
    cond = jnp.dot(first, cond_weight, preferred_element_type=jnp.float32)
    output = ((masked.astype(jnp.float32) + mixed + cond[:, None]) * mask_f).astype(jnp.bfloat16)
    sig = jax.nn.sigmoid(pre)
    dpre = (dact * sig * (1.0 + pre * (1.0 - sig))).astype(jnp.bfloat16)
    cond_back = jnp.dot(cot_sum, cond_weight.astype(jnp.float32).T, precision=lax.Precision.HIGHEST)
    dpre_rows = row_halo(dpre)
    dpre_pad = jnp.pad(dpre_rows, ((0, 0), (0, 0), (0, 0), (1, 1), (0, 0)))
    dmasked = spatial_sum(dpre_pad, spatial_weight, True)
    is_first = (frame_ids == 0).astype(jnp.float32)[None, :, None, None, None]
    grad_latents = (
        (cot.astype(jnp.float32) + dmasked + is_first * cond_back[:, None]) * mask_f
    ).astype(jnp.bfloat16)
    dims = (((0, 1, 2, 3), (0, 1, 2, 3)), ((), ()))
    spatial_terms = []
    for row_off in range(3):
        for col_off in range(3):
            piece = padded[:, :, row_off : row_off + rows, col_off : col_off + cols]
            spatial_terms.append(
                lax.dot_general(piece, dpre, dims, preferred_element_type=jnp.float32)
            )
    spatial_terms = jnp.stack(spatial_terms)
    cond_terms = lax.dot_general(
        first.astype(jnp.float32),
        cot_local,
        (((0, 1, 2), (0, 1, 2)), ((), ())),
        precision=lax.Precision.HIGHEST,
    )
    taps_s = spatial_terms.shape[0]
    taps_t = temporal_terms.shape[0]
    flat = jnp.concatenate(
        [
            spatial_terms.reshape(-1, chans),
            temporal_terms.reshape(-1, chans),
            cond_terms.reshape(-1, chans),
        ],
        axis=0,
    )
    scale = (clips * frames * rows * cols * lax.axis_size("space") * lax.axis_size("tm")) ** (-0.5)
    summed = all_sum_rounded(flat, ("tm", "space"), scale)
    n_s = taps_s * chans
    n_t = taps_t * chans
    grad_spatial = summed[:n_s].reshape(taps_s, chans, chans)
    grad_temporal = summed[n_s : n_s + n_t].reshape(taps_t, chans, chans)
    grad_cond = summed[n_s + n_t :]
    return (output, grad_latents, grad_spatial, grad_temporal, grad_cond)


def solution(mesh):
    return jax.shard_map(
        on_device,
        mesh=mesh,
        in_specs=(
            P("groups", "space", "tm", None, None),
            P("groups", "space", "tm", None, None),
            P("groups"),
            P(),
            P(),
            P(),
        ),
        out_specs=(
            P("groups", "space", "tm", None, None),
            P("groups", "space", "tm", None, None),
            P("groups", None, None),
            P("groups", None, None),
            P("groups", None),
        ),
        check_vma=False,
    )
```

```python
import jax
import jax.numpy as jnp
from jax import lax
from jax.sharding import PartitionSpec as P


def shifted(value, axis, by):
    count = lax.axis_size(axis)
    pairs = [(i, i + by) for i in range(count) if 0 <= i + by < count]
    return lax.ppermute(value, axis, pairs)


def tree_broadcast(value, axis):
    count = lax.axis_size(axis)
    me = lax.axis_index(axis)
    step = 1
    while step * 2 < count:
        step *= 2
    while step >= 1 and count > 1:
        pairs = [(i, i + step) for i in range(0, count, 2 * step) if i + step < count]
        got = lax.ppermute(value, axis, pairs)
        value = jnp.where(me % (2 * step) == step, got, value)
        step //= 2
    return value


def tree_reduce(value, axis):
    count = lax.axis_size(axis)
    step = 1
    while step < count:
        pairs = [(i + step, i) for i in range(0, count, 2 * step) if i + step < count]
        value = value + lax.ppermute(value, axis, pairs)
        step *= 2
    return value


def xor_halving(flat, axis, steps):
    me = lax.axis_index(axis)
    count = lax.axis_size(axis)
    for step in steps:
        half = flat.shape[0] // 2
        upper = (me // step) % 2
        keep = lax.dynamic_slice_in_dim(flat, upper * half, half, 0)
        send = lax.dynamic_slice_in_dim(flat, (1 - upper) * half, half, 0)
        pairs = [(i, i ^ step) for i in range(count)]
        flat = keep + lax.ppermute(send, axis, pairs)
    return flat


def xor_doubling(piece, axis, steps):
    me = lax.axis_index(axis)
    count = lax.axis_size(axis)
    for step in reversed(steps):
        got = lax.ppermute(piece, axis, [(i, i ^ step) for i in range(count)])
        upper = (me // step) % 2 == 1
        piece = jnp.where(
            upper, jnp.concatenate([got, piece], 0), jnp.concatenate([piece, got], 0)
        )
    return piece


def direct_scatter(flat, axis, low, high):
    me = lax.axis_index(axis)
    j = me // low
    blk = flat.shape[0] // high
    total = lax.dynamic_slice_in_dim(flat, j * blk, blk, 0)
    for d in range(1, high):
        send = lax.dynamic_slice_in_dim(flat, ((j + d) % high) * blk, blk, 0)
        pairs = [
            (a * low + b, ((a + d) % high) * low + b) for a in range(high) for b in range(low)
        ]
        total = total + lax.ppermute(send, axis, pairs)
    return total


def direct_gather(piece, axis, low, high):
    me = lax.axis_index(axis)
    j = me // low
    out = jnp.zeros((high,) + piece.shape, piece.dtype)
    out = lax.dynamic_update_index_in_dim(out, piece, j, 0)
    for d in range(1, high):
        pairs = [
            (a * low + b, ((a + d) % high) * low + b) for a in range(high) for b in range(low)
        ]
        got = lax.ppermute(piece, axis, pairs)
        out = lax.dynamic_update_index_in_dim(out, got, (j - d) % high, 0)
    return out.reshape((-1,) + piece.shape[1:])


def is_pow2(n):
    return n >= 1 and (n & (n - 1)) == 0


def all_sum_rounded(flat, scale):
    n_tm = lax.axis_size("tm")
    n_sp = lax.axis_size("space")
    if not (is_pow2(n_tm) and is_pow2(n_sp)):
        return (lax.psum(flat, ("tm", "space")) * scale).astype(jnp.bfloat16)
    high = min(4, n_sp)
    low = n_sp // high
    tm_steps = []
    s = 1
    while s < n_tm:
        tm_steps.append(s)
        s *= 2
    sp_steps = []
    s = 1
    while s < low:
        sp_steps.append(s)
        s *= 2
    rows = flat.shape[0]
    unit = n_tm * n_sp * 8
    padded_rows = -(-rows // unit) * unit
    if padded_rows != rows:
        flat = jnp.pad(flat, ((0, padded_rows - rows), (0, 0)))
    flat = xor_halving(flat, "tm", tm_steps)
    flat = xor_halving(flat, "space", sp_steps)
    flat = direct_scatter(flat, "space", low, high)
    piece = (flat * scale).astype(jnp.bfloat16)
    piece = direct_gather(piece, "space", low, high)
    piece = xor_doubling(piece, "space", sp_steps)
    piece = xor_doubling(piece, "tm", tm_steps)
    return piece[:rows]


def spatial_sum(padded, weights, flip):
    rows = padded.shape[2] - 2
    cols = padded.shape[3] - 2
    total = jnp.zeros(padded.shape[:2] + (rows, cols, weights.shape[2]), jnp.float32)
    for row_off in range(3):
        for col_off in range(3):
            if flip:
                piece = padded[
                    :, :, 2 - row_off : 2 - row_off + rows, 2 - col_off : 2 - col_off + cols
                ]
                kernel = weights[3 * row_off + col_off].T
            else:
                piece = padded[:, :, row_off : row_off + rows, col_off : col_off + cols]
                kernel = weights[3 * row_off + col_off]
            total = total + jnp.dot(piece, kernel, preferred_element_type=jnp.float32)
    return total


def lag_forward(padded_act, weights, count):
    total = 0.0
    for lag in range(3):
        total = total + jnp.dot(
            padded_act[:, 2 - lag : 2 - lag + count],
            weights[lag],
            preferred_element_type=jnp.float32,
        )
    return total


def lag_backward(padded_cot, weights, count):
    total = 0.0
    for lag in range(3):
        total = total + jnp.dot(
            padded_cot[:, lag : lag + count], weights[lag].T, preferred_element_type=jnp.float32
        )
    return total


def lag_grads(padded_act, cot, count):
    dims = (((0, 1, 2, 3), (0, 1, 2, 3)), ((), ()))
    terms = []
    for lag in range(3):
        terms.append(
            lax.dot_general(
                padded_act[:, 2 - lag : 2 - lag + count],
                cot,
                dims,
                preferred_element_type=jnp.float32,
            )
        )
    return jnp.stack(terms)


def row_halo(x):
    above = shifted(x[:, :, -1:], "tm", 1)
    below = shifted(x[:, :, :1], "tm", -1)
    return jnp.concatenate([above, x, below], axis=2)


def on_device(latents, cotangent, valid_frames, spatial_weight, temporal_weight, cond_weight):
    clips, frames, rows, cols, chans = latents.shape
    slab = lax.axis_index("space")
    frame_ids = slab * frames + jnp.arange(frames, dtype=jnp.int32)
    mask = (frame_ids[None, :] < valid_frames[:, None]).astype(jnp.bfloat16)[:, :, None, None, None]
    mask_f = mask.astype(jnp.float32)
    masked = latents * mask
    cot = cotangent * mask
    first = tree_broadcast(masked[:, 0], "space")
    cot_local = jnp.sum(cot, axis=1, dtype=jnp.float32)
    cot_sum = tree_reduce(cot_local, "space")
    later = shifted(cot, "space", -1)
    rows_pad = row_halo(masked)
    padded = jnp.pad(rows_pad, ((0, 0), (0, 0), (0, 0), (1, 1), (0, 0)))
    pre = spatial_sum(padded, spatial_weight, False)
    act = jax.nn.silu(pre).astype(jnp.bfloat16)
    earlier = shifted(act, "space", 1)
    act_pad = jnp.concatenate([earlier, act], axis=1)
    mixed = lag_forward(act_pad, temporal_weight, frames)
    cot_pad = jnp.concatenate([cot, later], axis=1)
    dact = lag_backward(cot_pad, temporal_weight, frames)
    temporal_terms = lag_grads(act_pad, cot, frames)
    cond = jnp.dot(first, cond_weight, preferred_element_type=jnp.float32)
    output = ((masked.astype(jnp.float32) + mixed + cond[:, None]) * mask_f).astype(jnp.bfloat16)
    sig = jax.nn.sigmoid(pre)
    dpre = (dact * sig * (1.0 + pre * (1.0 - sig))).astype(jnp.bfloat16)
    cond_back = jnp.dot(cot_sum, cond_weight.astype(jnp.float32).T, precision=lax.Precision.HIGHEST)
    dpre_rows = row_halo(dpre)
    dpre_pad = jnp.pad(dpre_rows, ((0, 0), (0, 0), (0, 0), (1, 1), (0, 0)))
    dmasked = spatial_sum(dpre_pad, spatial_weight, True)
    is_first = (frame_ids == 0).astype(jnp.float32)[None, :, None, None, None]
    grad_latents = (
        (cot.astype(jnp.float32) + dmasked + is_first * cond_back[:, None]) * mask_f
    ).astype(jnp.bfloat16)
    dims = (((0, 1, 2, 3), (0, 1, 2, 3)), ((), ()))
    spatial_terms = []
    for row_off in range(3):
        for col_off in range(3):
            piece = padded[:, :, row_off : row_off + rows, col_off : col_off + cols]
            spatial_terms.append(
                lax.dot_general(piece, dpre, dims, preferred_element_type=jnp.float32)
            )
    spatial_terms = jnp.stack(spatial_terms)
    cond_terms = lax.dot_general(
        first.astype(jnp.float32),
        cot_local,
        (((0, 1, 2), (0, 1, 2)), ((), ())),
        precision=lax.Precision.HIGHEST,
    )
    taps_s = spatial_terms.shape[0]
    taps_t = temporal_terms.shape[0]
    flat = jnp.concatenate(
        [
            spatial_terms.reshape(-1, chans),
            temporal_terms.reshape(-1, chans),
            cond_terms.reshape(-1, chans),
        ],
        axis=0,
    )
    scale = (clips * frames * rows * cols * lax.axis_size("space") * lax.axis_size("tm")) ** (-0.5)
    summed = all_sum_rounded(flat, scale)
    n_s = taps_s * chans
    n_t = taps_t * chans
    grad_spatial = summed[:n_s].reshape(taps_s, chans, chans)
    grad_temporal = summed[n_s : n_s + n_t].reshape(taps_t, chans, chans)
    grad_cond = summed[n_s + n_t :]
    return (output, grad_latents, grad_spatial, grad_temporal, grad_cond)


def solution(mesh):
    return jax.shard_map(
        on_device,
        mesh=mesh,
        in_specs=(
            P("groups", "space", "tm", None, None),
            P("groups", "space", "tm", None, None),
            P("groups"),
            P(),
            P(),
            P(),
        ),
        out_specs=(
            P("groups", "space", "tm", None, None),
            P("groups", "space", "tm", None, None),
            P("groups", None, None),
            P("groups", None, None),
            P("groups", None),
        ),
        check_vma=False,
    )
```

```python
import jax
import jax.numpy as jnp
from jax import lax
from jax.sharding import PartitionSpec as P


def shifted(value, axis, by):
    count = lax.axis_size(axis)
    pairs = [(i, i + by) for i in range(count) if 0 <= i + by < count]
    return lax.ppermute(value, axis, pairs)


def tree_broadcast(value, axis):
    count = lax.axis_size(axis)
    me = lax.axis_index(axis)
    step = 1
    while step * 2 < count:
        step *= 2
    while step >= 1 and count > 1:
        pairs = [(i, i + step) for i in range(0, count, 2 * step) if i + step < count]
        got = lax.ppermute(value, axis, pairs)
        value = jnp.where(me % (2 * step) == step, got, value)
        step //= 2
    return value


def tree_reduce(value, axis):
    count = lax.axis_size(axis)
    step = 1
    while step < count:
        pairs = [(i + step, i) for i in range(0, count, 2 * step) if i + step < count]
        value = value + lax.ppermute(value, axis, pairs)
        step *= 2
    return value


def xor_halving(flat, axis, steps):
    me = lax.axis_index(axis)
    count = lax.axis_size(axis)
    for step in steps:
        half = flat.shape[0] // 2
        upper = (me // step) % 2
        keep = lax.dynamic_slice_in_dim(flat, upper * half, half, 0)
        send = lax.dynamic_slice_in_dim(flat, (1 - upper) * half, half, 0)
        pairs = [(i, i ^ step) for i in range(count)]
        flat = keep + lax.ppermute(send, axis, pairs)
    return flat


def xor_doubling(piece, axis, steps):
    me = lax.axis_index(axis)
    count = lax.axis_size(axis)
    for step in reversed(steps):
        got = lax.ppermute(piece, axis, [(i, i ^ step) for i in range(count)])
        upper = (me // step) % 2 == 1
        piece = jnp.where(
            upper, jnp.concatenate([got, piece], 0), jnp.concatenate([piece, got], 0)
        )
    return piece


def direct_scatter(flat, axis, low, high):
    me = lax.axis_index(axis)
    j = me // low
    blk = flat.shape[0] // high
    total = lax.dynamic_slice_in_dim(flat, j * blk, blk, 0)
    for d in range(1, high):
        send = lax.dynamic_slice_in_dim(flat, ((j + d) % high) * blk, blk, 0)
        pairs = [
            (a * low + b, ((a + d) % high) * low + b) for a in range(high) for b in range(low)
        ]
        total = total + lax.ppermute(send, axis, pairs)
    return total


def direct_gather(piece, axis, low, high):
    me = lax.axis_index(axis)
    j = me // low
    out = jnp.zeros((high,) + piece.shape, piece.dtype)
    out = lax.dynamic_update_index_in_dim(out, piece, j, 0)
    for d in range(1, high):
        pairs = [
            (a * low + b, ((a + d) % high) * low + b) for a in range(high) for b in range(low)
        ]
        got = lax.ppermute(piece, axis, pairs)
        out = lax.dynamic_update_index_in_dim(out, got, (j - d) % high, 0)
    return out.reshape((-1,) + piece.shape[1:])


def is_pow2(n):
    return n >= 1 and (n & (n - 1)) == 0


def all_sum_rounded(flat, scale):
    n_tm = lax.axis_size("tm")
    n_sp = lax.axis_size("space")
    if not (is_pow2(n_tm) and is_pow2(n_sp)):
        return (lax.psum(flat, ("tm", "space")) * scale).astype(jnp.bfloat16)
    high = min(4, n_sp)
    low = n_sp // high
    tm_steps = []
    s = 1
    while s < n_tm:
        tm_steps.append(s)
        s *= 2
    sp_steps = []
    s = 1
    while s < low:
        sp_steps.append(s)
        s *= 2
    rows = flat.shape[0]
    unit = n_tm * n_sp * 8
    padded_rows = -(-rows // unit) * unit
    if padded_rows != rows:
        flat = jnp.pad(flat, ((0, padded_rows - rows), (0, 0)))
    flat = xor_halving(flat, "tm", tm_steps)
    flat = xor_halving(flat, "space", sp_steps)
    flat = direct_scatter(flat, "space", low, high)
    piece = (flat * scale).astype(jnp.bfloat16)
    piece = direct_gather(piece, "space", low, high)
    piece = xor_doubling(piece, "space", sp_steps)
    piece = xor_doubling(piece, "tm", tm_steps)
    return piece[:rows]


def spatial_sum(padded, weights, flip):
    rows = padded.shape[2] - 2
    cols = padded.shape[3] - 2
    total = jnp.zeros(padded.shape[:2] + (rows, cols, weights.shape[2]), jnp.float32)
    for row_off in range(3):
        for col_off in range(3):
            if flip:
                piece = padded[
                    :, :, 2 - row_off : 2 - row_off + rows, 2 - col_off : 2 - col_off + cols
                ]
                kernel = weights[3 * row_off + col_off].T
            else:
                piece = padded[:, :, row_off : row_off + rows, col_off : col_off + cols]
                kernel = weights[3 * row_off + col_off]
            total = total + jnp.dot(piece, kernel, preferred_element_type=jnp.float32)
    return total


def lag_forward(padded_act, weights, count):
    total = 0.0
    for lag in range(3):
        total = total + jnp.dot(
            padded_act[:, 2 - lag : 2 - lag + count],
            weights[lag],
            preferred_element_type=jnp.float32,
        )
    return total


def lag_backward(padded_cot, weights, count):
    total = 0.0
    for lag in range(3):
        total = total + jnp.dot(
            padded_cot[:, lag : lag + count], weights[lag].T, preferred_element_type=jnp.float32
        )
    return total


def lag_grads(padded_act, cot, count):
    dims = (((0, 1, 2, 3), (0, 1, 2, 3)), ((), ()))
    terms = []
    for lag in range(3):
        terms.append(
            lax.dot_general(
                padded_act[:, 2 - lag : 2 - lag + count],
                cot,
                dims,
                preferred_element_type=jnp.float32,
            )
        )
    return jnp.stack(terms)


def row_halo(x):
    above = shifted(x[:, :, -1:], "tm", 1)
    below = shifted(x[:, :, :1], "tm", -1)
    return jnp.concatenate([above, x, below], axis=2)


def on_device(latents, cotangent, valid_frames, spatial_weight, temporal_weight, cond_weight):
    clips, frames, rows, cols, chans = latents.shape
    slab = lax.axis_index("space")
    frame_ids = slab * frames + jnp.arange(frames, dtype=jnp.int32)
    mask = (frame_ids[None, :] < valid_frames[:, None]).astype(jnp.bfloat16)[:, :, None, None, None]
    mask_f = mask.astype(jnp.float32)
    masked = latents * mask
    cot = cotangent * mask
    first = tree_broadcast(masked[:, 0], "space")
    cot_local = jnp.sum(cot, axis=1, dtype=jnp.float32)
    cot_sum = tree_reduce(cot_local, "space")
    later = shifted(cot, "space", -1)
    rows_pad = row_halo(masked)
    padded = jnp.pad(rows_pad, ((0, 0), (0, 0), (0, 0), (1, 1), (0, 0)))
    pre = spatial_sum(padded, spatial_weight, False)
    act = jax.nn.silu(pre).astype(jnp.bfloat16)
    earlier = shifted(act, "space", 1)
    act_pad = jnp.concatenate([earlier, act], axis=1)
    mixed = lag_forward(act_pad, temporal_weight, frames)
    cot_pad = jnp.concatenate([cot, later], axis=1)
    dact = lag_backward(cot_pad, temporal_weight, frames)
    temporal_terms = lag_grads(act_pad, cot, frames)
    cond = jnp.dot(first, cond_weight, preferred_element_type=jnp.float32)
    output = ((masked.astype(jnp.float32) + mixed + cond[:, None]) * mask_f).astype(jnp.bfloat16)
    sig = jax.nn.sigmoid(pre)
    dpre = (dact * sig * (1.0 + pre * (1.0 - sig))).astype(jnp.bfloat16)
    cond_back = jnp.dot(cot_sum, cond_weight.astype(jnp.float32).T, precision=lax.Precision.HIGHEST)
    dpre_rows = row_halo(dpre)
    dpre_pad = jnp.pad(dpre_rows, ((0, 0), (0, 0), (0, 0), (1, 1), (0, 0)))
    dmasked = spatial_sum(dpre_pad, spatial_weight, True)
    is_first = (frame_ids == 0).astype(jnp.float32)[None, :, None, None, None]
    grad_latents = (
        (cot.astype(jnp.float32) + dmasked + is_first * cond_back[:, None]) * mask_f
    ).astype(jnp.bfloat16)
    dims = (((0, 1, 2, 3), (0, 1, 2, 3)), ((), ()))
    spatial_terms = []
    for row_off in range(3):
        for col_off in range(3):
            piece = padded[:, :, row_off : row_off + rows, col_off : col_off + cols]
            spatial_terms.append(
                lax.dot_general(piece, dpre, dims, preferred_element_type=jnp.float32)
            )
    spatial_terms = jnp.stack(spatial_terms)
    cond_terms = lax.dot_general(
        first.astype(jnp.float32),
        cot_local,
        (((0, 1, 2), (0, 1, 2)), ((), ())),
        precision=lax.Precision.HIGHEST,
    )
    taps_s = spatial_terms.shape[0]
    taps_t = temporal_terms.shape[0]
    scale = (clips * frames * rows * cols * lax.axis_size("space") * lax.axis_size("tm")) ** (-0.5)
    grad_spatial = all_sum_rounded(spatial_terms.reshape(-1, chans), scale)
    grad_spatial = grad_spatial.reshape(taps_s, chans, chans)
    late = jnp.concatenate(
        [temporal_terms.reshape(-1, chans), cond_terms.reshape(-1, chans)], axis=0
    )
    late = all_sum_rounded(late, scale)
    n_t = taps_t * chans
    grad_temporal = late[:n_t].reshape(taps_t, chans, chans)
    grad_cond = late[n_t:]
    return (output, grad_latents, grad_spatial, grad_temporal, grad_cond)


def solution(mesh):
    return jax.shard_map(
        on_device,
        mesh=mesh,
        in_specs=(
            P("groups", "space", "tm", None, None),
            P("groups", "space", "tm", None, None),
            P("groups"),
            P(),
            P(),
            P(),
        ),
        out_specs=(
            P("groups", "space", "tm", None, None),
            P("groups", "space", "tm", None, None),
            P("groups", None, None),
            P("groups", None, None),
            P("groups", None),
        ),
        check_vma=False,
    )
```

```python
import jax
import jax.numpy as jnp
from jax import lax
from jax.sharding import PartitionSpec as P


def shifted(value, axis, by):
    count = lax.axis_size(axis)
    pairs = [(i, i + by) for i in range(count) if 0 <= i + by < count]
    return lax.ppermute(value, axis, pairs)


def tree_broadcast(value, axis):
    count = lax.axis_size(axis)
    me = lax.axis_index(axis)
    step = 1
    while step * 2 < count:
        step *= 2
    while step >= 1 and count > 1:
        pairs = [(i, i + step) for i in range(0, count, 2 * step) if i + step < count]
        got = lax.ppermute(value, axis, pairs)
        value = jnp.where(me % (2 * step) == step, got, value)
        step //= 2
    return value


def tree_reduce(value, axis):
    count = lax.axis_size(axis)
    step = 1
    while step < count:
        pairs = [(i + step, i) for i in range(0, count, 2 * step) if i + step < count]
        value = value + lax.ppermute(value, axis, pairs)
        step *= 2
    return value


def xor_halving(flat, axis, steps):
    me = lax.axis_index(axis)
    count = lax.axis_size(axis)
    for step in steps:
        half = flat.shape[0] // 2
        upper = (me // step) % 2
        keep = lax.dynamic_slice_in_dim(flat, upper * half, half, 0)
        send = lax.dynamic_slice_in_dim(flat, (1 - upper) * half, half, 0)
        pairs = [(i, i ^ step) for i in range(count)]
        flat = keep + lax.ppermute(send, axis, pairs)
    return flat


def xor_doubling(piece, axis, steps):
    me = lax.axis_index(axis)
    count = lax.axis_size(axis)
    for step in reversed(steps):
        got = lax.ppermute(piece, axis, [(i, i ^ step) for i in range(count)])
        upper = (me // step) % 2 == 1
        piece = jnp.where(
            upper, jnp.concatenate([got, piece], 0), jnp.concatenate([piece, got], 0)
        )
    return piece


def direct_scatter(flat, axis, low, high):
    me = lax.axis_index(axis)
    j = me // low
    blk = flat.shape[0] // high
    total = lax.dynamic_slice_in_dim(flat, j * blk, blk, 0)
    for d in range(1, high):
        send = lax.dynamic_slice_in_dim(flat, ((j + d) % high) * blk, blk, 0)
        pairs = [
            (a * low + b, ((a + d) % high) * low + b) for a in range(high) for b in range(low)
        ]
        total = total + lax.ppermute(send, axis, pairs)
    return total


def direct_gather(piece, axis, low, high):
    me = lax.axis_index(axis)
    j = me // low
    out = jnp.zeros((high,) + piece.shape, piece.dtype)
    out = lax.dynamic_update_index_in_dim(out, piece, j, 0)
    for d in range(1, high):
        pairs = [
            (a * low + b, ((a + d) % high) * low + b) for a in range(high) for b in range(low)
        ]
        got = lax.ppermute(piece, axis, pairs)
        out = lax.dynamic_update_index_in_dim(out, got, (j - d) % high, 0)
    return out.reshape((-1,) + piece.shape[1:])


def is_pow2(n):
    return n >= 1 and (n & (n - 1)) == 0


def all_sum_rounded(flat, scale):
    n_tm = lax.axis_size("tm")
    n_sp = lax.axis_size("space")
    if not (is_pow2(n_tm) and is_pow2(n_sp)):
        return (lax.psum(flat, ("tm", "space")) * scale).astype(jnp.bfloat16)
    high = min(4, n_sp)
    low = n_sp // high
    tm_steps = []
    s = 1
    while s < n_tm:
        tm_steps.append(s)
        s *= 2
    sp_steps = []
    s = 1
    while s < low:
        sp_steps.append(s)
        s *= 2
    rows = flat.shape[0]
    unit = n_tm * n_sp * 8
    padded_rows = -(-rows // unit) * unit
    if padded_rows != rows:
        flat = jnp.pad(flat, ((0, padded_rows - rows), (0, 0)))
    flat = xor_halving(flat, "tm", tm_steps)
    flat = xor_halving(flat, "space", sp_steps)
    flat = direct_scatter(flat, "space", low, high)
    piece = (flat * scale).astype(jnp.bfloat16)
    blk = piece.shape[0]
    whole = lax.all_gather(piece, ("tm", "space"), axis=0, tiled=True)
    whole = whole.reshape(n_tm, high, low, blk, flat.shape[1])
    whole = jnp.transpose(whole, (0, 2, 1, 3, 4)).reshape(-1, flat.shape[1])
    return whole[:rows]


def spatial_sum(padded, weights, flip):
    rows = padded.shape[2] - 2
    cols = padded.shape[3] - 2
    total = jnp.zeros(padded.shape[:2] + (rows, cols, weights.shape[2]), jnp.float32)
    for row_off in range(3):
        for col_off in range(3):
            if flip:
                piece = padded[
                    :, :, 2 - row_off : 2 - row_off + rows, 2 - col_off : 2 - col_off + cols
                ]
                kernel = weights[3 * row_off + col_off].T
            else:
                piece = padded[:, :, row_off : row_off + rows, col_off : col_off + cols]
                kernel = weights[3 * row_off + col_off]
            total = total + jnp.dot(piece, kernel, preferred_element_type=jnp.float32)
    return total


def lag_forward(padded_act, weights, count):
    total = 0.0
    for lag in range(3):
        total = total + jnp.dot(
            padded_act[:, 2 - lag : 2 - lag + count],
            weights[lag],
            preferred_element_type=jnp.float32,
        )
    return total


def lag_backward(padded_cot, weights, count):
    total = 0.0
    for lag in range(3):
        total = total + jnp.dot(
            padded_cot[:, lag : lag + count], weights[lag].T, preferred_element_type=jnp.float32
        )
    return total


def lag_grads(padded_act, cot, count):
    dims = (((0, 1, 2, 3), (0, 1, 2, 3)), ((), ()))
    terms = []
    for lag in range(3):
        terms.append(
            lax.dot_general(
                padded_act[:, 2 - lag : 2 - lag + count],
                cot,
                dims,
                preferred_element_type=jnp.float32,
            )
        )
    return jnp.stack(terms)


def row_halo(x):
    if lax.axis_size("tm") == 2:
        me = lax.axis_index("tm")
        edge = jnp.where(me == 0, x[:, :, -1:], x[:, :, :1])
        got = lax.ppermute(edge, "tm", [(0, 1), (1, 0)])
        zero = jnp.zeros_like(got)
        above = jnp.where(me == 1, got, zero)
        below = jnp.where(me == 0, got, zero)
        return jnp.concatenate([above, x, below], axis=2)
    above = shifted(x[:, :, -1:], "tm", 1)
    below = shifted(x[:, :, :1], "tm", -1)
    return jnp.concatenate([above, x, below], axis=2)


def on_device(latents, cotangent, valid_frames, spatial_weight, temporal_weight, cond_weight):
    clips, frames, rows, cols, chans = latents.shape
    slab = lax.axis_index("space")
    frame_ids = slab * frames + jnp.arange(frames, dtype=jnp.int32)
    mask = (frame_ids[None, :] < valid_frames[:, None]).astype(jnp.bfloat16)[:, :, None, None, None]
    mask_f = mask.astype(jnp.float32)
    masked = latents * mask
    cot = cotangent * mask
    first = tree_broadcast(masked[:, 0], "space")
    cot_local = jnp.sum(cot, axis=1, dtype=jnp.float32)
    cot_sum = tree_reduce(cot_local, "space")
    later = shifted(cot, "space", -1)
    rows_pad = row_halo(masked)
    padded = jnp.pad(rows_pad, ((0, 0), (0, 0), (0, 0), (1, 1), (0, 0)))
    pre = spatial_sum(padded, spatial_weight, False)
    act = jax.nn.silu(pre).astype(jnp.bfloat16)
    earlier = shifted(act, "space", 1)
    act_pad = jnp.concatenate([earlier, act], axis=1)
    mixed = lag_forward(act_pad, temporal_weight, frames)
    cot_pad = jnp.concatenate([cot, later], axis=1)
    dact = lag_backward(cot_pad, temporal_weight, frames)
    temporal_terms = lag_grads(act_pad, cot, frames)
    cond = jnp.dot(first, cond_weight, preferred_element_type=jnp.float32)
    output = ((masked.astype(jnp.float32) + mixed + cond[:, None]) * mask_f).astype(jnp.bfloat16)
    sig = jax.nn.sigmoid(pre)
    dpre = (dact * sig * (1.0 + pre * (1.0 - sig))).astype(jnp.bfloat16)
    cond_back = jnp.dot(cot_sum, cond_weight.astype(jnp.float32).T, precision=lax.Precision.HIGHEST)
    dpre_rows = row_halo(dpre)
    dpre_pad = jnp.pad(dpre_rows, ((0, 0), (0, 0), (0, 0), (1, 1), (0, 0)))
    dmasked = spatial_sum(dpre_pad, spatial_weight, True)
    is_first = (frame_ids == 0).astype(jnp.float32)[None, :, None, None, None]
    grad_latents = (
        (cot.astype(jnp.float32) + dmasked + is_first * cond_back[:, None]) * mask_f
    ).astype(jnp.bfloat16)
    dims = (((0, 1, 2, 3), (0, 1, 2, 3)), ((), ()))
    spatial_terms = []
    for row_off in range(3):
        for col_off in range(3):
            piece = padded[:, :, row_off : row_off + rows, col_off : col_off + cols]
            spatial_terms.append(
                lax.dot_general(piece, dpre, dims, preferred_element_type=jnp.float32)
            )
    spatial_terms = jnp.stack(spatial_terms)
    cond_terms = lax.dot_general(
        first.astype(jnp.float32),
        cot_local,
        (((0, 1, 2), (0, 1, 2)), ((), ())),
        precision=lax.Precision.HIGHEST,
    )
    taps_s = spatial_terms.shape[0]
    taps_t = temporal_terms.shape[0]
    flat = jnp.concatenate(
        [
            spatial_terms.reshape(-1, chans),
            temporal_terms.reshape(-1, chans),
            cond_terms.reshape(-1, chans),
        ],
        axis=0,
    )
    scale = (clips * frames * rows * cols * lax.axis_size("space") * lax.axis_size("tm")) ** (-0.5)
    summed = all_sum_rounded(flat, scale)
    n_s = taps_s * chans
    n_t = taps_t * chans
    grad_spatial = summed[:n_s].reshape(taps_s, chans, chans)
    grad_temporal = summed[n_s : n_s + n_t].reshape(taps_t, chans, chans)
    grad_cond = summed[n_s + n_t :]
    return (output, grad_latents, grad_spatial, grad_temporal, grad_cond)


def solution(mesh):
    return jax.shard_map(
        on_device,
        mesh=mesh,
        in_specs=(
            P("groups", "space", "tm", None, None),
            P("groups", "space", "tm", None, None),
            P("groups"),
            P(),
            P(),
            P(),
        ),
        out_specs=(
            P("groups", "space", "tm", None, None),
            P("groups", "space", "tm", None, None),
            P("groups", None, None),
            P("groups", None, None),
            P("groups", None),
        ),
        check_vma=False,
    )
```

```python
import jax
import jax.numpy as jnp
from jax import lax
from jax.sharding import PartitionSpec as P


def shifted(value, axis, by):
    count = lax.axis_size(axis)
    pairs = [(i, i + by) for i in range(count) if 0 <= i + by < count]
    return lax.ppermute(value, axis, pairs)


def tree_broadcast(value, axis):
    count = lax.axis_size(axis)
    me = lax.axis_index(axis)
    step = 1
    while step * 2 < count:
        step *= 2
    while step >= 1 and count > 1:
        pairs = [(i, i + step) for i in range(0, count, 2 * step) if i + step < count]
        got = lax.ppermute(value, axis, pairs)
        value = jnp.where(me % (2 * step) == step, got, value)
        step //= 2
    return value


def tree_reduce(value, axis):
    count = lax.axis_size(axis)
    step = 1
    while step < count:
        pairs = [(i + step, i) for i in range(0, count, 2 * step) if i + step < count]
        value = value + lax.ppermute(value, axis, pairs)
        step *= 2
    return value


def xor_halving(flat, axis, steps):
    me = lax.axis_index(axis)
    count = lax.axis_size(axis)
    for step in steps:
        half = flat.shape[0] // 2
        upper = (me // step) % 2
        keep = lax.dynamic_slice_in_dim(flat, upper * half, half, 0)
        send = lax.dynamic_slice_in_dim(flat, (1 - upper) * half, half, 0)
        pairs = [(i, i ^ step) for i in range(count)]
        flat = keep + lax.ppermute(send, axis, pairs)
    return flat


def xor_doubling(piece, axis, steps):
    me = lax.axis_index(axis)
    count = lax.axis_size(axis)
    for step in reversed(steps):
        got = lax.ppermute(piece, axis, [(i, i ^ step) for i in range(count)])
        upper = (me // step) % 2 == 1
        piece = jnp.where(
            upper, jnp.concatenate([got, piece], 0), jnp.concatenate([piece, got], 0)
        )
    return piece


def direct_scatter(flat, axis, low, high):
    me = lax.axis_index(axis)
    j = me // low
    blk = flat.shape[0] // high
    total = lax.dynamic_slice_in_dim(flat, j * blk, blk, 0)
    for d in range(1, high):
        send = lax.dynamic_slice_in_dim(flat, ((j + d) % high) * blk, blk, 0)
        pairs = [
            (a * low + b, ((a + d) % high) * low + b) for a in range(high) for b in range(low)
        ]
        total = total + lax.ppermute(send, axis, pairs)
    return total


def direct_gather(piece, axis, low, high):
    me = lax.axis_index(axis)
    j = me // low
    out = jnp.zeros((high,) + piece.shape, piece.dtype)
    out = lax.dynamic_update_index_in_dim(out, piece, j, 0)
    for d in range(1, high):
        pairs = [
            (a * low + b, ((a + d) % high) * low + b) for a in range(high) for b in range(low)
        ]
        got = lax.ppermute(piece, axis, pairs)
        out = lax.dynamic_update_index_in_dim(out, got, (j - d) % high, 0)
    return out.reshape((-1,) + piece.shape[1:])


def is_pow2(n):
    return n >= 1 and (n & (n - 1)) == 0


def all_sum_rounded(flat, scale):
    n_tm = lax.axis_size("tm")
    n_sp = lax.axis_size("space")
    if not (is_pow2(n_tm) and is_pow2(n_sp)):
        return (lax.psum(flat, ("tm", "space")) * scale).astype(jnp.bfloat16)
    high = min(4, n_sp)
    low = n_sp // high
    tm_steps = []
    s = 1
    while s < n_tm:
        tm_steps.append(s)
        s *= 2
    sp_steps = []
    s = 1
    while s < low:
        sp_steps.append(s)
        s *= 2
    rows = flat.shape[0]
    unit = n_tm * n_sp * 8
    padded_rows = -(-rows // unit) * unit
    if padded_rows != rows:
        flat = jnp.pad(flat, ((0, padded_rows - rows), (0, 0)))
    flat = xor_halving(flat, "tm", tm_steps)
    flat = xor_halving(flat, "space", sp_steps)
    flat = direct_scatter(flat, "space", low, high)
    piece = (flat * scale).astype(jnp.bfloat16)
    piece = direct_gather(piece, "space", low, high)
    piece = xor_doubling(piece, "space", sp_steps)
    piece = xor_doubling(piece, "tm", tm_steps)
    return piece[:rows]


def spatial_sum(padded, weights, flip):
    rows = padded.shape[2] - 2
    cols = padded.shape[3] - 2
    total = jnp.zeros(padded.shape[:2] + (rows, cols, weights.shape[2]), jnp.float32)
    for row_off in range(3):
        for col_off in range(3):
            if flip:
                piece = padded[
                    :, :, 2 - row_off : 2 - row_off + rows, 2 - col_off : 2 - col_off + cols
                ]
                kernel = weights[3 * row_off + col_off].T
            else:
                piece = padded[:, :, row_off : row_off + rows, col_off : col_off + cols]
                kernel = weights[3 * row_off + col_off]
            total = total + jnp.dot(piece, kernel, preferred_element_type=jnp.float32)
    return total


def lag_forward(padded_act, weights, count):
    total = 0.0
    for lag in range(3):
        total = total + jnp.dot(
            padded_act[:, 2 - lag : 2 - lag + count],
            weights[lag],
            preferred_element_type=jnp.float32,
        )
    return total


def lag_backward(padded_cot, weights, count):
    total = 0.0
    for lag in range(3):
        total = total + jnp.dot(
            padded_cot[:, lag : lag + count], weights[lag].T, preferred_element_type=jnp.float32
        )
    return total


def lag_grads(act, padded_cot, count):
    dims = (((0, 1, 2, 3), (0, 1, 2, 3)), ((), ()))
    terms = []
    for lag in range(3):
        terms.append(
            lax.dot_general(
                act,
                padded_cot[:, lag : lag + count],
                dims,
                preferred_element_type=jnp.float32,
            )
        )
    return jnp.stack(terms)


def row_halo(x):
    if lax.axis_size("tm") == 2:
        me = lax.axis_index("tm")
        edge = jnp.where(me == 0, x[:, :, -1:], x[:, :, :1])
        got = lax.ppermute(edge, "tm", [(0, 1), (1, 0)])
        zero = jnp.zeros_like(got)
        above = jnp.where(me == 1, got, zero)
        below = jnp.where(me == 0, got, zero)
        return jnp.concatenate([above, x, below], axis=2)
    above = shifted(x[:, :, -1:], "tm", 1)
    below = shifted(x[:, :, :1], "tm", -1)
    return jnp.concatenate([above, x, below], axis=2)


def on_device(latents, cotangent, valid_frames, spatial_weight, temporal_weight, cond_weight):
    clips, frames, rows, cols, chans = latents.shape
    slab = lax.axis_index("space")
    frame_ids = slab * frames + jnp.arange(frames, dtype=jnp.int32)
    mask = (frame_ids[None, :] < valid_frames[:, None]).astype(jnp.bfloat16)[:, :, None, None, None]
    mask_f = mask.astype(jnp.float32)
    masked = latents * mask
    cot = cotangent * mask
    first = tree_broadcast(masked[:, 0], "space")
    cot_local = jnp.sum(cot, axis=1, dtype=jnp.float32)
    cot_sum = tree_reduce(cot_local, "space")
    later = shifted(cot, "space", -1)
    rows_pad = row_halo(masked)
    padded = jnp.pad(rows_pad, ((0, 0), (0, 0), (0, 0), (1, 1), (0, 0)))
    pre = spatial_sum(padded, spatial_weight, False)
    act = jax.nn.silu(pre).astype(jnp.bfloat16)
    earlier = shifted(act, "space", 1)
    act_pad = jnp.concatenate([earlier, act], axis=1)
    mixed = lag_forward(act_pad, temporal_weight, frames)
    cot_pad = jnp.concatenate([cot, later], axis=1)
    dact = lag_backward(cot_pad, temporal_weight, frames)
    temporal_terms = lag_grads(act, cot_pad, frames)
    cond = jnp.dot(first, cond_weight, preferred_element_type=jnp.float32)
    output = ((masked.astype(jnp.float32) + mixed + cond[:, None]) * mask_f).astype(jnp.bfloat16)
    sig = jax.nn.sigmoid(pre)
    dpre = (dact * sig * (1.0 + pre * (1.0 - sig))).astype(jnp.bfloat16)
    cond_back = jnp.dot(cot_sum, cond_weight.astype(jnp.float32).T, precision=lax.Precision.HIGHEST)
    dpre_rows = row_halo(dpre)
    dpre_pad = jnp.pad(dpre_rows, ((0, 0), (0, 0), (0, 0), (1, 1), (0, 0)))
    dmasked = spatial_sum(dpre_pad, spatial_weight, True)
    is_first = (frame_ids == 0).astype(jnp.float32)[None, :, None, None, None]
    grad_latents = (
        (cot.astype(jnp.float32) + dmasked + is_first * cond_back[:, None]) * mask_f
    ).astype(jnp.bfloat16)
    dims = (((0, 1, 2, 3), (0, 1, 2, 3)), ((), ()))
    spatial_terms = []
    for row_off in range(3):
        for col_off in range(3):
            piece = padded[:, :, row_off : row_off + rows, col_off : col_off + cols]
            spatial_terms.append(
                lax.dot_general(piece, dpre, dims, preferred_element_type=jnp.float32)
            )
    spatial_terms = jnp.stack(spatial_terms)
    cond_terms = lax.dot_general(
        first.astype(jnp.float32),
        cot_local,
        (((0, 1, 2), (0, 1, 2)), ((), ())),
        precision=lax.Precision.HIGHEST,
    )
    taps_s = spatial_terms.shape[0]
    taps_t = temporal_terms.shape[0]
    flat = jnp.concatenate(
        [
            spatial_terms.reshape(-1, chans),
            temporal_terms.reshape(-1, chans),
            cond_terms.reshape(-1, chans),
        ],
        axis=0,
    )
    scale = (clips * frames * rows * cols * lax.axis_size("space") * lax.axis_size("tm")) ** (-0.5)
    summed = all_sum_rounded(flat, scale)
    n_s = taps_s * chans
    n_t = taps_t * chans
    grad_spatial = summed[:n_s].reshape(taps_s, chans, chans)
    grad_temporal = summed[n_s : n_s + n_t].reshape(taps_t, chans, chans)
    grad_cond = summed[n_s + n_t :]
    return (output, grad_latents, grad_spatial, grad_temporal, grad_cond)


def solution(mesh):
    return jax.shard_map(
        on_device,
        mesh=mesh,
        in_specs=(
            P("groups", "space", "tm", None, None),
            P("groups", "space", "tm", None, None),
            P("groups"),
            P(),
            P(),
            P(),
        ),
        out_specs=(
            P("groups", "space", "tm", None, None),
            P("groups", "space", "tm", None, None),
            P("groups", None, None),
            P("groups", None, None),
            P("groups", None),
        ),
        check_vma=False,
    )
```

```python
import jax
import jax.numpy as jnp
from jax import lax
from jax.sharding import PartitionSpec as P


def shifted(value, axis, by):
    count = lax.axis_size(axis)
    pairs = [(i, i + by) for i in range(count) if 0 <= i + by < count]
    return lax.ppermute(value, axis, pairs)


def tree_broadcast(value, axis):
    count = lax.axis_size(axis)
    me = lax.axis_index(axis)
    step = 1
    while step * 2 < count:
        step *= 2
    while step >= 1 and count > 1:
        pairs = [(i, i + step) for i in range(0, count, 2 * step) if i + step < count]
        got = lax.ppermute(value, axis, pairs)
        value = jnp.where(me % (2 * step) == step, got, value)
        step //= 2
    return value


def tree_reduce(value, axis):
    count = lax.axis_size(axis)
    step = 1
    while step < count:
        pairs = [(i + step, i) for i in range(0, count, 2 * step) if i + step < count]
        value = value + lax.ppermute(value, axis, pairs)
        step *= 2
    return value


def xor_halving(flat, axis, steps):
    me = lax.axis_index(axis)
    count = lax.axis_size(axis)
    for step in steps:
        half = flat.shape[0] // 2
        upper = (me // step) % 2
        keep = lax.dynamic_slice_in_dim(flat, upper * half, half, 0)
        send = lax.dynamic_slice_in_dim(flat, (1 - upper) * half, half, 0)
        pairs = [(i, i ^ step) for i in range(count)]
        flat = keep + lax.ppermute(send, axis, pairs)
    return flat


def xor_doubling(piece, axis, steps):
    me = lax.axis_index(axis)
    count = lax.axis_size(axis)
    for step in reversed(steps):
        got = lax.ppermute(piece, axis, [(i, i ^ step) for i in range(count)])
        upper = (me // step) % 2 == 1
        piece = jnp.where(
            upper, jnp.concatenate([got, piece], 0), jnp.concatenate([piece, got], 0)
        )
    return piece


def direct_scatter(flat, axis, low, high):
    me = lax.axis_index(axis)
    j = me // low
    blk = flat.shape[0] // high
    total = lax.dynamic_slice_in_dim(flat, j * blk, blk, 0)
    for d in range(1, high):
        send = lax.dynamic_slice_in_dim(flat, ((j + d) % high) * blk, blk, 0)
        pairs = [
            (a * low + b, ((a + d) % high) * low + b) for a in range(high) for b in range(low)
        ]
        total = total + lax.ppermute(send, axis, pairs)
    return total


def direct_gather(piece, axis, low, high):
    me = lax.axis_index(axis)
    j = me // low
    out = jnp.zeros((high,) + piece.shape, piece.dtype)
    out = lax.dynamic_update_index_in_dim(out, piece, j, 0)
    for d in range(1, high):
        pairs = [
            (a * low + b, ((a + d) % high) * low + b) for a in range(high) for b in range(low)
        ]
        got = lax.ppermute(piece, axis, pairs)
        out = lax.dynamic_update_index_in_dim(out, got, (j - d) % high, 0)
    return out.reshape((-1,) + piece.shape[1:])


def is_pow2(n):
    return n >= 1 and (n & (n - 1)) == 0


def all_sum_rounded(flat, scale):
    n_tm = lax.axis_size("tm")
    n_sp = lax.axis_size("space")
    if not (is_pow2(n_tm) and is_pow2(n_sp)):
        return (lax.psum(flat, ("tm", "space")) * scale).astype(jnp.bfloat16)
    high = min(4, n_sp)
    low = n_sp // high
    tm_steps = []
    s = 1
    while s < n_tm:
        tm_steps.append(s)
        s *= 2
    sp_steps = []
    s = 1
    while s < low:
        sp_steps.append(s)
        s *= 2
    rows = flat.shape[0]
    unit = n_tm * n_sp * 8
    padded_rows = -(-rows // unit) * unit
    if padded_rows != rows:
        flat = jnp.pad(flat, ((0, padded_rows - rows), (0, 0)))
    flat = xor_halving(flat, "tm", tm_steps)
    flat = xor_halving(flat, "space", sp_steps)
    flat = direct_scatter(flat, "space", low, high)
    piece = (flat * scale).astype(jnp.bfloat16)
    piece = direct_gather(piece, "space", low, high)
    piece = xor_doubling(piece, "space", sp_steps)
    piece = xor_doubling(piece, "tm", tm_steps)
    return piece[:rows]


def spatial_sum(padded, weights, flip):
    rows = padded.shape[2] - 2
    cols = padded.shape[3] - 2
    total = jnp.zeros(padded.shape[:2] + (rows, cols, weights.shape[2]), jnp.float32)
    for row_off in range(3):
        for col_off in range(3):
            if flip:
                piece = padded[
                    :, :, 2 - row_off : 2 - row_off + rows, 2 - col_off : 2 - col_off + cols
                ]
                kernel = weights[3 * row_off + col_off].T
            else:
                piece = padded[:, :, row_off : row_off + rows, col_off : col_off + cols]
                kernel = weights[3 * row_off + col_off]
            total = total + jnp.dot(piece, kernel, preferred_element_type=jnp.float32)
    return total


def lag_forward(padded_act, weights, count):
    total = 0.0
    for lag in range(3):
        total = total + jnp.dot(
            padded_act[:, 2 - lag : 2 - lag + count],
            weights[lag],
            preferred_element_type=jnp.float32,
        )
    return total


def lag_backward(padded_cot, weights, count):
    total = 0.0
    for lag in range(3):
        total = total + jnp.dot(
            padded_cot[:, lag : lag + count], weights[lag].T, preferred_element_type=jnp.float32
        )
    return total


def lag_grads(act, padded_cot, count):
    dims = (((0, 1, 2, 3), (0, 1, 2, 3)), ((), ()))
    terms = []
    for lag in range(3):
        terms.append(
            lax.dot_general(
                act,
                padded_cot[:, lag : lag + count],
                dims,
                preferred_element_type=jnp.float32,
            )
        )
    return jnp.stack(terms)


def row_halo(x):
    if lax.axis_size("tm") == 2:
        me = lax.axis_index("tm")
        edge = jnp.where(me == 0, x[:, :, -1:], x[:, :, :1])
        got = lax.ppermute(edge, "tm", [(0, 1), (1, 0)])
        zero = jnp.zeros_like(got)
        above = jnp.where(me == 1, got, zero)
        below = jnp.where(me == 0, got, zero)
        return jnp.concatenate([above, x, below], axis=2)
    above = shifted(x[:, :, -1:], "tm", 1)
    below = shifted(x[:, :, :1], "tm", -1)
    return jnp.concatenate([above, x, below], axis=2)


def on_device(latents, cotangent, valid_frames, spatial_weight, temporal_weight, cond_weight):
    clips, frames, rows, cols, chans = latents.shape
    slab = lax.axis_index("space")
    frame_ids = slab * frames + jnp.arange(frames, dtype=jnp.int32)
    mask = (frame_ids[None, :] < valid_frames[:, None]).astype(jnp.bfloat16)[:, :, None, None, None]
    mask_f = mask.astype(jnp.float32)
    masked = latents * mask
    cot = cotangent * mask
    first = tree_broadcast(masked[:, 0], "space")
    cot_local = jnp.sum(cot, axis=1, dtype=jnp.float32)
    cot_sum = tree_reduce(cot_local, "space")
    later = shifted(cot, "space", -1)
    rows_pad = row_halo(masked)
    padded = jnp.pad(rows_pad, ((0, 0), (0, 0), (0, 0), (1, 1), (0, 0)))
    pre = spatial_sum(padded, spatial_weight, False)
    act = jax.nn.silu(pre).astype(jnp.bfloat16)
    earlier = shifted(act, "space", 1)
    act_pad = jnp.concatenate([earlier, act], axis=1)
    mixed = lag_forward(act_pad, temporal_weight, frames)
    cot_pad = jnp.concatenate([cot, later], axis=1)
    dact = lag_backward(cot_pad, temporal_weight, frames)
    temporal_terms = lag_grads(act, cot_pad, frames)
    cond = jnp.dot(first, cond_weight, preferred_element_type=jnp.float32)
    output = ((masked.astype(jnp.float32) + mixed + cond[:, None]) * mask_f).astype(jnp.bfloat16)
    sig = jax.nn.sigmoid(pre)
    dpre = (dact * sig * (1.0 + pre * (1.0 - sig))).astype(jnp.bfloat16)
    dims = (((0, 1, 2, 3), (0, 1, 2, 3)), ((), ()))
    spatial_terms = []
    for row_off in range(3):
        for col_off in range(3):
            piece = padded[:, :, row_off : row_off + rows, col_off : col_off + cols]
            spatial_terms.append(
                lax.dot_general(piece, dpre, dims, preferred_element_type=jnp.float32)
            )
    spatial_terms = jnp.stack(spatial_terms)
    cond_terms = lax.dot_general(
        first.astype(jnp.float32),
        cot_local,
        (((0, 1, 2), (0, 1, 2)), ((), ())),
        precision=lax.Precision.HIGHEST,
    )
    taps_s = spatial_terms.shape[0]
    taps_t = temporal_terms.shape[0]
    flat = jnp.concatenate(
        [
            spatial_terms.reshape(-1, chans),
            temporal_terms.reshape(-1, chans),
            cond_terms.reshape(-1, chans),
        ],
        axis=0,
    )
    scale = (clips * frames * rows * cols * lax.axis_size("space") * lax.axis_size("tm")) ** (-0.5)
    flat, cot_sum = lax.optimization_barrier((flat, cot_sum))
    summed = all_sum_rounded(flat, scale)
    cond_back = jnp.dot(cot_sum, cond_weight.astype(jnp.float32).T, precision=lax.Precision.HIGHEST)
    dpre_rows = row_halo(dpre)
    dpre_pad = jnp.pad(dpre_rows, ((0, 0), (0, 0), (0, 0), (1, 1), (0, 0)))
    dmasked = spatial_sum(dpre_pad, spatial_weight, True)
    is_first = (frame_ids == 0).astype(jnp.float32)[None, :, None, None, None]
    grad_latents = (
        (cot.astype(jnp.float32) + dmasked + is_first * cond_back[:, None]) * mask_f
    ).astype(jnp.bfloat16)
    n_s = taps_s * chans
    n_t = taps_t * chans
    grad_spatial = summed[:n_s].reshape(taps_s, chans, chans)
    grad_temporal = summed[n_s : n_s + n_t].reshape(taps_t, chans, chans)
    grad_cond = summed[n_s + n_t :]
    return (output, grad_latents, grad_spatial, grad_temporal, grad_cond)


def solution(mesh):
    return jax.shard_map(
        on_device,
        mesh=mesh,
        in_specs=(
            P("groups", "space", "tm", None, None),
            P("groups", "space", "tm", None, None),
            P("groups"),
            P(),
            P(),
            P(),
        ),
        out_specs=(
            P("groups", "space", "tm", None, None),
            P("groups", "space", "tm", None, None),
            P("groups", None, None),
            P("groups", None, None),
            P("groups", None),
        ),
        check_vma=False,
    )
```

```python
import jax
import jax.numpy as jnp
from jax import lax
from jax.sharding import PartitionSpec as P


def shifted(value, axis, by):
    count = lax.axis_size(axis)
    pairs = [(i, i + by) for i in range(count) if 0 <= i + by < count]
    return lax.ppermute(value, axis, pairs)


def tree_broadcast(value, axis):
    count = lax.axis_size(axis)
    me = lax.axis_index(axis)
    step = 1
    while step * 2 < count:
        step *= 2
    while step >= 1 and count > 1:
        pairs = [(i, i + step) for i in range(0, count, 2 * step) if i + step < count]
        got = lax.ppermute(value, axis, pairs)
        value = jnp.where(me % (2 * step) == step, got, value)
        step //= 2
    return value


def tree_reduce(value, axis, step=1):
    count = lax.axis_size(axis)
    while step < count:
        pairs = [(i + step, i) for i in range(0, count, 2 * step) if i + step < count]
        value = value + lax.ppermute(value, axis, pairs)
        step *= 2
    return value


def xor_halving(flat, axis, steps):
    me = lax.axis_index(axis)
    count = lax.axis_size(axis)
    for step in steps:
        half = flat.shape[0] // 2
        upper = (me // step) % 2
        keep = lax.dynamic_slice_in_dim(flat, upper * half, half, 0)
        send = lax.dynamic_slice_in_dim(flat, (1 - upper) * half, half, 0)
        pairs = [(i, i ^ step) for i in range(count)]
        flat = keep + lax.ppermute(send, axis, pairs)
    return flat


def xor_doubling(piece, axis, steps):
    me = lax.axis_index(axis)
    count = lax.axis_size(axis)
    for step in reversed(steps):
        got = lax.ppermute(piece, axis, [(i, i ^ step) for i in range(count)])
        upper = (me // step) % 2 == 1
        piece = jnp.where(
            upper, jnp.concatenate([got, piece], 0), jnp.concatenate([piece, got], 0)
        )
    return piece


def direct_scatter(flat, axis, low, high):
    me = lax.axis_index(axis)
    j = me // low
    blk = flat.shape[0] // high
    total = lax.dynamic_slice_in_dim(flat, j * blk, blk, 0)
    for d in range(1, high):
        send = lax.dynamic_slice_in_dim(flat, ((j + d) % high) * blk, blk, 0)
        pairs = [
            (a * low + b, ((a + d) % high) * low + b) for a in range(high) for b in range(low)
        ]
        total = total + lax.ppermute(send, axis, pairs)
    return total


def direct_gather(piece, axis, low, high):
    me = lax.axis_index(axis)
    j = me // low
    out = jnp.zeros((high,) + piece.shape, piece.dtype)
    out = lax.dynamic_update_index_in_dim(out, piece, j, 0)
    for d in range(1, high):
        pairs = [
            (a * low + b, ((a + d) % high) * low + b) for a in range(high) for b in range(low)
        ]
        got = lax.ppermute(piece, axis, pairs)
        out = lax.dynamic_update_index_in_dim(out, got, (j - d) % high, 0)
    return out.reshape((-1,) + piece.shape[1:])


def is_pow2(n):
    return n >= 1 and (n & (n - 1)) == 0


def all_sum_rounded(flat, scale):
    n_tm = lax.axis_size("tm")
    n_sp = lax.axis_size("space")
    if not (is_pow2(n_tm) and is_pow2(n_sp)):
        return (lax.psum(flat, ("tm", "space")) * scale).astype(jnp.bfloat16)
    high = min(4, n_sp)
    low = n_sp // high
    tm_steps = []
    s = 1
    while s < n_tm:
        tm_steps.append(s)
        s *= 2
    sp_steps = []
    s = 1
    while s < low:
        sp_steps.append(s)
        s *= 2
    rows = flat.shape[0]
    unit = n_tm * n_sp * 8
    padded_rows = -(-rows // unit) * unit
    if padded_rows != rows:
        flat = jnp.pad(flat, ((0, padded_rows - rows), (0, 0)))
    flat = xor_halving(flat, "tm", tm_steps)
    flat = xor_halving(flat, "space", sp_steps)
    flat = direct_scatter(flat, "space", low, high)
    piece = (flat * scale).astype(jnp.bfloat16)
    piece = direct_gather(piece, "space", low, high)
    piece = xor_doubling(piece, "space", sp_steps)
    piece = xor_doubling(piece, "tm", tm_steps)
    return piece[:rows]


def spatial_sum(padded, weights, flip):
    rows = padded.shape[2] - 2
    cols = padded.shape[3] - 2
    total = jnp.zeros(padded.shape[:2] + (rows, cols, weights.shape[2]), jnp.float32)
    for row_off in range(3):
        for col_off in range(3):
            if flip:
                piece = padded[
                    :, :, 2 - row_off : 2 - row_off + rows, 2 - col_off : 2 - col_off + cols
                ]
                kernel = weights[3 * row_off + col_off].T
            else:
                piece = padded[:, :, row_off : row_off + rows, col_off : col_off + cols]
                kernel = weights[3 * row_off + col_off]
            total = total + jnp.dot(piece, kernel, preferred_element_type=jnp.float32)
    return total


def lag_forward(padded_act, weights, count):
    total = 0.0
    for lag in range(3):
        total = total + jnp.dot(
            padded_act[:, 2 - lag : 2 - lag + count],
            weights[lag],
            preferred_element_type=jnp.float32,
        )
    return total


def lag_backward(padded_cot, weights, count):
    total = 0.0
    for lag in range(3):
        total = total + jnp.dot(
            padded_cot[:, lag : lag + count], weights[lag].T, preferred_element_type=jnp.float32
        )
    return total


def lag_grads(act, padded_cot, count):
    dims = (((0, 1, 2, 3), (0, 1, 2, 3)), ((), ()))
    terms = []
    for lag in range(3):
        terms.append(
            lax.dot_general(
                act,
                padded_cot[:, lag : lag + count],
                dims,
                preferred_element_type=jnp.float32,
            )
        )
    return jnp.stack(terms)


def row_halo(x):
    if lax.axis_size("tm") == 2:
        me = lax.axis_index("tm")
        edge = jnp.where(me == 0, x[:, :, -1:], x[:, :, :1])
        got = lax.ppermute(edge, "tm", [(0, 1), (1, 0)])
        zero = jnp.zeros_like(got)
        above = jnp.where(me == 1, got, zero)
        below = jnp.where(me == 0, got, zero)
        return jnp.concatenate([above, x, below], axis=2)
    above = shifted(x[:, :, -1:], "tm", 1)
    below = shifted(x[:, :, :1], "tm", -1)
    return jnp.concatenate([above, x, below], axis=2)


def on_device(latents, cotangent, valid_frames, spatial_weight, temporal_weight, cond_weight):
    clips, frames, rows, cols, chans = latents.shape
    slab = lax.axis_index("space")
    frame_ids = slab * frames + jnp.arange(frames, dtype=jnp.int32)
    mask = (frame_ids[None, :] < valid_frames[:, None]).astype(jnp.bfloat16)[:, :, None, None, None]
    mask_f = mask.astype(jnp.float32)
    masked = latents * mask
    cot = cotangent * mask
    first = tree_broadcast(masked[:, 0], "space")
    cot_local = jnp.sum(cot, axis=1, dtype=jnp.float32)
    later = shifted(cot, "space", -1)
    if lax.axis_size("space") % 2 == 0:
        cot_pair = cot_local + jnp.sum(later, axis=1, dtype=jnp.float32)
        cot_sum = tree_reduce(cot_pair, "space", 2)
    else:
        cot_sum = tree_reduce(cot_local, "space")
    rows_pad = row_halo(masked)
    padded = jnp.pad(rows_pad, ((0, 0), (0, 0), (0, 0), (1, 1), (0, 0)))
    pre = spatial_sum(padded, spatial_weight, False)
    act = jax.nn.silu(pre).astype(jnp.bfloat16)
    earlier = shifted(act, "space", 1)
    act_pad = jnp.concatenate([earlier, act], axis=1)
    mixed = lag_forward(act_pad, temporal_weight, frames)
    cot_pad = jnp.concatenate([cot, later], axis=1)
    dact = lag_backward(cot_pad, temporal_weight, frames)
    temporal_terms = lag_grads(act, cot_pad, frames)
    cond = jnp.dot(first, cond_weight, preferred_element_type=jnp.float32)
    output = ((masked.astype(jnp.float32) + mixed + cond[:, None]) * mask_f).astype(jnp.bfloat16)
    sig = jax.nn.sigmoid(pre)
    dpre = (dact * sig * (1.0 + pre * (1.0 - sig))).astype(jnp.bfloat16)
    cond_back = jnp.dot(cot_sum, cond_weight.astype(jnp.float32).T, precision=lax.Precision.HIGHEST)
    dpre_rows = row_halo(dpre)
    dpre_pad = jnp.pad(dpre_rows, ((0, 0), (0, 0), (0, 0), (1, 1), (0, 0)))
    dmasked = spatial_sum(dpre_pad, spatial_weight, True)
    is_first = (frame_ids == 0).astype(jnp.float32)[None, :, None, None, None]
    grad_latents = (
        (cot.astype(jnp.float32) + dmasked + is_first * cond_back[:, None]) * mask_f
    ).astype(jnp.bfloat16)
    dims = (((0, 1, 2, 3), (0, 1, 2, 3)), ((), ()))
    spatial_terms = []
    for row_off in range(3):
        for col_off in range(3):
            piece = padded[:, :, row_off : row_off + rows, col_off : col_off + cols]
            spatial_terms.append(
                lax.dot_general(piece, dpre, dims, preferred_element_type=jnp.float32)
            )
    spatial_terms = jnp.stack(spatial_terms)
    cond_terms = lax.dot_general(
        first.astype(jnp.float32),
        cot_local,
        (((0, 1, 2), (0, 1, 2)), ((), ())),
        precision=lax.Precision.HIGHEST,
    )
    taps_s = spatial_terms.shape[0]
    taps_t = temporal_terms.shape[0]
    flat = jnp.concatenate(
        [
            spatial_terms.reshape(-1, chans),
            temporal_terms.reshape(-1, chans),
            cond_terms.reshape(-1, chans),
        ],
        axis=0,
    )
    scale = (clips * frames * rows * cols * lax.axis_size("space") * lax.axis_size("tm")) ** (-0.5)
    summed = all_sum_rounded(flat, scale)
    n_s = taps_s * chans
    n_t = taps_t * chans
    grad_spatial = summed[:n_s].reshape(taps_s, chans, chans)
    grad_temporal = summed[n_s : n_s + n_t].reshape(taps_t, chans, chans)
    grad_cond = summed[n_s + n_t :]
    return (output, grad_latents, grad_spatial, grad_temporal, grad_cond)


def solution(mesh):
    return jax.shard_map(
        on_device,
        mesh=mesh,
        in_specs=(
            P("groups", "space", "tm", None, None),
            P("groups", "space", "tm", None, None),
            P("groups"),
            P(),
            P(),
            P(),
        ),
        out_specs=(
            P("groups", "space", "tm", None, None),
            P("groups", "space", "tm", None, None),
            P("groups", None, None),
            P("groups", None, None),
            P("groups", None),
        ),
        check_vma=False,
    )
```

```python
import jax
import jax.numpy as jnp
from jax import lax
from jax.sharding import PartitionSpec as P


def shifted(value, axis, by):
    count = lax.axis_size(axis)
    pairs = [(i, i + by) for i in range(count) if 0 <= i + by < count]
    return lax.ppermute(value, axis, pairs)


def tree_broadcast(value, axis):
    count = lax.axis_size(axis)
    me = lax.axis_index(axis)
    step = 1
    while step < count:
        pairs = [(i, i + step) for i in range(step) if i + step < count]
        got = lax.ppermute(value, axis, pairs)
        value = jnp.where((me >= step) & (me < 2 * step), got, value)
        step *= 2
    return value


def tree_reduce(value, axis, step=1):
    count = lax.axis_size(axis)
    while step < count:
        pairs = [(i + step, i) for i in range(0, count, 2 * step) if i + step < count]
        value = value + lax.ppermute(value, axis, pairs)
        step *= 2
    return value


def xor_halving(flat, axis, steps):
    me = lax.axis_index(axis)
    count = lax.axis_size(axis)
    for step in steps:
        half = flat.shape[0] // 2
        upper = (me // step) % 2
        keep = lax.dynamic_slice_in_dim(flat, upper * half, half, 0)
        send = lax.dynamic_slice_in_dim(flat, (1 - upper) * half, half, 0)
        pairs = [(i, i ^ step) for i in range(count)]
        flat = keep + lax.ppermute(send, axis, pairs)
    return flat


def xor_doubling(piece, axis, steps):
    me = lax.axis_index(axis)
    count = lax.axis_size(axis)
    for step in reversed(steps):
        got = lax.ppermute(piece, axis, [(i, i ^ step) for i in range(count)])
        upper = (me // step) % 2 == 1
        piece = jnp.where(
            upper, jnp.concatenate([got, piece], 0), jnp.concatenate([piece, got], 0)
        )
    return piece


def direct_scatter(flat, axis, low, high):
    me = lax.axis_index(axis)
    j = me // low
    blk = flat.shape[0] // high
    total = lax.dynamic_slice_in_dim(flat, j * blk, blk, 0)
    for d in range(1, high):
        send = lax.dynamic_slice_in_dim(flat, ((j + d) % high) * blk, blk, 0)
        pairs = [
            (a * low + b, ((a + d) % high) * low + b) for a in range(high) for b in range(low)
        ]
        total = total + lax.ppermute(send, axis, pairs)
    return total


def direct_gather(piece, axis, low, high):
    me = lax.axis_index(axis)
    j = me // low
    out = jnp.zeros((high,) + piece.shape, piece.dtype)
    out = lax.dynamic_update_index_in_dim(out, piece, j, 0)
    for d in range(1, high):
        pairs = [
            (a * low + b, ((a + d) % high) * low + b) for a in range(high) for b in range(low)
        ]
        got = lax.ppermute(piece, axis, pairs)
        out = lax.dynamic_update_index_in_dim(out, got, (j - d) % high, 0)
    return out.reshape((-1,) + piece.shape[1:])


def is_pow2(n):
    return n >= 1 and (n & (n - 1)) == 0


def all_sum_rounded(flat, scale):
    n_tm = lax.axis_size("tm")
    n_sp = lax.axis_size("space")
    if not (is_pow2(n_tm) and is_pow2(n_sp)):
        return (lax.psum(flat, ("tm", "space")) * scale).astype(jnp.bfloat16)
    high = min(4, n_sp)
    low = n_sp // high
    tm_steps = []
    s = 1
    while s < n_tm:
        tm_steps.append(s)
        s *= 2
    sp_steps = []
    s = 1
    while s < low:
        sp_steps.append(s)
        s *= 2
    rows = flat.shape[0]
    unit = n_tm * n_sp * 8
    padded_rows = -(-rows // unit) * unit
    if padded_rows != rows:
        flat = jnp.pad(flat, ((0, padded_rows - rows), (0, 0)))
    flat = xor_halving(flat, "tm", tm_steps)
    flat = xor_halving(flat, "space", sp_steps)
    flat = direct_scatter(flat, "space", low, high)
    piece = (flat * scale).astype(jnp.bfloat16)
    piece = direct_gather(piece, "space", low, high)
    piece = xor_doubling(piece, "space", sp_steps)
    piece = xor_doubling(piece, "tm", tm_steps)
    return piece[:rows]


def spatial_sum(padded, weights, flip):
    rows = padded.shape[2] - 2
    cols = padded.shape[3] - 2
    total = jnp.zeros(padded.shape[:2] + (rows, cols, weights.shape[2]), jnp.float32)
    for row_off in range(3):
        for col_off in range(3):
            if flip:
                piece = padded[
                    :, :, 2 - row_off : 2 - row_off + rows, 2 - col_off : 2 - col_off + cols
                ]
                kernel = weights[3 * row_off + col_off].T
            else:
                piece = padded[:, :, row_off : row_off + rows, col_off : col_off + cols]
                kernel = weights[3 * row_off + col_off]
            total = total + jnp.dot(piece, kernel, preferred_element_type=jnp.float32)
    return total


def lag_forward(padded_act, weights, count):
    total = 0.0
    for lag in range(3):
        total = total + jnp.dot(
            padded_act[:, 2 - lag : 2 - lag + count],
            weights[lag],
            preferred_element_type=jnp.float32,
        )
    return total


def lag_backward(padded_cot, weights, count):
    total = 0.0
    for lag in range(3):
        total = total + jnp.dot(
            padded_cot[:, lag : lag + count], weights[lag].T, preferred_element_type=jnp.float32
        )
    return total


def lag_grads(act, padded_cot, count):
    dims = (((0, 1, 2, 3), (0, 1, 2, 3)), ((), ()))
    terms = []
    for lag in range(3):
        terms.append(
            lax.dot_general(
                act,
                padded_cot[:, lag : lag + count],
                dims,
                preferred_element_type=jnp.float32,
            )
        )
    return jnp.stack(terms)


def row_halo(x):
    if lax.axis_size("tm") == 2:
        me = lax.axis_index("tm")
        edge = jnp.where(me == 0, x[:, :, -1:], x[:, :, :1])
        got = lax.ppermute(edge, "tm", [(0, 1), (1, 0)])
        zero = jnp.zeros_like(got)
        above = jnp.where(me == 1, got, zero)
        below = jnp.where(me == 0, got, zero)
        return jnp.concatenate([above, x, below], axis=2)
    above = shifted(x[:, :, -1:], "tm", 1)
    below = shifted(x[:, :, :1], "tm", -1)
    return jnp.concatenate([above, x, below], axis=2)


def on_device(latents, cotangent, valid_frames, spatial_weight, temporal_weight, cond_weight):
    clips, frames, rows, cols, chans = latents.shape
    slab = lax.axis_index("space")
    frame_ids = slab * frames + jnp.arange(frames, dtype=jnp.int32)
    mask = (frame_ids[None, :] < valid_frames[:, None]).astype(jnp.bfloat16)[:, :, None, None, None]
    mask_f = mask.astype(jnp.float32)
    masked = latents * mask
    cot = cotangent * mask
    first = tree_broadcast(masked[:, 0], "space")
    cot_local = jnp.sum(cot, axis=1, dtype=jnp.float32)
    later = shifted(cot, "space", -1)
    if lax.axis_size("space") % 2 == 0:
        cot_pair = cot_local + jnp.sum(later, axis=1, dtype=jnp.float32)
        cot_sum = tree_reduce(cot_pair, "space", 2)
    else:
        cot_sum = tree_reduce(cot_local, "space")
    rows_pad = row_halo(masked)
    padded = jnp.pad(rows_pad, ((0, 0), (0, 0), (0, 0), (1, 1), (0, 0)))
    pre = spatial_sum(padded, spatial_weight, False)
    act = jax.nn.silu(pre).astype(jnp.bfloat16)
    earlier = shifted(act, "space", 1)
    act_pad = jnp.concatenate([earlier, act], axis=1)
    mixed = lag_forward(act_pad, temporal_weight, frames)
    cot_pad = jnp.concatenate([cot, later], axis=1)
    dact = lag_backward(cot_pad, temporal_weight, frames)
    temporal_terms = lag_grads(act, cot_pad, frames)
    cond = jnp.dot(first, cond_weight, preferred_element_type=jnp.float32)
    output = ((masked.astype(jnp.float32) + mixed + cond[:, None]) * mask_f).astype(jnp.bfloat16)
    sig = jax.nn.sigmoid(pre)
    dpre = (dact * sig * (1.0 + pre * (1.0 - sig))).astype(jnp.bfloat16)
    cond_back = jnp.dot(cot_sum, cond_weight.astype(jnp.float32).T, precision=lax.Precision.HIGHEST)
    dpre_rows = row_halo(dpre)
    dpre_pad = jnp.pad(dpre_rows, ((0, 0), (0, 0), (0, 0), (1, 1), (0, 0)))
    dmasked = spatial_sum(dpre_pad, spatial_weight, True)
    is_first = (frame_ids == 0).astype(jnp.float32)[None, :, None, None, None]
    grad_latents = (
        (cot.astype(jnp.float32) + dmasked + is_first * cond_back[:, None]) * mask_f
    ).astype(jnp.bfloat16)
    dims = (((0, 1, 2, 3), (0, 1, 2, 3)), ((), ()))
    spatial_terms = []
    for row_off in range(3):
        for col_off in range(3):
            piece = padded[:, :, row_off : row_off + rows, col_off : col_off + cols]
            spatial_terms.append(
                lax.dot_general(piece, dpre, dims, preferred_element_type=jnp.float32)
            )
    spatial_terms = jnp.stack(spatial_terms)
    cond_terms = lax.dot_general(
        first.astype(jnp.float32),
        cot_local,
        (((0, 1, 2), (0, 1, 2)), ((), ())),
        precision=lax.Precision.HIGHEST,
    )
    taps_s = spatial_terms.shape[0]
    taps_t = temporal_terms.shape[0]
    flat = jnp.concatenate(
        [
            spatial_terms.reshape(-1, chans),
            temporal_terms.reshape(-1, chans),
            cond_terms.reshape(-1, chans),
        ],
        axis=0,
    )
    scale = (clips * frames * rows * cols * lax.axis_size("space") * lax.axis_size("tm")) ** (-0.5)
    summed = all_sum_rounded(flat, scale)
    n_s = taps_s * chans
    n_t = taps_t * chans
    grad_spatial = summed[:n_s].reshape(taps_s, chans, chans)
    grad_temporal = summed[n_s : n_s + n_t].reshape(taps_t, chans, chans)
    grad_cond = summed[n_s + n_t :]
    return (output, grad_latents, grad_spatial, grad_temporal, grad_cond)


def solution(mesh):
    return jax.shard_map(
        on_device,
        mesh=mesh,
        in_specs=(
            P("groups", "space", "tm", None, None),
            P("groups", "space", "tm", None, None),
            P("groups"),
            P(),
            P(),
            P(),
        ),
        out_specs=(
            P("groups", "space", "tm", None, None),
            P("groups", "space", "tm", None, None),
            P("groups", None, None),
            P("groups", None, None),
            P("groups", None),
        ),
        check_vma=False,
    )
```

```python
import jax
import jax.numpy as jnp
from jax import lax
from jax.sharding import PartitionSpec as P


def shifted(value, axis, by):
    count = lax.axis_size(axis)
    pairs = [(i, i + by) for i in range(count) if 0 <= i + by < count]
    return lax.ppermute(value, axis, pairs)


def tree_broadcast(value, axis):
    count = lax.axis_size(axis)
    me = lax.axis_index(axis)
    step = 1
    while step * 2 < count:
        step *= 2
    while step >= 1 and count > 1:
        pairs = [(i, i + step) for i in range(0, count, 2 * step) if i + step < count]
        got = lax.ppermute(value, axis, pairs)
        value = jnp.where(me % (2 * step) == step, got, value)
        step //= 2
    return value


def tree_reduce(value, axis, step=1):
    count = lax.axis_size(axis)
    while step < count:
        pairs = [(i + step, i) for i in range(0, count, 2 * step) if i + step < count]
        value = value + lax.ppermute(value, axis, pairs)
        step *= 2
    return value


def xor_halving(flat, axis, steps):
    me = lax.axis_index(axis)
    count = lax.axis_size(axis)
    for step in steps:
        half = flat.shape[0] // 2
        upper = (me // step) % 2
        keep = lax.dynamic_slice_in_dim(flat, upper * half, half, 0)
        send = lax.dynamic_slice_in_dim(flat, (1 - upper) * half, half, 0)
        pairs = [(i, i ^ step) for i in range(count)]
        flat = keep + lax.ppermute(send, axis, pairs)
    return flat


def xor_doubling(piece, axis, steps):
    me = lax.axis_index(axis)
    count = lax.axis_size(axis)
    for step in reversed(steps):
        got = lax.ppermute(piece, axis, [(i, i ^ step) for i in range(count)])
        upper = (me // step) % 2 == 1
        piece = jnp.where(
            upper, jnp.concatenate([got, piece], 0), jnp.concatenate([piece, got], 0)
        )
    return piece


def direct_scatter(flat, axis, low, high):
    me = lax.axis_index(axis)
    j = me // low
    blk = flat.shape[0] // high
    total = lax.dynamic_slice_in_dim(flat, j * blk, blk, 0)
    for d in range(1, high):
        send = lax.dynamic_slice_in_dim(flat, ((j + d) % high) * blk, blk, 0)
        pairs = [
            (a * low + b, ((a + d) % high) * low + b) for a in range(high) for b in range(low)
        ]
        total = total + lax.ppermute(send, axis, pairs)
    return total


def direct_gather(piece, axis, low, high):
    me = lax.axis_index(axis)
    j = me // low
    out = jnp.zeros((high,) + piece.shape, piece.dtype)
    out = lax.dynamic_update_index_in_dim(out, piece, j, 0)
    for d in range(1, high):
        pairs = [
            (a * low + b, ((a + d) % high) * low + b) for a in range(high) for b in range(low)
        ]
        got = lax.ppermute(piece, axis, pairs)
        out = lax.dynamic_update_index_in_dim(out, got, (j - d) % high, 0)
    return out.reshape((-1,) + piece.shape[1:])


def is_pow2(n):
    return n >= 1 and (n & (n - 1)) == 0


def all_sum_rounded(flat, scale):
    n_tm = lax.axis_size("tm")
    n_sp = lax.axis_size("space")
    if not (is_pow2(n_tm) and is_pow2(n_sp)):
        return (lax.psum(flat, ("tm", "space")) * scale).astype(jnp.bfloat16)
    high = min(4, n_sp)
    low = n_sp // high
    tm_steps = []
    s = 1
    while s < n_tm:
        tm_steps.append(s)
        s *= 2
    sp_steps = []
    s = 1
    while s < low:
        sp_steps.append(s)
        s *= 2
    rows = flat.shape[0]
    unit = n_tm * n_sp * 8
    padded_rows = -(-rows // unit) * unit
    if padded_rows != rows:
        flat = jnp.pad(flat, ((0, padded_rows - rows), (0, 0)))
    flat = xor_halving(flat, "tm", tm_steps)
    flat = xor_halving(flat, "space", sp_steps)
    flat = direct_scatter(flat, "space", low, high)
    piece = (flat * scale).astype(jnp.bfloat16)
    piece = direct_gather(piece, "space", low, high)
    piece = xor_doubling(piece, "space", sp_steps)
    piece = xor_doubling(piece, "tm", tm_steps)
    return piece[:rows]


def spatial_sum(padded, weights, flip):
    rows = padded.shape[2] - 2
    cols = padded.shape[3] - 2
    total = jnp.zeros(padded.shape[:2] + (rows, cols, weights.shape[2]), jnp.float32)
    for row_off in range(3):
        for col_off in range(3):
            if flip:
                piece = padded[
                    :, :, 2 - row_off : 2 - row_off + rows, 2 - col_off : 2 - col_off + cols
                ]
                kernel = weights[3 * row_off + col_off].T
            else:
                piece = padded[:, :, row_off : row_off + rows, col_off : col_off + cols]
                kernel = weights[3 * row_off + col_off]
            total = total + jnp.dot(piece, kernel, preferred_element_type=jnp.float32)
    return total


def lag_forward(padded_act, weights, count):
    total = 0.0
    for lag in range(3):
        total = total + jnp.dot(
            padded_act[:, 2 - lag : 2 - lag + count],
            weights[lag],
            preferred_element_type=jnp.float32,
        )
    return total


def lag_backward(padded_cot, weights, count):
    total = 0.0
    for lag in range(3):
        total = total + jnp.dot(
            padded_cot[:, lag : lag + count], weights[lag].T, preferred_element_type=jnp.float32
        )
    return total


def lag_grads(act, padded_cot, count):
    dims = (((0, 1, 2, 3), (0, 1, 2, 3)), ((), ()))
    terms = []
    for lag in range(3):
        terms.append(
            lax.dot_general(
                act,
                padded_cot[:, lag : lag + count],
                dims,
                preferred_element_type=jnp.float32,
            )
        )
    return jnp.stack(terms)


def row_halo(x):
    if lax.axis_size("tm") == 2:
        me = lax.axis_index("tm")
        edge = jnp.where(me == 0, x[:, :, -1:], x[:, :, :1])
        got = lax.ppermute(edge, "tm", [(0, 1), (1, 0)])
        zero = jnp.zeros_like(got)
        above = jnp.where(me == 1, got, zero)
        below = jnp.where(me == 0, got, zero)
        return jnp.concatenate([above, x, below], axis=2)
    above = shifted(x[:, :, -1:], "tm", 1)
    below = shifted(x[:, :, :1], "tm", -1)
    return jnp.concatenate([above, x, below], axis=2)


def on_device(latents, cotangent, valid_frames, spatial_weight, temporal_weight, cond_weight):
    clips, frames, rows, cols, chans = latents.shape
    slab = lax.axis_index("space")
    frame_ids = slab * frames + jnp.arange(frames, dtype=jnp.int32)
    mask = (frame_ids[None, :] < valid_frames[:, None]).astype(jnp.bfloat16)[:, :, None, None, None]
    mask_f = mask.astype(jnp.float32)
    masked = latents * mask
    cot = cotangent * mask
    first = tree_broadcast(masked[:, 0], "space")
    cot_local = jnp.sum(cot, axis=1, dtype=jnp.float32)
    later = shifted(cot, "space", -1)
    if lax.axis_size("space") % 2 == 0:
        cot_pair = cot_local + jnp.sum(later, axis=1, dtype=jnp.float32)
        cot_sum = tree_reduce(cot_pair, "space", 2)
    else:
        cot_sum = tree_reduce(cot_local, "space")
    rows_pad = row_halo(masked)
    padded = jnp.pad(rows_pad, ((0, 0), (0, 0), (0, 0), (1, 1), (0, 0)))
    pre = spatial_sum(padded, spatial_weight, False)
    act = jax.nn.silu(pre).astype(jnp.bfloat16)
    act_out, first = lax.optimization_barrier((act, first))
    earlier = shifted(act_out, "space", 1)
    act_pad = jnp.concatenate([earlier, act], axis=1)
    mixed = lag_forward(act_pad, temporal_weight, frames)
    cot_pad = jnp.concatenate([cot, later], axis=1)
    dact = lag_backward(cot_pad, temporal_weight, frames)
    temporal_terms = lag_grads(act, cot_pad, frames)
    cond = jnp.dot(first, cond_weight, preferred_element_type=jnp.float32)
    output = ((masked.astype(jnp.float32) + mixed + cond[:, None]) * mask_f).astype(jnp.bfloat16)
    sig = jax.nn.sigmoid(pre)
    dpre = (dact * sig * (1.0 + pre * (1.0 - sig))).astype(jnp.bfloat16)
    cond_back = jnp.dot(cot_sum, cond_weight.astype(jnp.float32).T, precision=lax.Precision.HIGHEST)
    dpre_rows = row_halo(dpre)
    dpre_pad = jnp.pad(dpre_rows, ((0, 0), (0, 0), (0, 0), (1, 1), (0, 0)))
    dmasked = spatial_sum(dpre_pad, spatial_weight, True)
    is_first = (frame_ids == 0).astype(jnp.float32)[None, :, None, None, None]
    grad_latents = (
        (cot.astype(jnp.float32) + dmasked + is_first * cond_back[:, None]) * mask_f
    ).astype(jnp.bfloat16)
    dims = (((0, 1, 2, 3), (0, 1, 2, 3)), ((), ()))
    spatial_terms = []
    for row_off in range(3):
        for col_off in range(3):
            piece = padded[:, :, row_off : row_off + rows, col_off : col_off + cols]
            spatial_terms.append(
                lax.dot_general(piece, dpre, dims, preferred_element_type=jnp.float32)
            )
    spatial_terms = jnp.stack(spatial_terms)
    cond_terms = lax.dot_general(
        first.astype(jnp.float32),
        cot_local,
        (((0, 1, 2), (0, 1, 2)), ((), ())),
        precision=lax.Precision.HIGHEST,
    )
    taps_s = spatial_terms.shape[0]
    taps_t = temporal_terms.shape[0]
    flat = jnp.concatenate(
        [
            spatial_terms.reshape(-1, chans),
            temporal_terms.reshape(-1, chans),
            cond_terms.reshape(-1, chans),
        ],
        axis=0,
    )
    scale = (clips * frames * rows * cols * lax.axis_size("space") * lax.axis_size("tm")) ** (-0.5)
    summed = all_sum_rounded(flat, scale)
    n_s = taps_s * chans
    n_t = taps_t * chans
    grad_spatial = summed[:n_s].reshape(taps_s, chans, chans)
    grad_temporal = summed[n_s : n_s + n_t].reshape(taps_t, chans, chans)
    grad_cond = summed[n_s + n_t :]
    return (output, grad_latents, grad_spatial, grad_temporal, grad_cond)


def solution(mesh):
    return jax.shard_map(
        on_device,
        mesh=mesh,
        in_specs=(
            P("groups", "space", "tm", None, None),
            P("groups", "space", "tm", None, None),
            P("groups"),
            P(),
            P(),
            P(),
        ),
        out_specs=(
            P("groups", "space", "tm", None, None),
            P("groups", "space", "tm", None, None),
            P("groups", None, None),
            P("groups", None, None),
            P("groups", None),
        ),
        check_vma=False,
    )
```

```python
import jax
import jax.numpy as jnp
from jax import lax
from jax.sharding import PartitionSpec as P


def shifted(value, axis, by):
    count = lax.axis_size(axis)
    pairs = [(i, i + by) for i in range(count) if 0 <= i + by < count]
    return lax.ppermute(value, axis, pairs)


def tree_broadcast(value, axis):
    count = lax.axis_size(axis)
    me = lax.axis_index(axis)
    step = 1
    while step * 2 < count:
        step *= 2
    while step >= 1 and count > 1:
        pairs = [(i, i + step) for i in range(0, count, 2 * step) if i + step < count]
        got = lax.ppermute(value, axis, pairs)
        value = jnp.where(me % (2 * step) == step, got, value)
        step //= 2
    return value


def tree_reduce(value, axis, step=1, stop=None):
    count = lax.axis_size(axis)
    stop = count if stop is None else stop
    while step < min(count, stop):
        pairs = [(i + step, i) for i in range(0, count, 2 * step) if i + step < count]
        value = value + lax.ppermute(value, axis, pairs)
        step *= 2
    return value


def xor_halving(flat, axis, steps):
    me = lax.axis_index(axis)
    count = lax.axis_size(axis)
    for step in steps:
        half = flat.shape[0] // 2
        upper = (me // step) % 2
        keep = lax.dynamic_slice_in_dim(flat, upper * half, half, 0)
        send = lax.dynamic_slice_in_dim(flat, (1 - upper) * half, half, 0)
        pairs = [(i, i ^ step) for i in range(count)]
        flat = keep + lax.ppermute(send, axis, pairs)
    return flat


def xor_doubling(piece, axis, steps):
    me = lax.axis_index(axis)
    count = lax.axis_size(axis)
    for step in reversed(steps):
        got = lax.ppermute(piece, axis, [(i, i ^ step) for i in range(count)])
        upper = (me // step) % 2 == 1
        piece = jnp.where(
            upper, jnp.concatenate([got, piece], 0), jnp.concatenate([piece, got], 0)
        )
    return piece


def direct_scatter(flat, axis, low, high):
    me = lax.axis_index(axis)
    j = me // low
    blk = flat.shape[0] // high
    total = lax.dynamic_slice_in_dim(flat, j * blk, blk, 0)
    for d in range(1, high):
        send = lax.dynamic_slice_in_dim(flat, ((j + d) % high) * blk, blk, 0)
        pairs = [
            (a * low + b, ((a + d) % high) * low + b) for a in range(high) for b in range(low)
        ]
        total = total + lax.ppermute(send, axis, pairs)
    return total


def direct_gather(piece, axis, low, high):
    me = lax.axis_index(axis)
    j = me // low
    out = jnp.zeros((high,) + piece.shape, piece.dtype)
    out = lax.dynamic_update_index_in_dim(out, piece, j, 0)
    for d in range(1, high):
        pairs = [
            (a * low + b, ((a + d) % high) * low + b) for a in range(high) for b in range(low)
        ]
        got = lax.ppermute(piece, axis, pairs)
        out = lax.dynamic_update_index_in_dim(out, got, (j - d) % high, 0)
    return out.reshape((-1,) + piece.shape[1:])


def is_pow2(n):
    return n >= 1 and (n & (n - 1)) == 0


def all_sum_rounded(flat, scale):
    n_tm = lax.axis_size("tm")
    n_sp = lax.axis_size("space")
    if not (is_pow2(n_tm) and is_pow2(n_sp)):
        return (lax.psum(flat, ("tm", "space")) * scale).astype(jnp.bfloat16)
    high = min(4, n_sp)
    low = n_sp // high
    tm_steps = []
    s = 1
    while s < n_tm:
        tm_steps.append(s)
        s *= 2
    sp_steps = []
    s = 1
    while s < low:
        sp_steps.append(s)
        s *= 2
    rows = flat.shape[0]
    unit = n_tm * n_sp * 8
    padded_rows = -(-rows // unit) * unit
    if padded_rows != rows:
        flat = jnp.pad(flat, ((0, padded_rows - rows), (0, 0)))
    flat = xor_halving(flat, "tm", tm_steps)
    flat = xor_halving(flat, "space", sp_steps)
    flat = direct_scatter(flat, "space", low, high)
    piece = (flat * scale).astype(jnp.bfloat16)
    piece = direct_gather(piece, "space", low, high)
    piece = xor_doubling(piece, "space", sp_steps)
    piece = xor_doubling(piece, "tm", tm_steps)
    return piece[:rows]


def spatial_sum(padded, weights, flip):
    rows = padded.shape[2] - 2
    cols = padded.shape[3] - 2
    total = jnp.zeros(padded.shape[:2] + (rows, cols, weights.shape[2]), jnp.float32)
    for row_off in range(3):
        for col_off in range(3):
            if flip:
                piece = padded[
                    :, :, 2 - row_off : 2 - row_off + rows, 2 - col_off : 2 - col_off + cols
                ]
                kernel = weights[3 * row_off + col_off].T
            else:
                piece = padded[:, :, row_off : row_off + rows, col_off : col_off + cols]
                kernel = weights[3 * row_off + col_off]
            total = total + jnp.dot(piece, kernel, preferred_element_type=jnp.float32)
    return total


def lag_forward(padded_act, weights, count):
    total = 0.0
    for lag in range(3):
        total = total + jnp.dot(
            padded_act[:, 2 - lag : 2 - lag + count],
            weights[lag],
            preferred_element_type=jnp.float32,
        )
    return total


def lag_backward(padded_cot, weights, count):
    total = 0.0
    for lag in range(3):
        total = total + jnp.dot(
            padded_cot[:, lag : lag + count], weights[lag].T, preferred_element_type=jnp.float32
        )
    return total


def lag_grads(act, padded_cot, count):
    dims = (((0, 1, 2, 3), (0, 1, 2, 3)), ((), ()))
    terms = []
    for lag in range(3):
        terms.append(
            lax.dot_general(
                act,
                padded_cot[:, lag : lag + count],
                dims,
                preferred_element_type=jnp.float32,
            )
        )
    return jnp.stack(terms)


def row_halo(x):
    if lax.axis_size("tm") == 2:
        me = lax.axis_index("tm")
        edge = jnp.where(me == 0, x[:, :, -1:], x[:, :, :1])
        got = lax.ppermute(edge, "tm", [(0, 1), (1, 0)])
        zero = jnp.zeros_like(got)
        above = jnp.where(me == 1, got, zero)
        below = jnp.where(me == 0, got, zero)
        return jnp.concatenate([above, x, below], axis=2)
    above = shifted(x[:, :, -1:], "tm", 1)
    below = shifted(x[:, :, :1], "tm", -1)
    return jnp.concatenate([above, x, below], axis=2)


def on_device(latents, cotangent, valid_frames, spatial_weight, temporal_weight, cond_weight):
    clips, frames, rows, cols, chans = latents.shape
    slab = lax.axis_index("space")
    frame_ids = slab * frames + jnp.arange(frames, dtype=jnp.int32)
    mask = (frame_ids[None, :] < valid_frames[:, None]).astype(jnp.bfloat16)[:, :, None, None, None]
    mask_f = mask.astype(jnp.float32)
    masked = latents * mask
    cot = cotangent * mask
    first = tree_broadcast(masked[:, 0], "space")
    cot_local = jnp.sum(cot, axis=1, dtype=jnp.float32)
    later = shifted(cot, "space", -1)
    if lax.axis_size("space") % 2 == 0:
        cot_pair = cot_local + jnp.sum(later, axis=1, dtype=jnp.float32)
        cot_part = tree_reduce(cot_pair, "space", 2, 4)
    else:
        cot_part = tree_reduce(cot_local, "space", 1, 2)
    rows_pad = row_halo(masked)
    padded = jnp.pad(rows_pad, ((0, 0), (0, 0), (0, 0), (1, 1), (0, 0)))
    pre = spatial_sum(padded, spatial_weight, False)
    act = jax.nn.silu(pre).astype(jnp.bfloat16)
    earlier = shifted(act, "space", 1)
    act_pad = jnp.concatenate([earlier, act], axis=1)
    mixed = lag_forward(act_pad, temporal_weight, frames)
    cot_pad = jnp.concatenate([cot, later], axis=1)
    dact = lag_backward(cot_pad, temporal_weight, frames)
    temporal_terms = lag_grads(act, cot_pad, frames)
    cond = jnp.dot(first, cond_weight, preferred_element_type=jnp.float32)
    output = ((masked.astype(jnp.float32) + mixed + cond[:, None]) * mask_f).astype(jnp.bfloat16)
    sig = jax.nn.sigmoid(pre)
    dpre = (dact * sig * (1.0 + pre * (1.0 - sig))).astype(jnp.bfloat16)
    dpre_rows = row_halo(dpre)
    dpre_pad = jnp.pad(dpre_rows, ((0, 0), (0, 0), (0, 0), (1, 1), (0, 0)))
    dmasked = spatial_sum(dpre_pad, spatial_weight, True)
    dims = (((0, 1, 2, 3), (0, 1, 2, 3)), ((), ()))
    spatial_terms = []
    for row_off in range(3):
        for col_off in range(3):
            piece = padded[:, :, row_off : row_off + rows, col_off : col_off + cols]
            spatial_terms.append(
                lax.dot_general(piece, dpre, dims, preferred_element_type=jnp.float32)
            )
    spatial_terms = jnp.stack(spatial_terms)
    cond_terms = lax.dot_general(
        first.astype(jnp.float32),
        cot_local,
        (((0, 1, 2), (0, 1, 2)), ((), ())),
        precision=lax.Precision.HIGHEST,
    )
    taps_s = spatial_terms.shape[0]
    taps_t = temporal_terms.shape[0]
    flat = jnp.concatenate(
        [
            spatial_terms.reshape(-1, chans),
            temporal_terms.reshape(-1, chans),
            cond_terms.reshape(-1, chans),
        ],
        axis=0,
    )
    scale = (clips * frames * rows * cols * lax.axis_size("space") * lax.axis_size("tm")) ** (-0.5)
    flat, cot_part = lax.optimization_barrier((flat, cot_part))
    if lax.axis_size("space") % 2 == 0:
        cot_sum = tree_reduce(cot_part, "space", 4)
    else:
        cot_sum = tree_reduce(cot_part, "space", 2)
    summed = all_sum_rounded(flat, scale)
    cond_back = jnp.dot(cot_sum, cond_weight.astype(jnp.float32).T, precision=lax.Precision.HIGHEST)
    is_first = (frame_ids == 0).astype(jnp.float32)[None, :, None, None, None]
    grad_latents = (
        (cot.astype(jnp.float32) + dmasked + is_first * cond_back[:, None]) * mask_f
    ).astype(jnp.bfloat16)
    n_s = taps_s * chans
    n_t = taps_t * chans
    grad_spatial = summed[:n_s].reshape(taps_s, chans, chans)
    grad_temporal = summed[n_s : n_s + n_t].reshape(taps_t, chans, chans)
    grad_cond = summed[n_s + n_t :]
    return (output, grad_latents, grad_spatial, grad_temporal, grad_cond)


def solution(mesh):
    return jax.shard_map(
        on_device,
        mesh=mesh,
        in_specs=(
            P("groups", "space", "tm", None, None),
            P("groups", "space", "tm", None, None),
            P("groups"),
            P(),
            P(),
            P(),
        ),
        out_specs=(
            P("groups", "space", "tm", None, None),
            P("groups", "space", "tm", None, None),
            P("groups", None, None),
            P("groups", None, None),
            P("groups", None),
        ),
        check_vma=False,
    )
```

```python
import jax
import jax.numpy as jnp
from jax import lax
from jax.sharding import PartitionSpec as P


def shifted(value, axis, by):
    count = lax.axis_size(axis)
    pairs = [(i, i + by) for i in range(count) if 0 <= i + by < count]
    return lax.ppermute(value, axis, pairs)


def tree_broadcast(value, axis):
    count = lax.axis_size(axis)
    me = lax.axis_index(axis)
    step = 1
    while step * 2 < count:
        step *= 2
    while step >= 1 and count > 1:
        pairs = [(i, i + step) for i in range(0, count, 2 * step) if i + step < count]
        got = lax.ppermute(value, axis, pairs)
        value = jnp.where(me % (2 * step) == step, got, value)
        step //= 2
    return value


def tree_reduce(value, axis, step=1):
    count = lax.axis_size(axis)
    while step < count:
        pairs = [(i + step, i) for i in range(0, count, 2 * step) if i + step < count]
        value = value + lax.ppermute(value, axis, pairs)
        step *= 2
    return value


def xor_halving(flat, axis, steps):
    me = lax.axis_index(axis)
    count = lax.axis_size(axis)
    for step in steps:
        half = flat.shape[0] // 2
        upper = (me // step) % 2
        keep = lax.dynamic_slice_in_dim(flat, upper * half, half, 0)
        send = lax.dynamic_slice_in_dim(flat, (1 - upper) * half, half, 0)
        pairs = [(i, i ^ step) for i in range(count)]
        flat = keep + lax.ppermute(send, axis, pairs)
    return flat


def xor_doubling(piece, axis, steps):
    me = lax.axis_index(axis)
    count = lax.axis_size(axis)
    for step in reversed(steps):
        got = lax.ppermute(piece, axis, [(i, i ^ step) for i in range(count)])
        upper = (me // step) % 2 == 1
        piece = jnp.where(
            upper, jnp.concatenate([got, piece], 0), jnp.concatenate([piece, got], 0)
        )
    return piece


def direct_scatter(flat, axis, low, high):
    me = lax.axis_index(axis)
    j = me // low
    blk = flat.shape[0] // high
    total = lax.dynamic_slice_in_dim(flat, j * blk, blk, 0)
    for d in range(1, high):
        send = lax.dynamic_slice_in_dim(flat, ((j + d) % high) * blk, blk, 0)
        pairs = [
            (a * low + b, ((a + d) % high) * low + b) for a in range(high) for b in range(low)
        ]
        total = total + lax.ppermute(send, axis, pairs)
    return total


def direct_gather(piece, axis, low, high):
    me = lax.axis_index(axis)
    j = me // low
    out = jnp.zeros((high,) + piece.shape, piece.dtype)
    out = lax.dynamic_update_index_in_dim(out, piece, j, 0)
    for d in range(1, high):
        pairs = [
            (a * low + b, ((a + d) % high) * low + b) for a in range(high) for b in range(low)
        ]
        got = lax.ppermute(piece, axis, pairs)
        out = lax.dynamic_update_index_in_dim(out, got, (j - d) % high, 0)
    return out.reshape((-1,) + piece.shape[1:])


def is_pow2(n):
    return n >= 1 and (n & (n - 1)) == 0


def all_sum_rounded(flat, scale):
    n_tm = lax.axis_size("tm")
    n_sp = lax.axis_size("space")
    if not (is_pow2(n_tm) and is_pow2(n_sp)):
        return (lax.psum(flat, ("tm", "space")) * scale).astype(jnp.bfloat16)
    high = min(4, n_sp)
    low = n_sp // high
    tm_steps = []
    s = 1
    while s < n_tm:
        tm_steps.append(s)
        s *= 2
    sp_steps = []
    s = 1
    while s < low:
        sp_steps.append(s)
        s *= 2
    rows = flat.shape[0]
    unit = n_tm * n_sp * 8
    padded_rows = -(-rows // unit) * unit
    if padded_rows != rows:
        flat = jnp.pad(flat, ((0, padded_rows - rows), (0, 0)))
    flat = xor_halving(flat, "tm", tm_steps)
    flat = direct_scatter(flat, "space", low, high)
    flat = xor_halving(flat, "space", sp_steps)
    piece = (flat * scale).astype(jnp.bfloat16)
    piece = xor_doubling(piece, "space", sp_steps)
    piece = direct_gather(piece, "space", low, high)
    piece = xor_doubling(piece, "tm", tm_steps)
    return piece[:rows]


def spatial_sum(padded, weights, flip):
    rows = padded.shape[2] - 2
    cols = padded.shape[3] - 2
    total = jnp.zeros(padded.shape[:2] + (rows, cols, weights.shape[2]), jnp.float32)
    for row_off in range(3):
        for col_off in range(3):
            if flip:
                piece = padded[
                    :, :, 2 - row_off : 2 - row_off + rows, 2 - col_off : 2 - col_off + cols
                ]
                kernel = weights[3 * row_off + col_off].T
            else:
                piece = padded[:, :, row_off : row_off + rows, col_off : col_off + cols]
                kernel = weights[3 * row_off + col_off]
            total = total + jnp.dot(piece, kernel, preferred_element_type=jnp.float32)
    return total


def lag_forward(padded_act, weights, count):
    total = 0.0
    for lag in range(3):
        total = total + jnp.dot(
            padded_act[:, 2 - lag : 2 - lag + count],
            weights[lag],
            preferred_element_type=jnp.float32,
        )
    return total


def lag_backward(padded_cot, weights, count):
    total = 0.0
    for lag in range(3):
        total = total + jnp.dot(
            padded_cot[:, lag : lag + count], weights[lag].T, preferred_element_type=jnp.float32
        )
    return total


def lag_grads(act, padded_cot, count):
    dims = (((0, 1, 2, 3), (0, 1, 2, 3)), ((), ()))
    terms = []
    for lag in range(3):
        terms.append(
            lax.dot_general(
                act,
                padded_cot[:, lag : lag + count],
                dims,
                preferred_element_type=jnp.float32,
            )
        )
    return jnp.stack(terms)


def row_halo(x):
    if lax.axis_size("tm") == 2:
        me = lax.axis_index("tm")
        edge = jnp.where(me == 0, x[:, :, -1:], x[:, :, :1])
        got = lax.ppermute(edge, "tm", [(0, 1), (1, 0)])
        zero = jnp.zeros_like(got)
        above = jnp.where(me == 1, got, zero)
        below = jnp.where(me == 0, got, zero)
        return jnp.concatenate([above, x, below], axis=2)
    above = shifted(x[:, :, -1:], "tm", 1)
    below = shifted(x[:, :, :1], "tm", -1)
    return jnp.concatenate([above, x, below], axis=2)


def on_device(latents, cotangent, valid_frames, spatial_weight, temporal_weight, cond_weight):
    clips, frames, rows, cols, chans = latents.shape
    slab = lax.axis_index("space")
    frame_ids = slab * frames + jnp.arange(frames, dtype=jnp.int32)
    mask = (frame_ids[None, :] < valid_frames[:, None]).astype(jnp.bfloat16)[:, :, None, None, None]
    mask_f = mask.astype(jnp.float32)
    masked = latents * mask
    cot = cotangent * mask
    first = tree_broadcast(masked[:, 0], "space")
    cot_local = jnp.sum(cot, axis=1, dtype=jnp.float32)
    later = shifted(cot, "space", -1)
    if lax.axis_size("space") % 2 == 0:
        cot_pair = cot_local + jnp.sum(later, axis=1, dtype=jnp.float32)
        cot_sum = tree_reduce(cot_pair, "space", 2)
    else:
        cot_sum = tree_reduce(cot_local, "space")
    rows_pad = row_halo(masked)
    padded = jnp.pad(rows_pad, ((0, 0), (0, 0), (0, 0), (1, 1), (0, 0)))
    pre = spatial_sum(padded, spatial_weight, False)
    act = jax.nn.silu(pre).astype(jnp.bfloat16)
    earlier = shifted(act, "space", 1)
    act_pad = jnp.concatenate([earlier, act], axis=1)
    mixed = lag_forward(act_pad, temporal_weight, frames)
    cot_pad = jnp.concatenate([cot, later], axis=1)
    dact = lag_backward(cot_pad, temporal_weight, frames)
    temporal_terms = lag_grads(act, cot_pad, frames)
    cond = jnp.dot(first, cond_weight, preferred_element_type=jnp.float32)
    output = ((masked.astype(jnp.float32) + mixed + cond[:, None]) * mask_f).astype(jnp.bfloat16)
    sig = jax.nn.sigmoid(pre)
    dpre = (dact * sig * (1.0 + pre * (1.0 - sig))).astype(jnp.bfloat16)
    cond_back = jnp.dot(cot_sum, cond_weight.astype(jnp.float32).T, precision=lax.Precision.HIGHEST)
    dpre_rows = row_halo(dpre)
    dpre_pad = jnp.pad(dpre_rows, ((0, 0), (0, 0), (0, 0), (1, 1), (0, 0)))
    dmasked = spatial_sum(dpre_pad, spatial_weight, True)
    is_first = (frame_ids == 0).astype(jnp.float32)[None, :, None, None, None]
    grad_latents = (
        (cot.astype(jnp.float32) + dmasked + is_first * cond_back[:, None]) * mask_f
    ).astype(jnp.bfloat16)
    dims = (((0, 1, 2, 3), (0, 1, 2, 3)), ((), ()))
    spatial_terms = []
    for row_off in range(3):
        for col_off in range(3):
            piece = padded[:, :, row_off : row_off + rows, col_off : col_off + cols]
            spatial_terms.append(
                lax.dot_general(piece, dpre, dims, preferred_element_type=jnp.float32)
            )
    spatial_terms = jnp.stack(spatial_terms)
    cond_terms = lax.dot_general(
        first.astype(jnp.float32),
        cot_local,
        (((0, 1, 2), (0, 1, 2)), ((), ())),
        precision=lax.Precision.HIGHEST,
    )
    taps_s = spatial_terms.shape[0]
    taps_t = temporal_terms.shape[0]
    flat = jnp.concatenate(
        [
            spatial_terms.reshape(-1, chans),
            temporal_terms.reshape(-1, chans),
            cond_terms.reshape(-1, chans),
        ],
        axis=0,
    )
    scale = (clips * frames * rows * cols * lax.axis_size("space") * lax.axis_size("tm")) ** (-0.5)
    summed = all_sum_rounded(flat, scale)
    n_s = taps_s * chans
    n_t = taps_t * chans
    grad_spatial = summed[:n_s].reshape(taps_s, chans, chans)
    grad_temporal = summed[n_s : n_s + n_t].reshape(taps_t, chans, chans)
    grad_cond = summed[n_s + n_t :]
    return (output, grad_latents, grad_spatial, grad_temporal, grad_cond)


def solution(mesh):
    return jax.shard_map(
        on_device,
        mesh=mesh,
        in_specs=(
            P("groups", "space", "tm", None, None),
            P("groups", "space", "tm", None, None),
            P("groups"),
            P(),
            P(),
            P(),
        ),
        out_specs=(
            P("groups", "space", "tm", None, None),
            P("groups", "space", "tm", None, None),
            P("groups", None, None),
            P("groups", None, None),
            P("groups", None),
        ),
        check_vma=False,
    )
```

```python
import jax
import jax.numpy as jnp
from jax import lax
from jax.sharding import PartitionSpec as P


def shifted(value, axis, by):
    count = lax.axis_size(axis)
    pairs = [(i, i + by) for i in range(count) if 0 <= i + by < count]
    return lax.ppermute(value, axis, pairs)


def tree_broadcast(value, axis):
    count = lax.axis_size(axis)
    me = lax.axis_index(axis)
    step = 1
    while step * 2 < count:
        step *= 2
    while step >= 1 and count > 1:
        pairs = [(i, i + step) for i in range(0, count, 2 * step) if i + step < count]
        got = lax.ppermute(value, axis, pairs)
        value = jnp.where(me % (2 * step) == step, got, value)
        step //= 2
    return value


def tree_reduce(value, axis, step=1):
    count = lax.axis_size(axis)
    while step < count:
        pairs = [(i + step, i) for i in range(0, count, 2 * step) if i + step < count]
        value = value + lax.ppermute(value, axis, pairs)
        step *= 2
    return value


def xor_halving(flat, axis, steps):
    me = lax.axis_index(axis)
    count = lax.axis_size(axis)
    for step in steps:
        half = flat.shape[0] // 2
        upper = (me // step) % 2
        keep = lax.dynamic_slice_in_dim(flat, upper * half, half, 0)
        send = lax.dynamic_slice_in_dim(flat, (1 - upper) * half, half, 0)
        pairs = [(i, i ^ step) for i in range(count)]
        flat = keep + lax.ppermute(send, axis, pairs)
    return flat


def xor_doubling(piece, axis, steps):
    me = lax.axis_index(axis)
    count = lax.axis_size(axis)
    for step in reversed(steps):
        got = lax.ppermute(piece, axis, [(i, i ^ step) for i in range(count)])
        upper = (me // step) % 2 == 1
        piece = jnp.where(
            upper, jnp.concatenate([got, piece], 0), jnp.concatenate([piece, got], 0)
        )
    return piece


def direct_scatter(flat, axis, low, high):
    me = lax.axis_index(axis)
    j = me // low
    blk = flat.shape[0] // high
    total = lax.dynamic_slice_in_dim(flat, j * blk, blk, 0)
    for d in range(1, high):
        send = lax.dynamic_slice_in_dim(flat, ((j + d) % high) * blk, blk, 0)
        pairs = [
            (a * low + b, ((a + d) % high) * low + b) for a in range(high) for b in range(low)
        ]
        total = total + lax.ppermute(send, axis, pairs)
    return total


def direct_gather(piece, axis, low, high):
    me = lax.axis_index(axis)
    j = me // low
    out = jnp.zeros((high,) + piece.shape, piece.dtype)
    out = lax.dynamic_update_index_in_dim(out, piece, j, 0)
    for d in range(1, high):
        pairs = [
            (a * low + b, ((a + d) % high) * low + b) for a in range(high) for b in range(low)
        ]
        got = lax.ppermute(piece, axis, pairs)
        out = lax.dynamic_update_index_in_dim(out, got, (j - d) % high, 0)
    return out.reshape((-1,) + piece.shape[1:])


def is_pow2(n):
    return n >= 1 and (n & (n - 1)) == 0


def all_sum_rounded(flat, scale):
    n_tm = lax.axis_size("tm")
    n_sp = lax.axis_size("space")
    if not (is_pow2(n_tm) and is_pow2(n_sp)):
        return (lax.psum(flat, ("tm", "space")) * scale).astype(jnp.bfloat16)
    high = min(4, n_sp)
    low = n_sp // high
    tm_steps = []
    s = 1
    while s < n_tm:
        tm_steps.append(s)
        s *= 2
    sp_steps = []
    s = 1
    while s < low:
        sp_steps.append(s)
        s *= 2
    rows = flat.shape[0]
    unit = n_tm * n_sp * 8
    padded_rows = -(-rows // unit) * unit
    if padded_rows != rows:
        flat = jnp.pad(flat, ((0, padded_rows - rows), (0, 0)))
    flat = xor_halving(flat, "tm", tm_steps)
    flat = direct_scatter(flat, "space", low, high)
    flat = xor_halving(flat, "space", sp_steps)
    piece = (flat * scale).astype(jnp.bfloat16)
    piece = xor_doubling(piece, "space", sp_steps)
    piece = direct_gather(piece, "space", low, high)
    piece = xor_doubling(piece, "tm", tm_steps)
    return piece[:rows]


def spatial_sum(padded, weights, flip):
    rows = padded.shape[2] - 2
    cols = padded.shape[3] - 2
    total = jnp.zeros(padded.shape[:2] + (rows, cols, weights.shape[2]), jnp.float32)
    for row_off in range(3):
        for col_off in range(3):
            if flip:
                piece = padded[
                    :, :, 2 - row_off : 2 - row_off + rows, 2 - col_off : 2 - col_off + cols
                ]
                kernel = weights[3 * row_off + col_off].T
            else:
                piece = padded[:, :, row_off : row_off + rows, col_off : col_off + cols]
                kernel = weights[3 * row_off + col_off]
            total = total + jnp.dot(piece, kernel, preferred_element_type=jnp.float32)
    return total


def lag_forward(padded_act, weights, count):
    total = 0.0
    for lag in range(3):
        total = total + jnp.dot(
            padded_act[:, 2 - lag : 2 - lag + count],
            weights[lag],
            preferred_element_type=jnp.float32,
        )
    return total


def lag_backward(padded_cot, weights, count):
    total = 0.0
    for lag in range(3):
        total = total + jnp.dot(
            padded_cot[:, lag : lag + count], weights[lag].T, preferred_element_type=jnp.float32
        )
    return total


def lag_grads(act, padded_cot, count):
    dims = (((0, 1, 2, 3), (0, 1, 2, 3)), ((), ()))
    terms = []
    for lag in range(3):
        terms.append(
            lax.dot_general(
                act,
                padded_cot[:, lag : lag + count],
                dims,
                preferred_element_type=jnp.float32,
            )
        )
    return jnp.stack(terms)


def row_halo(x):
    if lax.axis_size("tm") == 2:
        me = lax.axis_index("tm")
        edge = jnp.where(me == 0, x[:, :, -1:], x[:, :, :1])
        got = lax.ppermute(edge, "tm", [(0, 1), (1, 0)])
        zero = jnp.zeros_like(got)
        above = jnp.where(me == 1, got, zero)
        below = jnp.where(me == 0, got, zero)
        return jnp.concatenate([above, x, below], axis=2)
    above = shifted(x[:, :, -1:], "tm", 1)
    below = shifted(x[:, :, :1], "tm", -1)
    return jnp.concatenate([above, x, below], axis=2)


def on_device(latents, cotangent, valid_frames, spatial_weight, temporal_weight, cond_weight):
    clips, frames, rows, cols, chans = latents.shape
    slab = lax.axis_index("space")
    frame_ids = slab * frames + jnp.arange(frames, dtype=jnp.int32)
    mask = (frame_ids[None, :] < valid_frames[:, None]).astype(jnp.bfloat16)[:, :, None, None, None]
    mask_f = mask.astype(jnp.float32)
    masked = latents * mask
    cot = cotangent * mask
    first = tree_broadcast(masked[:, 0], "space")
    cot_local = jnp.sum(cot, axis=1, dtype=jnp.float32)
    later = shifted(cot, "space", -1)
    if lax.axis_size("space") % 2 == 0:
        cot_pair = cot_local + jnp.sum(later, axis=1, dtype=jnp.float32)
        cot_sum = tree_reduce(cot_pair, "space", 2)
    else:
        cot_sum = tree_reduce(cot_local, "space")
    rows_pad = row_halo(masked)
    padded = jnp.pad(rows_pad, ((0, 0), (0, 0), (0, 0), (1, 1), (0, 0)))
    pre = spatial_sum(padded, spatial_weight, False)
    act = jax.nn.silu(pre).astype(jnp.bfloat16)
    earlier = shifted(act, "space", 1)
    act_pad = jnp.concatenate([earlier, act], axis=1)
    mixed = lag_forward(act_pad, temporal_weight, frames)
    cot_pad = jnp.concatenate([cot, later], axis=1)
    dact = lag_backward(cot_pad, temporal_weight, frames)
    temporal_terms = lag_grads(act, cot_pad, frames)
    cond = jnp.dot(first, cond_weight, preferred_element_type=jnp.float32)
    output = ((masked.astype(jnp.float32) + mixed + cond[:, None]) * mask_f).astype(jnp.bfloat16)
    sig = jax.nn.sigmoid(pre)
    dpre = (dact * sig * (1.0 + pre * (1.0 - sig))).astype(jnp.bfloat16)
    cond_back = jnp.dot(cot_sum, cond_weight.astype(jnp.float32).T, precision=lax.Precision.HIGHEST)
    dpre_rows = row_halo(dpre)
    dpre_pad = jnp.pad(dpre_rows, ((0, 0), (0, 0), (0, 0), (1, 1), (0, 0)))
    dmasked = spatial_sum(dpre_pad, spatial_weight, True)
    is_first = (frame_ids == 0).astype(jnp.float32)[None, :, None, None, None]
    grad_latents = (
        (cot.astype(jnp.float32) + dmasked + is_first * cond_back[:, None]) * mask_f
    ).astype(jnp.bfloat16)
    dims = (((0, 1, 2, 3), (0, 1, 2, 3)), ((), ()))
    spatial_terms = []
    for row_off in range(3):
        for col_off in range(3):
            piece = padded[:, :, row_off : row_off + rows, col_off : col_off + cols]
            spatial_terms.append(
                lax.dot_general(piece, dpre, dims, preferred_element_type=jnp.float32)
            )
    spatial_terms = jnp.stack(spatial_terms)
    cond_terms = lax.dot_general(
        first.astype(jnp.float32),
        cot_local,
        (((0, 1, 2), (0, 1, 2)), ((), ())),
        precision=lax.Precision.HIGHEST,
    )
    taps_s = spatial_terms.shape[0]
    taps_t = temporal_terms.shape[0]
    flat = jnp.concatenate(
        [spatial_terms.reshape(-1, chans), temporal_terms.reshape(-1, chans)], axis=0
    )
    scale = (clips * frames * rows * cols * lax.axis_size("space") * lax.axis_size("tm")) ** (-0.5)
    summed = all_sum_rounded(flat, scale)
    grad_cond = all_sum_rounded(cond_terms, scale)
    n_s = taps_s * chans
    n_t = taps_t * chans
    grad_spatial = summed[:n_s].reshape(taps_s, chans, chans)
    grad_temporal = summed[n_s : n_s + n_t].reshape(taps_t, chans, chans)
    return (output, grad_latents, grad_spatial, grad_temporal, grad_cond)


def solution(mesh):
    return jax.shard_map(
        on_device,
        mesh=mesh,
        in_specs=(
            P("groups", "space", "tm", None, None),
            P("groups", "space", "tm", None, None),
            P("groups"),
            P(),
            P(),
            P(),
        ),
        out_specs=(
            P("groups", "space", "tm", None, None),
            P("groups", "space", "tm", None, None),
            P("groups", None, None),
            P("groups", None, None),
            P("groups", None),
        ),
        check_vma=False,
    )
```

```python
import jax
import jax.numpy as jnp
from jax import lax
from jax.sharding import PartitionSpec as P


def shifted(value, axis, by):
    count = lax.axis_size(axis)
    pairs = [(i, i + by) for i in range(count) if 0 <= i + by < count]
    return lax.ppermute(value, axis, pairs)


def tree_broadcast(value, axis):
    count = lax.axis_size(axis)
    me = lax.axis_index(axis)
    step = 1
    while step * 2 < count:
        step *= 2
    while step >= 1 and count > 1:
        pairs = [(i, i + step) for i in range(0, count, 2 * step) if i + step < count]
        got = lax.ppermute(value, axis, pairs)
        value = jnp.where(me % (2 * step) == step, got, value)
        step //= 2
    return value


def tree_reduce(value, axis, step=1):
    count = lax.axis_size(axis)
    while step < count:
        pairs = [(i + step, i) for i in range(0, count, 2 * step) if i + step < count]
        value = value + lax.ppermute(value, axis, pairs)
        step *= 2
    return value


def xor_halving(flat, axis, steps):
    me = lax.axis_index(axis)
    count = lax.axis_size(axis)
    for step in steps:
        half = flat.shape[0] // 2
        upper = (me // step) % 2
        keep = lax.dynamic_slice_in_dim(flat, upper * half, half, 0)
        send = lax.dynamic_slice_in_dim(flat, (1 - upper) * half, half, 0)
        pairs = [(i, i ^ step) for i in range(count)]
        flat = keep + lax.ppermute(send, axis, pairs)
    return flat


def xor_doubling(piece, axis, steps):
    me = lax.axis_index(axis)
    count = lax.axis_size(axis)
    for step in reversed(steps):
        got = lax.ppermute(piece, axis, [(i, i ^ step) for i in range(count)])
        upper = (me // step) % 2 == 1
        piece = jnp.where(
            upper, jnp.concatenate([got, piece], 0), jnp.concatenate([piece, got], 0)
        )
    return piece


def direct_scatter(flat, axis, low, high):
    me = lax.axis_index(axis)
    j = me // low
    blk = flat.shape[0] // high
    total = lax.dynamic_slice_in_dim(flat, j * blk, blk, 0)
    for d in range(1, high):
        send = lax.dynamic_slice_in_dim(flat, ((j + d) % high) * blk, blk, 0)
        pairs = [
            (a * low + b, ((a + d) % high) * low + b) for a in range(high) for b in range(low)
        ]
        total = total + lax.ppermute(send, axis, pairs)
    return total


def direct_gather(piece, axis, low, high):
    me = lax.axis_index(axis)
    j = me // low
    out = jnp.zeros((high,) + piece.shape, piece.dtype)
    out = lax.dynamic_update_index_in_dim(out, piece, j, 0)
    for d in range(1, high):
        pairs = [
            (a * low + b, ((a + d) % high) * low + b) for a in range(high) for b in range(low)
        ]
        got = lax.ppermute(piece, axis, pairs)
        out = lax.dynamic_update_index_in_dim(out, got, (j - d) % high, 0)
    return out.reshape((-1,) + piece.shape[1:])


def is_pow2(n):
    return n >= 1 and (n & (n - 1)) == 0


def all_sum_rounded(flat, scale):
    n_tm = lax.axis_size("tm")
    n_sp = lax.axis_size("space")
    if not (is_pow2(n_tm) and is_pow2(n_sp)):
        return (lax.psum(flat, ("tm", "space")) * scale).astype(jnp.bfloat16), [], flat.shape[0]
    high = min(4, n_sp)
    low = n_sp // high
    tm_steps = []
    s = 1
    while s < n_tm:
        tm_steps.append(s)
        s *= 2
    sp_steps = []
    s = 1
    while s < low:
        sp_steps.append(s)
        s *= 2
    rows = flat.shape[0]
    unit = n_tm * n_sp * 8
    padded_rows = -(-rows // unit) * unit
    if padded_rows != rows:
        flat = jnp.pad(flat, ((0, padded_rows - rows), (0, 0)))
    flat = xor_halving(flat, "tm", tm_steps)
    flat = direct_scatter(flat, "space", low, high)
    flat = xor_halving(flat, "space", sp_steps)
    piece = (flat * scale).astype(jnp.bfloat16)
    piece = xor_doubling(piece, "space", sp_steps)
    piece = direct_gather(piece, "space", low, high)
    return piece, tm_steps, rows


def split_rows(gathered, cuts):
    piece, tm_steps, rows = gathered
    if len(tm_steps) != 1:
        whole = xor_doubling(piece, "tm", tm_steps)
        return [whole[a:b] for a, b in cuts]
    me = lax.axis_index("tm")
    got = lax.ppermute(piece, "tm", [(0, 1), (1, 0)])
    lower = jnp.where(me == 0, piece, got)
    upper = jnp.where(me == 0, got, piece)
    half = piece.shape[0]
    outs = []
    for a, b in cuts:
        parts = []
        if a < half:
            parts.append(lower[a : min(b, half)])
        if b > half:
            parts.append(upper[max(a, half) - half : b - half])
        outs.append(parts[0] if len(parts) == 1 else jnp.concatenate(parts, 0))
    return outs


def spatial_sum(padded, weights, flip):
    rows = padded.shape[2] - 2
    cols = padded.shape[3] - 2
    total = jnp.zeros(padded.shape[:2] + (rows, cols, weights.shape[2]), jnp.float32)
    for row_off in range(3):
        for col_off in range(3):
            if flip:
                piece = padded[
                    :, :, 2 - row_off : 2 - row_off + rows, 2 - col_off : 2 - col_off + cols
                ]
                kernel = weights[3 * row_off + col_off].T
            else:
                piece = padded[:, :, row_off : row_off + rows, col_off : col_off + cols]
                kernel = weights[3 * row_off + col_off]
            total = total + jnp.dot(piece, kernel, preferred_element_type=jnp.float32)
    return total


def lag_forward(padded_act, weights, count):
    total = 0.0
    for lag in range(3):
        total = total + jnp.dot(
            padded_act[:, 2 - lag : 2 - lag + count],
            weights[lag],
            preferred_element_type=jnp.float32,
        )
    return total


def lag_backward(padded_cot, weights, count):
    total = 0.0
    for lag in range(3):
        total = total + jnp.dot(
            padded_cot[:, lag : lag + count], weights[lag].T, preferred_element_type=jnp.float32
        )
    return total


def lag_grads(act, padded_cot, count):
    dims = (((0, 1, 2, 3), (0, 1, 2, 3)), ((), ()))
    terms = []
    for lag in range(3):
        terms.append(
            lax.dot_general(
                act,
                padded_cot[:, lag : lag + count],
                dims,
                preferred_element_type=jnp.float32,
            )
        )
    return jnp.stack(terms)


def row_halo(x):
    if lax.axis_size("tm") == 2:
        me = lax.axis_index("tm")
        edge = jnp.where(me == 0, x[:, :, -1:], x[:, :, :1])
        got = lax.ppermute(edge, "tm", [(0, 1), (1, 0)])
        zero = jnp.zeros_like(got)
        above = jnp.where(me == 1, got, zero)
        below = jnp.where(me == 0, got, zero)
        return jnp.concatenate([above, x, below], axis=2)
    above = shifted(x[:, :, -1:], "tm", 1)
    below = shifted(x[:, :, :1], "tm", -1)
    return jnp.concatenate([above, x, below], axis=2)


def on_device(latents, cotangent, valid_frames, spatial_weight, temporal_weight, cond_weight):
    clips, frames, rows, cols, chans = latents.shape
    slab = lax.axis_index("space")
    frame_ids = slab * frames + jnp.arange(frames, dtype=jnp.int32)
    mask = (frame_ids[None, :] < valid_frames[:, None]).astype(jnp.bfloat16)[:, :, None, None, None]
    mask_f = mask.astype(jnp.float32)
    masked = latents * mask
    cot = cotangent * mask
    first = tree_broadcast(masked[:, 0], "space")
    cot_local = jnp.sum(cot, axis=1, dtype=jnp.float32)
    later = shifted(cot, "space", -1)
    if lax.axis_size("space") % 2 == 0:
        cot_pair = cot_local + jnp.sum(later, axis=1, dtype=jnp.float32)
        cot_sum = tree_reduce(cot_pair, "space", 2)
    else:
        cot_sum = tree_reduce(cot_local, "space")
    rows_pad = row_halo(masked)
    padded = jnp.pad(rows_pad, ((0, 0), (0, 0), (0, 0), (1, 1), (0, 0)))
    pre = spatial_sum(padded, spatial_weight, False)
    act = jax.nn.silu(pre).astype(jnp.bfloat16)
    earlier = shifted(act, "space", 1)
    act_pad = jnp.concatenate([earlier, act], axis=1)
    mixed = lag_forward(act_pad, temporal_weight, frames)
    cot_pad = jnp.concatenate([cot, later], axis=1)
    dact = lag_backward(cot_pad, temporal_weight, frames)
    temporal_terms = lag_grads(act, cot_pad, frames)
    cond = jnp.dot(first, cond_weight, preferred_element_type=jnp.float32)
    output = ((masked.astype(jnp.float32) + mixed + cond[:, None]) * mask_f).astype(jnp.bfloat16)
    sig = jax.nn.sigmoid(pre)
    dpre = (dact * sig * (1.0 + pre * (1.0 - sig))).astype(jnp.bfloat16)
    cond_back = jnp.dot(cot_sum, cond_weight.astype(jnp.float32).T, precision=lax.Precision.HIGHEST)
    dpre_rows = row_halo(dpre)
    dpre_pad = jnp.pad(dpre_rows, ((0, 0), (0, 0), (0, 0), (1, 1), (0, 0)))
    dmasked = spatial_sum(dpre_pad, spatial_weight, True)
    is_first = (frame_ids == 0).astype(jnp.float32)[None, :, None, None, None]
    grad_latents = (
        (cot.astype(jnp.float32) + dmasked + is_first * cond_back[:, None]) * mask_f
    ).astype(jnp.bfloat16)
    dims = (((0, 1, 2, 3), (0, 1, 2, 3)), ((), ()))
    spatial_terms = []
    for row_off in range(3):
        for col_off in range(3):
            piece = padded[:, :, row_off : row_off + rows, col_off : col_off + cols]
            spatial_terms.append(
                lax.dot_general(piece, dpre, dims, preferred_element_type=jnp.float32)
            )
    spatial_terms = jnp.stack(spatial_terms)
    cond_terms = lax.dot_general(
        first.astype(jnp.float32),
        cot_local,
        (((0, 1, 2), (0, 1, 2)), ((), ())),
        precision=lax.Precision.HIGHEST,
    )
    taps_s = spatial_terms.shape[0]
    taps_t = temporal_terms.shape[0]
    flat = jnp.concatenate(
        [
            spatial_terms.reshape(-1, chans),
            temporal_terms.reshape(-1, chans),
            cond_terms.reshape(-1, chans),
        ],
        axis=0,
    )
    scale = (clips * frames * rows * cols * lax.axis_size("space") * lax.axis_size("tm")) ** (-0.5)
    summed = all_sum_rounded(flat, scale)
    n_s = taps_s * chans
    n_t = taps_t * chans
    grad_spatial, grad_temporal, grad_cond = split_rows(
        summed, [(0, n_s), (n_s, n_s + n_t), (n_s + n_t, n_s + n_t + chans)]
    )
    grad_spatial = grad_spatial.reshape(taps_s, chans, chans)
    grad_temporal = grad_temporal.reshape(taps_t, chans, chans)
    return (output, grad_latents, grad_spatial, grad_temporal, grad_cond)


def solution(mesh):
    return jax.shard_map(
        on_device,
        mesh=mesh,
        in_specs=(
            P("groups", "space", "tm", None, None),
            P("groups", "space", "tm", None, None),
            P("groups"),
            P(),
            P(),
            P(),
        ),
        out_specs=(
            P("groups", "space", "tm", None, None),
            P("groups", "space", "tm", None, None),
            P("groups", None, None),
            P("groups", None, None),
            P("groups", None),
        ),
        check_vma=False,
    )
```

```python
import jax
import jax.numpy as jnp
from jax import lax
from jax.sharding import PartitionSpec as P


def shifted(value, axis, by):
    count = lax.axis_size(axis)
    pairs = [(i, i + by) for i in range(count) if 0 <= i + by < count]
    return lax.ppermute(value, axis, pairs)


def tree_broadcast(value, axis):
    count = lax.axis_size(axis)
    me = lax.axis_index(axis)
    step = 1
    while step * 2 < count:
        step *= 2
    while step >= 1 and count > 1:
        pairs = [(i, i + step) for i in range(0, count, 2 * step) if i + step < count]
        got = lax.ppermute(value, axis, pairs)
        value = jnp.where(me % (2 * step) == step, got, value)
        step //= 2
    return value


def tree_reduce(value, axis, step=1):
    count = lax.axis_size(axis)
    while step < count:
        pairs = [(i + step, i) for i in range(0, count, 2 * step) if i + step < count]
        value = value + lax.ppermute(value, axis, pairs)
        step *= 2
    return value


def chain_reduce(value, axis, step):
    count = lax.axis_size(axis)
    holders = list(range(0, count, step))
    if len(holders) > 4:
        return tree_reduce(value, axis, step)
    for k in range(len(holders) - 1, 0, -1):
        value = value + lax.ppermute(value, axis, [(holders[k], holders[k - 1])])
    return value


def xor_halving(flat, axis, steps):
    me = lax.axis_index(axis)
    count = lax.axis_size(axis)
    for step in steps:
        half = flat.shape[0] // 2
        upper = (me // step) % 2
        keep = lax.dynamic_slice_in_dim(flat, upper * half, half, 0)
        send = lax.dynamic_slice_in_dim(flat, (1 - upper) * half, half, 0)
        pairs = [(i, i ^ step) for i in range(count)]
        flat = keep + lax.ppermute(send, axis, pairs)
    return flat


def xor_doubling(piece, axis, steps):
    me = lax.axis_index(axis)
    count = lax.axis_size(axis)
    for step in reversed(steps):
        got = lax.ppermute(piece, axis, [(i, i ^ step) for i in range(count)])
        upper = (me // step) % 2 == 1
        piece = jnp.where(
            upper, jnp.concatenate([got, piece], 0), jnp.concatenate([piece, got], 0)
        )
    return piece


def direct_scatter(flat, axis, low, high):
    me = lax.axis_index(axis)
    j = me // low
    blk = flat.shape[0] // high
    total = lax.dynamic_slice_in_dim(flat, j * blk, blk, 0)
    for d in range(1, high):
        send = lax.dynamic_slice_in_dim(flat, ((j + d) % high) * blk, blk, 0)
        pairs = [
            (a * low + b, ((a + d) % high) * low + b) for a in range(high) for b in range(low)
        ]
        total = total + lax.ppermute(send, axis, pairs)
    return total


def direct_gather(piece, axis, low, high):
    me = lax.axis_index(axis)
    j = me // low
    out = jnp.zeros((high,) + piece.shape, piece.dtype)
    out = lax.dynamic_update_index_in_dim(out, piece, j, 0)
    for d in range(1, high):
        pairs = [
            (a * low + b, ((a + d) % high) * low + b) for a in range(high) for b in range(low)
        ]
        got = lax.ppermute(piece, axis, pairs)
        out = lax.dynamic_update_index_in_dim(out, got, (j - d) % high, 0)
    return out.reshape((-1,) + piece.shape[1:])


def is_pow2(n):
    return n >= 1 and (n & (n - 1)) == 0


def all_sum_rounded(flat, scale):
    n_tm = lax.axis_size("tm")
    n_sp = lax.axis_size("space")
    if not (is_pow2(n_tm) and is_pow2(n_sp)):
        return (lax.psum(flat, ("tm", "space")) * scale).astype(jnp.bfloat16), [], flat.shape[0]
    high = min(4, n_sp)
    low = n_sp // high
    tm_steps = []
    s = 1
    while s < n_tm:
        tm_steps.append(s)
        s *= 2
    sp_steps = []
    s = 1
    while s < low:
        sp_steps.append(s)
        s *= 2
    rows = flat.shape[0]
    unit = n_tm * n_sp * 8
    padded_rows = -(-rows // unit) * unit
    if padded_rows != rows:
        flat = jnp.pad(flat, ((0, padded_rows - rows), (0, 0)))
    flat = xor_halving(flat, "tm", tm_steps)
    flat = direct_scatter(flat, "space", low, high)
    flat = xor_halving(flat, "space", sp_steps)
    piece = (flat * scale).astype(jnp.bfloat16)
    piece = xor_doubling(piece, "space", sp_steps)
    piece = direct_gather(piece, "space", low, high)
    return piece, tm_steps, rows


def split_rows(gathered, cuts):
    piece, tm_steps, rows = gathered
    if len(tm_steps) != 1:
        whole = xor_doubling(piece, "tm", tm_steps)
        return [whole[a:b] for a, b in cuts]
    me = lax.axis_index("tm")
    got = lax.ppermute(piece, "tm", [(0, 1), (1, 0)])
    lower = jnp.where(me == 0, piece, got)
    upper = jnp.where(me == 0, got, piece)
    half = piece.shape[0]
    outs = []
    for a, b in cuts:
        parts = []
        if a < half:
            parts.append(lower[a : min(b, half)])
        if b > half:
            parts.append(upper[max(a, half) - half : b - half])
        outs.append(parts[0] if len(parts) == 1 else jnp.concatenate(parts, 0))
    return outs


def spatial_sum(padded, weights, flip):
    rows = padded.shape[2] - 2
    cols = padded.shape[3] - 2
    total = jnp.zeros(padded.shape[:2] + (rows, cols, weights.shape[2]), jnp.float32)
    for row_off in range(3):
        for col_off in range(3):
            if flip:
                piece = padded[
                    :, :, 2 - row_off : 2 - row_off + rows, 2 - col_off : 2 - col_off + cols
                ]
                kernel = weights[3 * row_off + col_off].T
            else:
                piece = padded[:, :, row_off : row_off + rows, col_off : col_off + cols]
                kernel = weights[3 * row_off + col_off]
            total = total + jnp.dot(piece, kernel, preferred_element_type=jnp.float32)
    return total


def lag_forward(padded_act, weights, count):
    total = 0.0
    for lag in range(3):
        total = total + jnp.dot(
            padded_act[:, 2 - lag : 2 - lag + count],
            weights[lag],
            preferred_element_type=jnp.float32,
        )
    return total


def lag_backward(padded_cot, weights, count):
    total = 0.0
    for lag in range(3):
        total = total + jnp.dot(
            padded_cot[:, lag : lag + count], weights[lag].T, preferred_element_type=jnp.float32
        )
    return total


def lag_grads(act, padded_cot, count):
    dims = (((0, 1, 2, 3), (0, 1, 2, 3)), ((), ()))
    terms = []
    for lag in range(3):
        terms.append(
            lax.dot_general(
                act,
                padded_cot[:, lag : lag + count],
                dims,
                preferred_element_type=jnp.float32,
            )
        )
    return jnp.stack(terms)


def row_halo(x):
    if lax.axis_size("tm") == 2:
        me = lax.axis_index("tm")
        edge = jnp.where(me == 0, x[:, :, -1:], x[:, :, :1])
        got = lax.ppermute(edge, "tm", [(0, 1), (1, 0)])
        zero = jnp.zeros_like(got)
        above = jnp.where(me == 1, got, zero)
        below = jnp.where(me == 0, got, zero)
        return jnp.concatenate([above, x, below], axis=2)
    above = shifted(x[:, :, -1:], "tm", 1)
    below = shifted(x[:, :, :1], "tm", -1)
    return jnp.concatenate([above, x, below], axis=2)


def on_device(latents, cotangent, valid_frames, spatial_weight, temporal_weight, cond_weight):
    clips, frames, rows, cols, chans = latents.shape
    slab = lax.axis_index("space")
    frame_ids = slab * frames + jnp.arange(frames, dtype=jnp.int32)
    mask = (frame_ids[None, :] < valid_frames[:, None]).astype(jnp.bfloat16)[:, :, None, None, None]
    mask_f = mask.astype(jnp.float32)
    masked = latents * mask
    cot = cotangent * mask
    first = tree_broadcast(masked[:, 0], "space")
    cot_local = jnp.sum(cot, axis=1, dtype=jnp.float32)
    later = shifted(cot, "space", -1)
    if lax.axis_size("space") % 2 == 0:
        cot_pair = cot_local + jnp.sum(later, axis=1, dtype=jnp.float32)
        cot_sum = chain_reduce(cot_pair, "space", 2)
    else:
        cot_sum = tree_reduce(cot_local, "space")
    rows_pad = row_halo(masked)
    padded = jnp.pad(rows_pad, ((0, 0), (0, 0), (0, 0), (1, 1), (0, 0)))
    pre = spatial_sum(padded, spatial_weight, False)
    act = jax.nn.silu(pre).astype(jnp.bfloat16)
    earlier = shifted(act, "space", 1)
    act_pad = jnp.concatenate([earlier, act], axis=1)
    mixed = lag_forward(act_pad, temporal_weight, frames)
    cot_pad = jnp.concatenate([cot, later], axis=1)
    dact = lag_backward(cot_pad, temporal_weight, frames)
    temporal_terms = lag_grads(act, cot_pad, frames)
    cond = jnp.dot(first, cond_weight, preferred_element_type=jnp.float32)
    output = ((masked.astype(jnp.float32) + mixed + cond[:, None]) * mask_f).astype(jnp.bfloat16)
    sig = jax.nn.sigmoid(pre)
    dpre = (dact * sig * (1.0 + pre * (1.0 - sig))).astype(jnp.bfloat16)
    cond_back = jnp.dot(cot_sum, cond_weight.astype(jnp.float32).T, precision=lax.Precision.HIGHEST)
    dpre_rows = row_halo(dpre)
    dpre_pad = jnp.pad(dpre_rows, ((0, 0), (0, 0), (0, 0), (1, 1), (0, 0)))
    dmasked = spatial_sum(dpre_pad, spatial_weight, True)
    is_first = (frame_ids == 0).astype(jnp.float32)[None, :, None, None, None]
    grad_latents = (
        (cot.astype(jnp.float32) + dmasked + is_first * cond_back[:, None]) * mask_f
    ).astype(jnp.bfloat16)
    dims = (((0, 1, 2, 3), (0, 1, 2, 3)), ((), ()))
    spatial_terms = []
    for row_off in range(3):
        for col_off in range(3):
            piece = padded[:, :, row_off : row_off + rows, col_off : col_off + cols]
            spatial_terms.append(
                lax.dot_general(piece, dpre, dims, preferred_element_type=jnp.float32)
            )
    spatial_terms = jnp.stack(spatial_terms)
    cond_terms = lax.dot_general(
        first.astype(jnp.float32),
        cot_local,
        (((0, 1, 2), (0, 1, 2)), ((), ())),
        precision=lax.Precision.HIGHEST,
    )
    taps_s = spatial_terms.shape[0]
    taps_t = temporal_terms.shape[0]
    flat = jnp.concatenate(
        [
            spatial_terms.reshape(-1, chans),
            temporal_terms.reshape(-1, chans),
            cond_terms.reshape(-1, chans),
        ],
        axis=0,
    )
    scale = (clips * frames * rows * cols * lax.axis_size("space") * lax.axis_size("tm")) ** (-0.5)
    summed = all_sum_rounded(flat, scale)
    n_s = taps_s * chans
    n_t = taps_t * chans
    grad_spatial, grad_temporal, grad_cond = split_rows(
        summed, [(0, n_s), (n_s, n_s + n_t), (n_s + n_t, n_s + n_t + chans)]
    )
    grad_spatial = grad_spatial.reshape(taps_s, chans, chans)
    grad_temporal = grad_temporal.reshape(taps_t, chans, chans)
    return (output, grad_latents, grad_spatial, grad_temporal, grad_cond)


def solution(mesh):
    return jax.shard_map(
        on_device,
        mesh=mesh,
        in_specs=(
            P("groups", "space", "tm", None, None),
            P("groups", "space", "tm", None, None),
            P("groups"),
            P(),
            P(),
            P(),
        ),
        out_specs=(
            P("groups", "space", "tm", None, None),
            P("groups", "space", "tm", None, None),
            P("groups", None, None),
            P("groups", None, None),
            P("groups", None),
        ),
        check_vma=False,
    )
```

```python
import jax
import jax.numpy as jnp
from jax import lax
from jax.sharding import PartitionSpec as P


def shifted(value, axis, by):
    count = lax.axis_size(axis)
    pairs = [(i, i + by) for i in range(count) if 0 <= i + by < count]
    return lax.ppermute(value, axis, pairs)


def rounds_broadcast(value, axis, rounds):
    me = lax.axis_index(axis)
    for permutes in rounds:
        for pairs in permutes:
            got = lax.ppermute(value, axis, pairs)
            takes = me == pairs[0][1]
            for _, dst in pairs[1:]:
                takes = takes | (me == dst)
            value = jnp.where(takes, got, value)
    return value


def tree_broadcast(value, axis):
    count = lax.axis_size(axis)
    me = lax.axis_index(axis)
    if count == 8:
        rounds = [
            [[(0, 1)], [(0, 4)]],
            [[(0, 2), (4, 6), (1, 5)]],
            [[(1, 3), (5, 7)]],
        ]
        return rounds_broadcast(value, axis, rounds)
    step = 1
    while step * 2 < count:
        step *= 2
    while step >= 1 and count > 1:
        pairs = [(i, i + step) for i in range(0, count, 2 * step) if i + step < count]
        got = lax.ppermute(value, axis, pairs)
        value = jnp.where(me % (2 * step) == step, got, value)
        step //= 2
    return value


def tree_reduce(value, axis, step=1):
    count = lax.axis_size(axis)
    while step < count:
        pairs = [(i + step, i) for i in range(0, count, 2 * step) if i + step < count]
        value = value + lax.ppermute(value, axis, pairs)
        step *= 2
    return value


def xor_halving(flat, axis, steps):
    me = lax.axis_index(axis)
    count = lax.axis_size(axis)
    for step in steps:
        half = flat.shape[0] // 2
        upper = (me // step) % 2
        keep = lax.dynamic_slice_in_dim(flat, upper * half, half, 0)
        send = lax.dynamic_slice_in_dim(flat, (1 - upper) * half, half, 0)
        pairs = [(i, i ^ step) for i in range(count)]
        flat = keep + lax.ppermute(send, axis, pairs)
    return flat


def xor_doubling(piece, axis, steps):
    me = lax.axis_index(axis)
    count = lax.axis_size(axis)
    for step in reversed(steps):
        got = lax.ppermute(piece, axis, [(i, i ^ step) for i in range(count)])
        upper = (me // step) % 2 == 1
        piece = jnp.where(
            upper, jnp.concatenate([got, piece], 0), jnp.concatenate([piece, got], 0)
        )
    return piece


def direct_scatter(flat, axis, low, high):
    me = lax.axis_index(axis)
    j = me // low
    blk = flat.shape[0] // high
    total = lax.dynamic_slice_in_dim(flat, j * blk, blk, 0)
    for d in range(1, high):
        send = lax.dynamic_slice_in_dim(flat, ((j + d) % high) * blk, blk, 0)
        pairs = [
            (a * low + b, ((a + d) % high) * low + b) for a in range(high) for b in range(low)
        ]
        total = total + lax.ppermute(send, axis, pairs)
    return total


def direct_gather(piece, axis, low, high):
    me = lax.axis_index(axis)
    j = me // low
    out = jnp.zeros((high,) + piece.shape, piece.dtype)
    out = lax.dynamic_update_index_in_dim(out, piece, j, 0)
    for d in range(1, high):
        pairs = [
            (a * low + b, ((a + d) % high) * low + b) for a in range(high) for b in range(low)
        ]
        got = lax.ppermute(piece, axis, pairs)
        out = lax.dynamic_update_index_in_dim(out, got, (j - d) % high, 0)
    return out.reshape((-1,) + piece.shape[1:])


def is_pow2(n):
    return n >= 1 and (n & (n - 1)) == 0


def all_sum_rounded(flat, scale):
    n_tm = lax.axis_size("tm")
    n_sp = lax.axis_size("space")
    if not (is_pow2(n_tm) and is_pow2(n_sp)):
        return (lax.psum(flat, ("tm", "space")) * scale).astype(jnp.bfloat16), [], flat.shape[0]
    high = min(4, n_sp)
    low = n_sp // high
    tm_steps = []
    s = 1
    while s < n_tm:
        tm_steps.append(s)
        s *= 2
    sp_steps = []
    s = 1
    while s < low:
        sp_steps.append(s)
        s *= 2
    rows = flat.shape[0]
    unit = n_tm * n_sp * 8
    padded_rows = -(-rows // unit) * unit
    if padded_rows != rows:
        flat = jnp.pad(flat, ((0, padded_rows - rows), (0, 0)))
    flat = xor_halving(flat, "tm", tm_steps)
    flat = direct_scatter(flat, "space", low, high)
    flat = xor_halving(flat, "space", sp_steps)
    piece = (flat * scale).astype(jnp.bfloat16)
    piece = xor_doubling(piece, "space", sp_steps)
    piece = direct_gather(piece, "space", low, high)
    return piece, tm_steps, rows


def split_rows(gathered, cuts):
    piece, tm_steps, rows = gathered
    if len(tm_steps) != 1:
        whole = xor_doubling(piece, "tm", tm_steps)
        return [whole[a:b] for a, b in cuts]
    me = lax.axis_index("tm")
    got = lax.ppermute(piece, "tm", [(0, 1), (1, 0)])
    lower = jnp.where(me == 0, piece, got)
    upper = jnp.where(me == 0, got, piece)
    half = piece.shape[0]
    outs = []
    for a, b in cuts:
        parts = []
        if a < half:
            parts.append(lower[a : min(b, half)])
        if b > half:
            parts.append(upper[max(a, half) - half : b - half])
        outs.append(parts[0] if len(parts) == 1 else jnp.concatenate(parts, 0))
    return outs


def spatial_sum(padded, weights, flip):
    rows = padded.shape[2] - 2
    cols = padded.shape[3] - 2
    total = jnp.zeros(padded.shape[:2] + (rows, cols, weights.shape[2]), jnp.float32)
    for row_off in range(3):
        for col_off in range(3):
            if flip:
                piece = padded[
                    :, :, 2 - row_off : 2 - row_off + rows, 2 - col_off : 2 - col_off + cols
                ]
                kernel = weights[3 * row_off + col_off].T
            else:
                piece = padded[:, :, row_off : row_off + rows, col_off : col_off + cols]
                kernel = weights[3 * row_off + col_off]
            total = total + jnp.dot(piece, kernel, preferred_element_type=jnp.float32)
    return total


def lag_forward(padded_act, weights, count):
    total = 0.0
    for lag in range(3):
        total = total + jnp.dot(
            padded_act[:, 2 - lag : 2 - lag + count],
            weights[lag],
            preferred_element_type=jnp.float32,
        )
    return total


def lag_backward(padded_cot, weights, count):
    total = 0.0
    for lag in range(3):
        total = total + jnp.dot(
            padded_cot[:, lag : lag + count], weights[lag].T, preferred_element_type=jnp.float32
        )
    return total


def lag_grads(act, padded_cot, count):
    dims = (((0, 1, 2, 3), (0, 1, 2, 3)), ((), ()))
    terms = []
    for lag in range(3):
        terms.append(
            lax.dot_general(
                act,
                padded_cot[:, lag : lag + count],
                dims,
                preferred_element_type=jnp.float32,
            )
        )
    return jnp.stack(terms)


def row_halo(x):
    if lax.axis_size("tm") == 2:
        me = lax.axis_index("tm")
        edge = jnp.where(me == 0, x[:, :, -1:], x[:, :, :1])
        got = lax.ppermute(edge, "tm", [(0, 1), (1, 0)])
        zero = jnp.zeros_like(got)
        above = jnp.where(me == 1, got, zero)
        below = jnp.where(me == 0, got, zero)
        return jnp.concatenate([above, x, below], axis=2)
    above = shifted(x[:, :, -1:], "tm", 1)
    below = shifted(x[:, :, :1], "tm", -1)
    return jnp.concatenate([above, x, below], axis=2)


def on_device(latents, cotangent, valid_frames, spatial_weight, temporal_weight, cond_weight):
    clips, frames, rows, cols, chans = latents.shape
    slab = lax.axis_index("space")
    frame_ids = slab * frames + jnp.arange(frames, dtype=jnp.int32)
    mask = (frame_ids[None, :] < valid_frames[:, None]).astype(jnp.bfloat16)[:, :, None, None, None]
    mask_f = mask.astype(jnp.float32)
    masked = latents * mask
    cot = cotangent * mask
    first = tree_broadcast(masked[:, 0], "space")
    cot_local = jnp.sum(cot, axis=1, dtype=jnp.float32)
    later = shifted(cot, "space", -1)
    if lax.axis_size("space") % 2 == 0:
        cot_pair = cot_local + jnp.sum(later, axis=1, dtype=jnp.float32)
        cot_sum = tree_reduce(cot_pair, "space", 2)
    else:
        cot_sum = tree_reduce(cot_local, "space")
    rows_pad = row_halo(masked)
    padded = jnp.pad(rows_pad, ((0, 0), (0, 0), (0, 0), (1, 1), (0, 0)))
    pre = spatial_sum(padded, spatial_weight, False)
    act = jax.nn.silu(pre).astype(jnp.bfloat16)
    earlier = shifted(act, "space", 1)
    act_pad = jnp.concatenate([earlier, act], axis=1)
    mixed = lag_forward(act_pad, temporal_weight, frames)
    cot_pad = jnp.concatenate([cot, later], axis=1)
    dact = lag_backward(cot_pad, temporal_weight, frames)
    temporal_terms = lag_grads(act, cot_pad, frames)
    cond = jnp.dot(first, cond_weight, preferred_element_type=jnp.float32)
    output = ((masked.astype(jnp.float32) + mixed + cond[:, None]) * mask_f).astype(jnp.bfloat16)
    sig = jax.nn.sigmoid(pre)
    dpre = (dact * sig * (1.0 + pre * (1.0 - sig))).astype(jnp.bfloat16)
    cond_back = jnp.dot(cot_sum, cond_weight.astype(jnp.float32).T, precision=lax.Precision.HIGHEST)
    dpre_rows = row_halo(dpre)
    dpre_pad = jnp.pad(dpre_rows, ((0, 0), (0, 0), (0, 0), (1, 1), (0, 0)))
    dmasked = spatial_sum(dpre_pad, spatial_weight, True)
    is_first = (frame_ids == 0).astype(jnp.float32)[None, :, None, None, None]
    grad_latents = (
        (cot.astype(jnp.float32) + dmasked + is_first * cond_back[:, None]) * mask_f
    ).astype(jnp.bfloat16)
    dims = (((0, 1, 2, 3), (0, 1, 2, 3)), ((), ()))
    spatial_terms = []
    for row_off in range(3):
        for col_off in range(3):
            piece = padded[:, :, row_off : row_off + rows, col_off : col_off + cols]
            spatial_terms.append(
                lax.dot_general(piece, dpre, dims, preferred_element_type=jnp.float32)
            )
    spatial_terms = jnp.stack(spatial_terms)
    cond_terms = lax.dot_general(
        first.astype(jnp.float32),
        cot_local,
        (((0, 1, 2), (0, 1, 2)), ((), ())),
        precision=lax.Precision.HIGHEST,
    )
    taps_s = spatial_terms.shape[0]
    taps_t = temporal_terms.shape[0]
    flat = jnp.concatenate(
        [
            spatial_terms.reshape(-1, chans),
            temporal_terms.reshape(-1, chans),
            cond_terms.reshape(-1, chans),
        ],
        axis=0,
    )
    scale = (clips * frames * rows * cols * lax.axis_size("space") * lax.axis_size("tm")) ** (-0.5)
    summed = all_sum_rounded(flat, scale)
    n_s = taps_s * chans
    n_t = taps_t * chans
    grad_spatial, grad_temporal, grad_cond = split_rows(
        summed, [(0, n_s), (n_s, n_s + n_t), (n_s + n_t, n_s + n_t + chans)]
    )
    grad_spatial = grad_spatial.reshape(taps_s, chans, chans)
    grad_temporal = grad_temporal.reshape(taps_t, chans, chans)
    return (output, grad_latents, grad_spatial, grad_temporal, grad_cond)


def solution(mesh):
    return jax.shard_map(
        on_device,
        mesh=mesh,
        in_specs=(
            P("groups", "space", "tm", None, None),
            P("groups", "space", "tm", None, None),
            P("groups"),
            P(),
            P(),
            P(),
        ),
        out_specs=(
            P("groups", "space", "tm", None, None),
            P("groups", "space", "tm", None, None),
            P("groups", None, None),
            P("groups", None, None),
            P("groups", None),
        ),
        check_vma=False,
    )
```

```python
import jax
import jax.numpy as jnp
from jax import lax
from jax.sharding import PartitionSpec as P


def shifted(value, axis, by):
    count = lax.axis_size(axis)
    pairs = [(i, i + by) for i in range(count) if 0 <= i + by < count]
    return lax.ppermute(value, axis, pairs)


def tree_broadcast(value, axis):
    count = lax.axis_size(axis)
    me = lax.axis_index(axis)
    step = 1
    while step * 2 < count:
        step *= 2
    while step >= 1 and count > 1:
        pairs = [(i, i + step) for i in range(0, count, 2 * step) if i + step < count]
        got = lax.ppermute(value, axis, pairs)
        value = jnp.where(me % (2 * step) == step, got, value)
        step //= 2
    return value


def tree_reduce(value, axis, step=1):
    count = lax.axis_size(axis)
    while step < count:
        pairs = [(i + step, i) for i in range(0, count, 2 * step) if i + step < count]
        value = value + lax.ppermute(value, axis, pairs)
        step *= 2
    return value


def xor_halving(flat, axis, steps):
    me = lax.axis_index(axis)
    count = lax.axis_size(axis)
    for step in steps:
        half = flat.shape[0] // 2
        upper = (me // step) % 2
        keep = lax.dynamic_slice_in_dim(flat, upper * half, half, 0)
        send = lax.dynamic_slice_in_dim(flat, (1 - upper) * half, half, 0)
        pairs = [(i, i ^ step) for i in range(count)]
        flat = keep + lax.ppermute(send, axis, pairs)
    return flat


def xor_doubling(piece, axis, steps):
    me = lax.axis_index(axis)
    count = lax.axis_size(axis)
    for step in reversed(steps):
        got = lax.ppermute(piece, axis, [(i, i ^ step) for i in range(count)])
        upper = (me // step) % 2 == 1
        piece = jnp.where(
            upper, jnp.concatenate([got, piece], 0), jnp.concatenate([piece, got], 0)
        )
    return piece


def direct_scatter(flat, axis, low, high):
    me = lax.axis_index(axis)
    j = me // low
    blk = flat.shape[0] // high
    total = lax.dynamic_slice_in_dim(flat, j * blk, blk, 0)
    for d in range(1, high):
        send = lax.dynamic_slice_in_dim(flat, ((j + d) % high) * blk, blk, 0)
        pairs = [
            (a * low + b, ((a + d) % high) * low + b) for a in range(high) for b in range(low)
        ]
        total = total + lax.ppermute(send, axis, pairs)
    return total


def direct_gather(piece, axis, low, high):
    me = lax.axis_index(axis)
    j = me // low
    out = jnp.zeros((high,) + piece.shape, piece.dtype)
    out = lax.dynamic_update_index_in_dim(out, piece, j, 0)
    for d in range(1, high):
        pairs = [
            (a * low + b, ((a + d) % high) * low + b) for a in range(high) for b in range(low)
        ]
        got = lax.ppermute(piece, axis, pairs)
        out = lax.dynamic_update_index_in_dim(out, got, (j - d) % high, 0)
    return out.reshape((-1,) + piece.shape[1:])


def is_pow2(n):
    return n >= 1 and (n & (n - 1)) == 0


def all_sum_rounded(flat, scale, held=None):
    n_tm = lax.axis_size("tm")
    n_sp = lax.axis_size("space")
    if not (is_pow2(n_tm) and is_pow2(n_sp)):
        return (lax.psum(flat, ("tm", "space")) * scale).astype(jnp.bfloat16), [], flat.shape[0], held
    high = min(4, n_sp)
    low = n_sp // high
    tm_steps = []
    s = 1
    while s < n_tm:
        tm_steps.append(s)
        s *= 2
    sp_steps = []
    s = 1
    while s < low:
        sp_steps.append(s)
        s *= 2
    rows = flat.shape[0]
    unit = n_tm * n_sp * 8
    padded_rows = -(-rows // unit) * unit
    if padded_rows != rows:
        flat = jnp.pad(flat, ((0, padded_rows - rows), (0, 0)))
    flat = xor_halving(flat, "tm", tm_steps)
    flat = direct_scatter(flat, "space", low, high)
    flat, held = lax.optimization_barrier((flat, held))
    flat = xor_halving(flat, "space", sp_steps)
    piece = (flat * scale).astype(jnp.bfloat16)
    piece = xor_doubling(piece, "space", sp_steps)
    piece = direct_gather(piece, "space", low, high)
    return piece, tm_steps, rows, held


def split_rows(gathered, cuts):
    piece, tm_steps, rows, _ = gathered
    if len(tm_steps) != 1:
        whole = xor_doubling(piece, "tm", tm_steps)
        return [whole[a:b] for a, b in cuts]
    me = lax.axis_index("tm")
    got = lax.ppermute(piece, "tm", [(0, 1), (1, 0)])
    lower = jnp.where(me == 0, piece, got)
    upper = jnp.where(me == 0, got, piece)
    half = piece.shape[0]
    outs = []
    for a, b in cuts:
        parts = []
        if a < half:
            parts.append(lower[a : min(b, half)])
        if b > half:
            parts.append(upper[max(a, half) - half : b - half])
        outs.append(parts[0] if len(parts) == 1 else jnp.concatenate(parts, 0))
    return outs


def spatial_sum(padded, weights, flip):
    rows = padded.shape[2] - 2
    cols = padded.shape[3] - 2
    total = jnp.zeros(padded.shape[:2] + (rows, cols, weights.shape[2]), jnp.float32)
    for row_off in range(3):
        for col_off in range(3):
            if flip:
                piece = padded[
                    :, :, 2 - row_off : 2 - row_off + rows, 2 - col_off : 2 - col_off + cols
                ]
                kernel = weights[3 * row_off + col_off].T
            else:
                piece = padded[:, :, row_off : row_off + rows, col_off : col_off + cols]
                kernel = weights[3 * row_off + col_off]
            total = total + jnp.dot(piece, kernel, preferred_element_type=jnp.float32)
    return total


def lag_forward(padded_act, weights, count):
    total = 0.0
    for lag in range(3):
        total = total + jnp.dot(
            padded_act[:, 2 - lag : 2 - lag + count],
            weights[lag],
            preferred_element_type=jnp.float32,
        )
    return total


def lag_backward(padded_cot, weights, count):
    total = 0.0
    for lag in range(3):
        total = total + jnp.dot(
            padded_cot[:, lag : lag + count], weights[lag].T, preferred_element_type=jnp.float32
        )
    return total


def lag_grads(act, padded_cot, count):
    dims = (((0, 1, 2, 3), (0, 1, 2, 3)), ((), ()))
    terms = []
    for lag in range(3):
        terms.append(
            lax.dot_general(
                act,
                padded_cot[:, lag : lag + count],
                dims,
                preferred_element_type=jnp.float32,
            )
        )
    return jnp.stack(terms)


def row_halo(x):
    if lax.axis_size("tm") == 2:
        me = lax.axis_index("tm")
        edge = jnp.where(me == 0, x[:, :, -1:], x[:, :, :1])
        got = lax.ppermute(edge, "tm", [(0, 1), (1, 0)])
        zero = jnp.zeros_like(got)
        above = jnp.where(me == 1, got, zero)
        below = jnp.where(me == 0, got, zero)
        return jnp.concatenate([above, x, below], axis=2)
    above = shifted(x[:, :, -1:], "tm", 1)
    below = shifted(x[:, :, :1], "tm", -1)
    return jnp.concatenate([above, x, below], axis=2)


def on_device(latents, cotangent, valid_frames, spatial_weight, temporal_weight, cond_weight):
    clips, frames, rows, cols, chans = latents.shape
    slab = lax.axis_index("space")
    frame_ids = slab * frames + jnp.arange(frames, dtype=jnp.int32)
    mask = (frame_ids[None, :] < valid_frames[:, None]).astype(jnp.bfloat16)[:, :, None, None, None]
    mask_f = mask.astype(jnp.float32)
    masked = latents * mask
    cot = cotangent * mask
    first = tree_broadcast(masked[:, 0], "space")
    cot_local = jnp.sum(cot, axis=1, dtype=jnp.float32)
    later = shifted(cot, "space", -1)
    if lax.axis_size("space") % 2 == 0:
        cot_pair = cot_local + jnp.sum(later, axis=1, dtype=jnp.float32)
        cot_step = 2
    else:
        cot_pair = cot_local
        cot_step = 1
    rows_pad = row_halo(masked)
    padded = jnp.pad(rows_pad, ((0, 0), (0, 0), (0, 0), (1, 1), (0, 0)))
    pre = spatial_sum(padded, spatial_weight, False)
    act = jax.nn.silu(pre).astype(jnp.bfloat16)
    earlier = shifted(act, "space", 1)
    act_pad = jnp.concatenate([earlier, act], axis=1)
    mixed = lag_forward(act_pad, temporal_weight, frames)
    cot_pad = jnp.concatenate([cot, later], axis=1)
    dact = lag_backward(cot_pad, temporal_weight, frames)
    temporal_terms = lag_grads(act, cot_pad, frames)
    cond = jnp.dot(first, cond_weight, preferred_element_type=jnp.float32)
    output = ((masked.astype(jnp.float32) + mixed + cond[:, None]) * mask_f).astype(jnp.bfloat16)
    sig = jax.nn.sigmoid(pre)
    dpre = (dact * sig * (1.0 + pre * (1.0 - sig))).astype(jnp.bfloat16)
    dpre_rows = row_halo(dpre)
    dpre_pad = jnp.pad(dpre_rows, ((0, 0), (0, 0), (0, 0), (1, 1), (0, 0)))
    dmasked = spatial_sum(dpre_pad, spatial_weight, True)
    dims = (((0, 1, 2, 3), (0, 1, 2, 3)), ((), ()))
    spatial_terms = []
    for row_off in range(3):
        for col_off in range(3):
            piece = padded[:, :, row_off : row_off + rows, col_off : col_off + cols]
            spatial_terms.append(
                lax.dot_general(piece, dpre, dims, preferred_element_type=jnp.float32)
            )
    spatial_terms = jnp.stack(spatial_terms)
    cond_terms = lax.dot_general(
        first.astype(jnp.float32),
        cot_local,
        (((0, 1, 2), (0, 1, 2)), ((), ())),
        precision=lax.Precision.HIGHEST,
    )
    taps_s = spatial_terms.shape[0]
    taps_t = temporal_terms.shape[0]
    flat = jnp.concatenate(
        [
            spatial_terms.reshape(-1, chans),
            temporal_terms.reshape(-1, chans),
            cond_terms.reshape(-1, chans),
        ],
        axis=0,
    )
    scale = (clips * frames * rows * cols * lax.axis_size("space") * lax.axis_size("tm")) ** (-0.5)
    summed = all_sum_rounded(flat, scale, cot_pair)
    cot_sum = tree_reduce(summed[3], "space", cot_step)
    cond_back = jnp.dot(cot_sum, cond_weight.astype(jnp.float32).T, precision=lax.Precision.HIGHEST)
    is_first = (frame_ids == 0).astype(jnp.float32)[None, :, None, None, None]
    grad_latents = (
        (cot.astype(jnp.float32) + dmasked + is_first * cond_back[:, None]) * mask_f
    ).astype(jnp.bfloat16)
    n_s = taps_s * chans
    n_t = taps_t * chans
    grad_spatial, grad_temporal, grad_cond = split_rows(
        summed, [(0, n_s), (n_s, n_s + n_t), (n_s + n_t, n_s + n_t + chans)]
    )
    grad_spatial = grad_spatial.reshape(taps_s, chans, chans)
    grad_temporal = grad_temporal.reshape(taps_t, chans, chans)
    return (output, grad_latents, grad_spatial, grad_temporal, grad_cond)


def solution(mesh):
    return jax.shard_map(
        on_device,
        mesh=mesh,
        in_specs=(
            P("groups", "space", "tm", None, None),
            P("groups", "space", "tm", None, None),
            P("groups"),
            P(),
            P(),
            P(),
        ),
        out_specs=(
            P("groups", "space", "tm", None, None),
            P("groups", "space", "tm", None, None),
            P("groups", None, None),
            P("groups", None, None),
            P("groups", None),
        ),
        check_vma=False,
    )
```

```python
import jax
import jax.numpy as jnp
from jax import lax
from jax.sharding import PartitionSpec as P


def shifted(value, axis, by):
    count = lax.axis_size(axis)
    pairs = [(i, i + by) for i in range(count) if 0 <= i + by < count]
    return lax.ppermute(value, axis, pairs)


def tree_broadcast(value, axis):
    count = lax.axis_size(axis)
    me = lax.axis_index(axis)
    step = 1
    while step * 2 < count:
        step *= 2
    while step >= 1 and count > 1:
        pairs = [(i, i + step) for i in range(0, count, 2 * step) if i + step < count]
        got = lax.ppermute(value, axis, pairs)
        value = jnp.where(me % (2 * step) == step, got, value)
        step //= 2
    return value


def tree_broadcast_from(value, axis, unit):
    count = lax.axis_size(axis)
    me = lax.axis_index(axis)
    step = unit
    while step * 2 < count:
        step *= 2
    while step >= unit:
        pairs = [(i, i + step) for i in range(0, count, 2 * step) if i + step < count]
        got = lax.ppermute(value, axis, pairs)
        value = jnp.where(me % (2 * step) == step, got, value)
        step //= 2
    return value


def tree_reduce(value, axis, step=1):
    count = lax.axis_size(axis)
    while step < count:
        pairs = [(i + step, i) for i in range(0, count, 2 * step) if i + step < count]
        value = value + lax.ppermute(value, axis, pairs)
        step *= 2
    return value


def xor_halving(flat, axis, steps):
    me = lax.axis_index(axis)
    count = lax.axis_size(axis)
    for step in steps:
        half = flat.shape[0] // 2
        upper = (me // step) % 2
        keep = lax.dynamic_slice_in_dim(flat, upper * half, half, 0)
        send = lax.dynamic_slice_in_dim(flat, (1 - upper) * half, half, 0)
        pairs = [(i, i ^ step) for i in range(count)]
        flat = keep + lax.ppermute(send, axis, pairs)
    return flat


def xor_doubling(piece, axis, steps):
    me = lax.axis_index(axis)
    count = lax.axis_size(axis)
    for step in reversed(steps):
        got = lax.ppermute(piece, axis, [(i, i ^ step) for i in range(count)])
        upper = (me // step) % 2 == 1
        piece = jnp.where(
            upper, jnp.concatenate([got, piece], 0), jnp.concatenate([piece, got], 0)
        )
    return piece


def direct_scatter(flat, axis, low, high):
    me = lax.axis_index(axis)
    j = me // low
    blk = flat.shape[0] // high
    total = lax.dynamic_slice_in_dim(flat, j * blk, blk, 0)
    for d in range(1, high):
        send = lax.dynamic_slice_in_dim(flat, ((j + d) % high) * blk, blk, 0)
        pairs = [
            (a * low + b, ((a + d) % high) * low + b) for a in range(high) for b in range(low)
        ]
        total = total + lax.ppermute(send, axis, pairs)
    return total


def direct_gather(piece, axis, low, high):
    me = lax.axis_index(axis)
    j = me // low
    out = jnp.zeros((high,) + piece.shape, piece.dtype)
    out = lax.dynamic_update_index_in_dim(out, piece, j, 0)
    for d in range(1, high):
        pairs = [
            (a * low + b, ((a + d) % high) * low + b) for a in range(high) for b in range(low)
        ]
        got = lax.ppermute(piece, axis, pairs)
        out = lax.dynamic_update_index_in_dim(out, got, (j - d) % high, 0)
    return out.reshape((-1,) + piece.shape[1:])


def is_pow2(n):
    return n >= 1 and (n & (n - 1)) == 0


def all_sum_rounded(flat, scale):
    n_tm = lax.axis_size("tm")
    n_sp = lax.axis_size("space")
    if not (is_pow2(n_tm) and is_pow2(n_sp)):
        return (lax.psum(flat, ("tm", "space")) * scale).astype(jnp.bfloat16), [], flat.shape[0]
    high = min(4, n_sp)
    low = n_sp // high
    tm_steps = []
    s = 1
    while s < n_tm:
        tm_steps.append(s)
        s *= 2
    sp_steps = []
    s = 1
    while s < low:
        sp_steps.append(s)
        s *= 2
    rows = flat.shape[0]
    unit = n_tm * n_sp * 8
    padded_rows = -(-rows // unit) * unit
    if padded_rows != rows:
        flat = jnp.pad(flat, ((0, padded_rows - rows), (0, 0)))
    flat = xor_halving(flat, "tm", tm_steps)
    flat = direct_scatter(flat, "space", low, high)
    flat = xor_halving(flat, "space", sp_steps)
    piece = (flat * scale).astype(jnp.bfloat16)
    piece = xor_doubling(piece, "space", sp_steps)
    piece = direct_gather(piece, "space", low, high)
    return piece, tm_steps, rows


def split_rows(gathered, cuts):
    piece, tm_steps, rows = gathered
    if len(tm_steps) != 1:
        whole = xor_doubling(piece, "tm", tm_steps)
        return [whole[a:b] for a, b in cuts]
    me = lax.axis_index("tm")
    got = lax.ppermute(piece, "tm", [(0, 1), (1, 0)])
    lower = jnp.where(me == 0, piece, got)
    upper = jnp.where(me == 0, got, piece)
    half = piece.shape[0]
    outs = []
    for a, b in cuts:
        parts = []
        if a < half:
            parts.append(lower[a : min(b, half)])
        if b > half:
            parts.append(upper[max(a, half) - half : b - half])
        outs.append(parts[0] if len(parts) == 1 else jnp.concatenate(parts, 0))
    return outs


def spatial_sum(padded, weights, flip):
    rows = padded.shape[2] - 2
    cols = padded.shape[3] - 2
    total = jnp.zeros(padded.shape[:2] + (rows, cols, weights.shape[2]), jnp.float32)
    for row_off in range(3):
        for col_off in range(3):
            if flip:
                piece = padded[
                    :, :, 2 - row_off : 2 - row_off + rows, 2 - col_off : 2 - col_off + cols
                ]
                kernel = weights[3 * row_off + col_off].T
            else:
                piece = padded[:, :, row_off : row_off + rows, col_off : col_off + cols]
                kernel = weights[3 * row_off + col_off]
            total = total + jnp.dot(piece, kernel, preferred_element_type=jnp.float32)
    return total


def lag_forward(padded_act, weights, count):
    total = 0.0
    for lag in range(3):
        total = total + jnp.dot(
            padded_act[:, 2 - lag : 2 - lag + count],
            weights[lag],
            preferred_element_type=jnp.float32,
        )
    return total


def lag_backward(padded_cot, weights, count):
    total = 0.0
    for lag in range(3):
        total = total + jnp.dot(
            padded_cot[:, lag : lag + count], weights[lag].T, preferred_element_type=jnp.float32
        )
    return total


def lag_grads(act, padded_cot, count):
    dims = (((0, 1, 2, 3), (0, 1, 2, 3)), ((), ()))
    terms = []
    for lag in range(3):
        terms.append(
            lax.dot_general(
                act,
                padded_cot[:, lag : lag + count],
                dims,
                preferred_element_type=jnp.float32,
            )
        )
    return jnp.stack(terms)


def row_halo(x):
    if lax.axis_size("tm") == 2:
        me = lax.axis_index("tm")
        edge = jnp.where(me == 0, x[:, :, -1:], x[:, :, :1])
        got = lax.ppermute(edge, "tm", [(0, 1), (1, 0)])
        zero = jnp.zeros_like(got)
        above = jnp.where(me == 1, got, zero)
        below = jnp.where(me == 0, got, zero)
        return jnp.concatenate([above, x, below], axis=2)
    above = shifted(x[:, :, -1:], "tm", 1)
    below = shifted(x[:, :, :1], "tm", -1)
    return jnp.concatenate([above, x, below], axis=2)


def on_device(latents, cotangent, valid_frames, spatial_weight, temporal_weight, cond_weight):
    clips, frames, rows, cols, chans = latents.shape
    slab = lax.axis_index("space")
    frame_ids = slab * frames + jnp.arange(frames, dtype=jnp.int32)
    mask = (frame_ids[None, :] < valid_frames[:, None]).astype(jnp.bfloat16)[:, :, None, None, None]
    mask_f = mask.astype(jnp.float32)
    masked = latents * mask
    cot = cotangent * mask
    pair_first = lax.axis_size("space") % 2 == 0
    if pair_first:
        first = tree_broadcast_from(masked[:, 0], "space", 2)
    else:
        first = tree_broadcast(masked[:, 0], "space")
    cot_local = jnp.sum(cot, axis=1, dtype=jnp.float32)
    later = shifted(cot, "space", -1)
    if lax.axis_size("space") % 2 == 0:
        cot_pair = cot_local + jnp.sum(later, axis=1, dtype=jnp.float32)
        cot_sum = tree_reduce(cot_pair, "space", 2)
    else:
        cot_sum = tree_reduce(cot_local, "space")
    rows_pad = row_halo(masked)
    padded = jnp.pad(rows_pad, ((0, 0), (0, 0), (0, 0), (1, 1), (0, 0)))
    pre = spatial_sum(padded, spatial_weight, False)
    act = jax.nn.silu(pre).astype(jnp.bfloat16)
    if pair_first:
        sent = shifted(jnp.concatenate([act, first[:, None]], axis=1), "space", 1)
        earlier = sent[:, :frames]
        first = jnp.where(slab % 2 == 1, sent[:, frames], first)
    else:
        earlier = shifted(act, "space", 1)
    act_pad = jnp.concatenate([earlier, act], axis=1)
    mixed = lag_forward(act_pad, temporal_weight, frames)
    cot_pad = jnp.concatenate([cot, later], axis=1)
    dact = lag_backward(cot_pad, temporal_weight, frames)
    temporal_terms = lag_grads(act, cot_pad, frames)
    cond = jnp.dot(first, cond_weight, preferred_element_type=jnp.float32)
    output = ((masked.astype(jnp.float32) + mixed + cond[:, None]) * mask_f).astype(jnp.bfloat16)
    sig = jax.nn.sigmoid(pre)
    dpre = (dact * sig * (1.0 + pre * (1.0 - sig))).astype(jnp.bfloat16)
    cond_back = jnp.dot(cot_sum, cond_weight.astype(jnp.float32).T, precision=lax.Precision.HIGHEST)
    dpre_rows = row_halo(dpre)
    dpre_pad = jnp.pad(dpre_rows, ((0, 0), (0, 0), (0, 0), (1, 1), (0, 0)))
    dmasked = spatial_sum(dpre_pad, spatial_weight, True)
    is_first = (frame_ids == 0).astype(jnp.float32)[None, :, None, None, None]
    grad_latents = (
        (cot.astype(jnp.float32) + dmasked + is_first * cond_back[:, None]) * mask_f
    ).astype(jnp.bfloat16)
    dims = (((0, 1, 2, 3), (0, 1, 2, 3)), ((), ()))
    spatial_terms = []
    for row_off in range(3):
        for col_off in range(3):
            piece = padded[:, :, row_off : row_off + rows, col_off : col_off + cols]
            spatial_terms.append(
                lax.dot_general(piece, dpre, dims, preferred_element_type=jnp.float32)
            )
    spatial_terms = jnp.stack(spatial_terms)
    cond_terms = lax.dot_general(
        first.astype(jnp.float32),
        cot_local,
        (((0, 1, 2), (0, 1, 2)), ((), ())),
        precision=lax.Precision.HIGHEST,
    )
    taps_s = spatial_terms.shape[0]
    taps_t = temporal_terms.shape[0]
    flat = jnp.concatenate(
        [
            spatial_terms.reshape(-1, chans),
            temporal_terms.reshape(-1, chans),
            cond_terms.reshape(-1, chans),
        ],
        axis=0,
    )
    scale = (clips * frames * rows * cols * lax.axis_size("space") * lax.axis_size("tm")) ** (-0.5)
    summed = all_sum_rounded(flat, scale)
    n_s = taps_s * chans
    n_t = taps_t * chans
    grad_spatial, grad_temporal, grad_cond = split_rows(
        summed, [(0, n_s), (n_s, n_s + n_t), (n_s + n_t, n_s + n_t + chans)]
    )
    grad_spatial = grad_spatial.reshape(taps_s, chans, chans)
    grad_temporal = grad_temporal.reshape(taps_t, chans, chans)
    return (output, grad_latents, grad_spatial, grad_temporal, grad_cond)


def solution(mesh):
    return jax.shard_map(
        on_device,
        mesh=mesh,
        in_specs=(
            P("groups", "space", "tm", None, None),
            P("groups", "space", "tm", None, None),
            P("groups"),
            P(),
            P(),
            P(),
        ),
        out_specs=(
            P("groups", "space", "tm", None, None),
            P("groups", "space", "tm", None, None),
            P("groups", None, None),
            P("groups", None, None),
            P("groups", None),
        ),
        check_vma=False,
    )
```

```python
import jax
import jax.numpy as jnp
from jax import lax
from jax.sharding import PartitionSpec as P


def shifted(value, axis, by):
    count = lax.axis_size(axis)
    pairs = [(i, i + by) for i in range(count) if 0 <= i + by < count]
    return lax.ppermute(value, axis, pairs)


def tree_broadcast(value, axis):
    count = lax.axis_size(axis)
    me = lax.axis_index(axis)
    step = 1
    while step * 2 < count:
        step *= 2
    while step >= 1 and count > 1:
        pairs = [(i, i + step) for i in range(0, count, 2 * step) if i + step < count]
        got = lax.ppermute(value, axis, pairs)
        value = jnp.where(me % (2 * step) == step, got, value)
        step //= 2
    return value


def tree_reduce(value, axis, step=1):
    count = lax.axis_size(axis)
    while step < count:
        pairs = [(i + step, i) for i in range(0, count, 2 * step) if i + step < count]
        value = value + lax.ppermute(value, axis, pairs)
        step *= 2
    return value


def two_column_sum(pair, local, axis):
    count = lax.axis_size(axis)
    me = lax.axis_index(axis)
    half = pair.shape[0] // 2
    odd = me % 2 == 1
    value = jnp.where(odd, pair[half:], pair[:half])
    n = count // 2
    step = 1
    while step < n:
        pairs = []
        for i in range(0, n, 2 * step):
            if i + step < n:
                pairs.append((2 * (i + step), 2 * i))
                if 2 * (i + step) + 1 < count:
                    pairs.append((2 * (i + step) + 1, 2 * i + 1))
        value = value + lax.ppermute(value, axis, pairs)
        step *= 2
    got = lax.ppermute(value, axis, [(1, 0)])
    return jnp.concatenate([value, got + local[half:]], axis=0)


def xor_halving(flat, axis, steps):
    me = lax.axis_index(axis)
    count = lax.axis_size(axis)
    for step in steps:
        half = flat.shape[0] // 2
        upper = (me // step) % 2
        keep = lax.dynamic_slice_in_dim(flat, upper * half, half, 0)
        send = lax.dynamic_slice_in_dim(flat, (1 - upper) * half, half, 0)
        pairs = [(i, i ^ step) for i in range(count)]
        flat = keep + lax.ppermute(send, axis, pairs)
    return flat


def xor_doubling(piece, axis, steps):
    me = lax.axis_index(axis)
    count = lax.axis_size(axis)
    for step in reversed(steps):
        got = lax.ppermute(piece, axis, [(i, i ^ step) for i in range(count)])
        upper = (me // step) % 2 == 1
        piece = jnp.where(
            upper, jnp.concatenate([got, piece], 0), jnp.concatenate([piece, got], 0)
        )
    return piece


def direct_scatter(flat, axis, low, high):
    me = lax.axis_index(axis)
    j = me // low
    blk = flat.shape[0] // high
    total = lax.dynamic_slice_in_dim(flat, j * blk, blk, 0)
    for d in range(1, high):
        send = lax.dynamic_slice_in_dim(flat, ((j + d) % high) * blk, blk, 0)
        pairs = [
            (a * low + b, ((a + d) % high) * low + b) for a in range(high) for b in range(low)
        ]
        total = total + lax.ppermute(send, axis, pairs)
    return total


def direct_gather(piece, axis, low, high):
    me = lax.axis_index(axis)
    j = me // low
    out = jnp.zeros((high,) + piece.shape, piece.dtype)
    out = lax.dynamic_update_index_in_dim(out, piece, j, 0)
    for d in range(1, high):
        pairs = [
            (a * low + b, ((a + d) % high) * low + b) for a in range(high) for b in range(low)
        ]
        got = lax.ppermute(piece, axis, pairs)
        out = lax.dynamic_update_index_in_dim(out, got, (j - d) % high, 0)
    return out.reshape((-1,) + piece.shape[1:])


def is_pow2(n):
    return n >= 1 and (n & (n - 1)) == 0


def all_sum_rounded(flat, scale):
    n_tm = lax.axis_size("tm")
    n_sp = lax.axis_size("space")
    if not (is_pow2(n_tm) and is_pow2(n_sp)):
        return (lax.psum(flat, ("tm", "space")) * scale).astype(jnp.bfloat16), [], flat.shape[0]
    high = min(4, n_sp)
    low = n_sp // high
    tm_steps = []
    s = 1
    while s < n_tm:
        tm_steps.append(s)
        s *= 2
    sp_steps = []
    s = 1
    while s < low:
        sp_steps.append(s)
        s *= 2
    rows = flat.shape[0]
    unit = n_tm * n_sp * 8
    padded_rows = -(-rows // unit) * unit
    if padded_rows != rows:
        flat = jnp.pad(flat, ((0, padded_rows - rows), (0, 0)))
    flat = xor_halving(flat, "tm", tm_steps)
    flat = direct_scatter(flat, "space", low, high)
    flat = xor_halving(flat, "space", sp_steps)
    piece = (flat * scale).astype(jnp.bfloat16)
    piece = xor_doubling(piece, "space", sp_steps)
    piece = direct_gather(piece, "space", low, high)
    return piece, tm_steps, rows


def split_rows(gathered, cuts):
    piece, tm_steps, rows = gathered
    if len(tm_steps) != 1:
        whole = xor_doubling(piece, "tm", tm_steps)
        return [whole[a:b] for a, b in cuts]
    me = lax.axis_index("tm")
    got = lax.ppermute(piece, "tm", [(0, 1), (1, 0)])
    lower = jnp.where(me == 0, piece, got)
    upper = jnp.where(me == 0, got, piece)
    half = piece.shape[0]
    outs = []
    for a, b in cuts:
        parts = []
        if a < half:
            parts.append(lower[a : min(b, half)])
        if b > half:
            parts.append(upper[max(a, half) - half : b - half])
        outs.append(parts[0] if len(parts) == 1 else jnp.concatenate(parts, 0))
    return outs


def spatial_sum(padded, weights, flip):
    rows = padded.shape[2] - 2
    cols = padded.shape[3] - 2
    total = jnp.zeros(padded.shape[:2] + (rows, cols, weights.shape[2]), jnp.float32)
    for row_off in range(3):
        for col_off in range(3):
            if flip:
                piece = padded[
                    :, :, 2 - row_off : 2 - row_off + rows, 2 - col_off : 2 - col_off + cols
                ]
                kernel = weights[3 * row_off + col_off].T
            else:
                piece = padded[:, :, row_off : row_off + rows, col_off : col_off + cols]
                kernel = weights[3 * row_off + col_off]
            total = total + jnp.dot(piece, kernel, preferred_element_type=jnp.float32)
    return total


def lag_forward(padded_act, weights, count):
    total = 0.0
    for lag in range(3):
        total = total + jnp.dot(
            padded_act[:, 2 - lag : 2 - lag + count],
            weights[lag],
            preferred_element_type=jnp.float32,
        )
    return total


def lag_backward(padded_cot, weights, count):
    total = 0.0
    for lag in range(3):
        total = total + jnp.dot(
            padded_cot[:, lag : lag + count], weights[lag].T, preferred_element_type=jnp.float32
        )
    return total


def lag_grads(act, padded_cot, count):
    dims = (((0, 1, 2, 3), (0, 1, 2, 3)), ((), ()))
    terms = []
    for lag in range(3):
        terms.append(
            lax.dot_general(
                act,
                padded_cot[:, lag : lag + count],
                dims,
                preferred_element_type=jnp.float32,
            )
        )
    return jnp.stack(terms)


def row_halo(x):
    if lax.axis_size("tm") == 2:
        me = lax.axis_index("tm")
        edge = jnp.where(me == 0, x[:, :, -1:], x[:, :, :1])
        got = lax.ppermute(edge, "tm", [(0, 1), (1, 0)])
        zero = jnp.zeros_like(got)
        above = jnp.where(me == 1, got, zero)
        below = jnp.where(me == 0, got, zero)
        return jnp.concatenate([above, x, below], axis=2)
    above = shifted(x[:, :, -1:], "tm", 1)
    below = shifted(x[:, :, :1], "tm", -1)
    return jnp.concatenate([above, x, below], axis=2)


def on_device(latents, cotangent, valid_frames, spatial_weight, temporal_weight, cond_weight):
    clips, frames, rows, cols, chans = latents.shape
    slab = lax.axis_index("space")
    frame_ids = slab * frames + jnp.arange(frames, dtype=jnp.int32)
    mask = (frame_ids[None, :] < valid_frames[:, None]).astype(jnp.bfloat16)[:, :, None, None, None]
    mask_f = mask.astype(jnp.float32)
    masked = latents * mask
    cot = cotangent * mask
    first = tree_broadcast(masked[:, 0], "space")
    cot_local = jnp.sum(cot, axis=1, dtype=jnp.float32)
    later = shifted(cot, "space", -1)
    if lax.axis_size("space") % 2 == 0:
        cot_pair = cot_local + jnp.sum(later, axis=1, dtype=jnp.float32)
        if clips % 2 == 0 and lax.axis_size("space") >= 4:
            cot_sum = two_column_sum(cot_pair, cot_local, "space")
        else:
            cot_sum = tree_reduce(cot_pair, "space", 2)
    else:
        cot_sum = tree_reduce(cot_local, "space")
    rows_pad = row_halo(masked)
    padded = jnp.pad(rows_pad, ((0, 0), (0, 0), (0, 0), (1, 1), (0, 0)))
    pre = spatial_sum(padded, spatial_weight, False)
    act = jax.nn.silu(pre).astype(jnp.bfloat16)
    earlier = shifted(act, "space", 1)
    act_pad = jnp.concatenate([earlier, act], axis=1)
    mixed = lag_forward(act_pad, temporal_weight, frames)
    cot_pad = jnp.concatenate([cot, later], axis=1)
    dact = lag_backward(cot_pad, temporal_weight, frames)
    temporal_terms = lag_grads(act, cot_pad, frames)
    cond = jnp.dot(first, cond_weight, preferred_element_type=jnp.float32)
    output = ((masked.astype(jnp.float32) + mixed + cond[:, None]) * mask_f).astype(jnp.bfloat16)
    sig = jax.nn.sigmoid(pre)
    dpre = (dact * sig * (1.0 + pre * (1.0 - sig))).astype(jnp.bfloat16)
    cond_back = jnp.dot(cot_sum, cond_weight.astype(jnp.float32).T, precision=lax.Precision.HIGHEST)
    dpre_rows = row_halo(dpre)
    dpre_pad = jnp.pad(dpre_rows, ((0, 0), (0, 0), (0, 0), (1, 1), (0, 0)))
    dmasked = spatial_sum(dpre_pad, spatial_weight, True)
    is_first = (frame_ids == 0).astype(jnp.float32)[None, :, None, None, None]
    grad_latents = (
        (cot.astype(jnp.float32) + dmasked + is_first * cond_back[:, None]) * mask_f
    ).astype(jnp.bfloat16)
    dims = (((0, 1, 2, 3), (0, 1, 2, 3)), ((), ()))
    spatial_terms = []
    for row_off in range(3):
        for col_off in range(3):
            piece = padded[:, :, row_off : row_off + rows, col_off : col_off + cols]
            spatial_terms.append(
                lax.dot_general(piece, dpre, dims, preferred_element_type=jnp.float32)
            )
    spatial_terms = jnp.stack(spatial_terms)
    cond_terms = lax.dot_general(
        first.astype(jnp.float32),
        cot_local,
        (((0, 1, 2), (0, 1, 2)), ((), ())),
        precision=lax.Precision.HIGHEST,
    )
    taps_s = spatial_terms.shape[0]
    taps_t = temporal_terms.shape[0]
    flat = jnp.concatenate(
        [
            spatial_terms.reshape(-1, chans),
            temporal_terms.reshape(-1, chans),
            cond_terms.reshape(-1, chans),
        ],
        axis=0,
    )
    scale = (clips * frames * rows * cols * lax.axis_size("space") * lax.axis_size("tm")) ** (-0.5)
    summed = all_sum_rounded(flat, scale)
    n_s = taps_s * chans
    n_t = taps_t * chans
    grad_spatial, grad_temporal, grad_cond = split_rows(
        summed, [(0, n_s), (n_s, n_s + n_t), (n_s + n_t, n_s + n_t + chans)]
    )
    grad_spatial = grad_spatial.reshape(taps_s, chans, chans)
    grad_temporal = grad_temporal.reshape(taps_t, chans, chans)
    return (output, grad_latents, grad_spatial, grad_temporal, grad_cond)


def solution(mesh):
    return jax.shard_map(
        on_device,
        mesh=mesh,
        in_specs=(
            P("groups", "space", "tm", None, None),
            P("groups", "space", "tm", None, None),
            P("groups"),
            P(),
            P(),
            P(),
        ),
        out_specs=(
            P("groups", "space", "tm", None, None),
            P("groups", "space", "tm", None, None),
            P("groups", None, None),
            P("groups", None, None),
            P("groups", None),
        ),
        check_vma=False,
    )
```

```python
import jax
import jax.numpy as jnp
from jax import lax
from jax.sharding import PartitionSpec as P


def shifted(value, axis, by):
    count = lax.axis_size(axis)
    pairs = [(i, i + by) for i in range(count) if 0 <= i + by < count]
    return lax.ppermute(value, axis, pairs)


def tree_broadcast(value, axis):
    count = lax.axis_size(axis)
    me = lax.axis_index(axis)
    step = 1
    while step * 2 < count:
        step *= 2
    while step >= 1 and count > 1:
        pairs = [(i, i + step) for i in range(0, count, 2 * step) if i + step < count]
        got = lax.ppermute(value, axis, pairs)
        value = jnp.where(me % (2 * step) == step, got, value)
        step //= 2
    return value


def tree_reduce(value, axis, step=1):
    count = lax.axis_size(axis)
    while step < count:
        pairs = [(i + step, i) for i in range(0, count, 2 * step) if i + step < count]
        value = value + lax.ppermute(value, axis, pairs)
        step *= 2
    return value


def two_column_broadcast(value, axis):
    count = lax.axis_size(axis)
    me = lax.axis_index(axis)
    half = value.shape[0] // 2
    odd = me % 2 == 1
    hop = lax.ppermute(value[half:], axis, [(0, 1)])
    part = jnp.where(odd, hop, value[:half])
    n = count // 2
    step = 1
    while step * 2 < n:
        step *= 2
    while step >= 1:
        pairs = []
        for i in range(0, n, 2 * step):
            if i + step < n:
                pairs.append((2 * i, 2 * (i + step)))
                if 2 * (i + step) + 1 < count:
                    pairs.append((2 * i + 1, 2 * (i + step) + 1))
        got = lax.ppermute(part, axis, pairs)
        part = jnp.where((me // 2) % (2 * step) == step, got, part)
        step //= 2
    other = lax.ppermute(part, axis, [(i, i ^ 1) for i in range(count)])
    return jnp.where(
        odd, jnp.concatenate([other, part], 0), jnp.concatenate([part, other], 0)
    )


def two_column_sum(pair, local, axis):
    count = lax.axis_size(axis)
    me = lax.axis_index(axis)
    half = pair.shape[0] // 2
    odd = me % 2 == 1
    value = jnp.where(odd, pair[half:], pair[:half])
    n = count // 2
    step = 1
    while step < n:
        pairs = []
        for i in range(0, n, 2 * step):
            if i + step < n:
                pairs.append((2 * (i + step), 2 * i))
                if 2 * (i + step) + 1 < count:
                    pairs.append((2 * (i + step) + 1, 2 * i + 1))
        value = value + lax.ppermute(value, axis, pairs)
        step *= 2
    got = lax.ppermute(value, axis, [(1, 0)])
    return jnp.concatenate([value, got + local[half:]], axis=0)


def xor_halving(flat, axis, steps):
    me = lax.axis_index(axis)
    count = lax.axis_size(axis)
    for step in steps:
        half = flat.shape[0] // 2
        upper = (me // step) % 2
        keep = lax.dynamic_slice_in_dim(flat, upper * half, half, 0)
        send = lax.dynamic_slice_in_dim(flat, (1 - upper) * half, half, 0)
        pairs = [(i, i ^ step) for i in range(count)]
        flat = keep + lax.ppermute(send, axis, pairs)
    return flat


def xor_doubling(piece, axis, steps):
    me = lax.axis_index(axis)
    count = lax.axis_size(axis)
    for step in reversed(steps):
        got = lax.ppermute(piece, axis, [(i, i ^ step) for i in range(count)])
        upper = (me // step) % 2 == 1
        piece = jnp.where(
            upper, jnp.concatenate([got, piece], 0), jnp.concatenate([piece, got], 0)
        )
    return piece


def direct_scatter(flat, axis, low, high):
    me = lax.axis_index(axis)
    j = me // low
    blk = flat.shape[0] // high
    total = lax.dynamic_slice_in_dim(flat, j * blk, blk, 0)
    for d in range(1, high):
        send = lax.dynamic_slice_in_dim(flat, ((j + d) % high) * blk, blk, 0)
        pairs = [
            (a * low + b, ((a + d) % high) * low + b) for a in range(high) for b in range(low)
        ]
        total = total + lax.ppermute(send, axis, pairs)
    return total


def direct_gather(piece, axis, low, high):
    me = lax.axis_index(axis)
    j = me // low
    out = jnp.zeros((high,) + piece.shape, piece.dtype)
    out = lax.dynamic_update_index_in_dim(out, piece, j, 0)
    for d in range(1, high):
        pairs = [
            (a * low + b, ((a + d) % high) * low + b) for a in range(high) for b in range(low)
        ]
        got = lax.ppermute(piece, axis, pairs)
        out = lax.dynamic_update_index_in_dim(out, got, (j - d) % high, 0)
    return out.reshape((-1,) + piece.shape[1:])


def is_pow2(n):
    return n >= 1 and (n & (n - 1)) == 0


def all_sum_rounded(flat, scale):
    n_tm = lax.axis_size("tm")
    n_sp = lax.axis_size("space")
    if not (is_pow2(n_tm) and is_pow2(n_sp)):
        return (lax.psum(flat, ("tm", "space")) * scale).astype(jnp.bfloat16), [], flat.shape[0]
    high = min(4, n_sp)
    low = n_sp // high
    tm_steps = []
    s = 1
    while s < n_tm:
        tm_steps.append(s)
        s *= 2
    sp_steps = []
    s = 1
    while s < low:
        sp_steps.append(s)
        s *= 2
    rows = flat.shape[0]
    unit = n_tm * n_sp * 8
    padded_rows = -(-rows // unit) * unit
    if padded_rows != rows:
        flat = jnp.pad(flat, ((0, padded_rows - rows), (0, 0)))
    flat = xor_halving(flat, "tm", tm_steps)
    flat = direct_scatter(flat, "space", low, high)
    flat = xor_halving(flat, "space", sp_steps)
    piece = (flat * scale).astype(jnp.bfloat16)
    piece = xor_doubling(piece, "space", sp_steps)
    piece = direct_gather(piece, "space", low, high)
    return piece, tm_steps, rows


def split_rows(gathered, cuts):
    piece, tm_steps, rows = gathered
    if len(tm_steps) != 1:
        whole = xor_doubling(piece, "tm", tm_steps)
        return [whole[a:b] for a, b in cuts]
    me = lax.axis_index("tm")
    got = lax.ppermute(piece, "tm", [(0, 1), (1, 0)])
    lower = jnp.where(me == 0, piece, got)
    upper = jnp.where(me == 0, got, piece)
    half = piece.shape[0]
    outs = []
    for a, b in cuts:
        parts = []
        if a < half:
            parts.append(lower[a : min(b, half)])
        if b > half:
            parts.append(upper[max(a, half) - half : b - half])
        outs.append(parts[0] if len(parts) == 1 else jnp.concatenate(parts, 0))
    return outs


def spatial_sum(padded, weights, flip):
    rows = padded.shape[2] - 2
    cols = padded.shape[3] - 2
    total = jnp.zeros(padded.shape[:2] + (rows, cols, weights.shape[2]), jnp.float32)
    for row_off in range(3):
        for col_off in range(3):
            if flip:
                piece = padded[
                    :, :, 2 - row_off : 2 - row_off + rows, 2 - col_off : 2 - col_off + cols
                ]
                kernel = weights[3 * row_off + col_off].T
            else:
                piece = padded[:, :, row_off : row_off + rows, col_off : col_off + cols]
                kernel = weights[3 * row_off + col_off]
            total = total + jnp.dot(piece, kernel, preferred_element_type=jnp.float32)
    return total


def lag_forward(padded_act, weights, count):
    total = 0.0
    for lag in range(3):
        total = total + jnp.dot(
            padded_act[:, 2 - lag : 2 - lag + count],
            weights[lag],
            preferred_element_type=jnp.float32,
        )
    return total


def lag_backward(padded_cot, weights, count):
    total = 0.0
    for lag in range(3):
        total = total + jnp.dot(
            padded_cot[:, lag : lag + count], weights[lag].T, preferred_element_type=jnp.float32
        )
    return total


def lag_grads(act, padded_cot, count):
    dims = (((0, 1, 2, 3), (0, 1, 2, 3)), ((), ()))
    terms = []
    for lag in range(3):
        terms.append(
            lax.dot_general(
                act,
                padded_cot[:, lag : lag + count],
                dims,
                preferred_element_type=jnp.float32,
            )
        )
    return jnp.stack(terms)


def row_halo(x):
    if lax.axis_size("tm") == 2:
        me = lax.axis_index("tm")
        edge = jnp.where(me == 0, x[:, :, -1:], x[:, :, :1])
        got = lax.ppermute(edge, "tm", [(0, 1), (1, 0)])
        zero = jnp.zeros_like(got)
        above = jnp.where(me == 1, got, zero)
        below = jnp.where(me == 0, got, zero)
        return jnp.concatenate([above, x, below], axis=2)
    above = shifted(x[:, :, -1:], "tm", 1)
    below = shifted(x[:, :, :1], "tm", -1)
    return jnp.concatenate([above, x, below], axis=2)


def on_device(latents, cotangent, valid_frames, spatial_weight, temporal_weight, cond_weight):
    clips, frames, rows, cols, chans = latents.shape
    slab = lax.axis_index("space")
    frame_ids = slab * frames + jnp.arange(frames, dtype=jnp.int32)
    mask = (frame_ids[None, :] < valid_frames[:, None]).astype(jnp.bfloat16)[:, :, None, None, None]
    mask_f = mask.astype(jnp.float32)
    masked = latents * mask
    cot = cotangent * mask
    if clips % 2 == 0 and lax.axis_size("space") >= 4 and lax.axis_size("space") % 2 == 0:
        first = two_column_broadcast(masked[:, 0], "space")
    else:
        first = tree_broadcast(masked[:, 0], "space")
    cot_local = jnp.sum(cot, axis=1, dtype=jnp.float32)
    later = shifted(cot, "space", -1)
    if lax.axis_size("space") % 2 == 0:
        cot_pair = cot_local + jnp.sum(later, axis=1, dtype=jnp.float32)
        if clips % 2 == 0 and lax.axis_size("space") >= 4:
            cot_sum = two_column_sum(cot_pair, cot_local, "space")
        else:
            cot_sum = tree_reduce(cot_pair, "space", 2)
    else:
        cot_sum = tree_reduce(cot_local, "space")
    rows_pad = row_halo(masked)
    padded = jnp.pad(rows_pad, ((0, 0), (0, 0), (0, 0), (1, 1), (0, 0)))
    pre = spatial_sum(padded, spatial_weight, False)
    act = jax.nn.silu(pre).astype(jnp.bfloat16)
    earlier = shifted(act, "space", 1)
    act_pad = jnp.concatenate([earlier, act], axis=1)
    mixed = lag_forward(act_pad, temporal_weight, frames)
    cot_pad = jnp.concatenate([cot, later], axis=1)
    dact = lag_backward(cot_pad, temporal_weight, frames)
    temporal_terms = lag_grads(act, cot_pad, frames)
    cond = jnp.dot(first, cond_weight, preferred_element_type=jnp.float32)
    output = ((masked.astype(jnp.float32) + mixed + cond[:, None]) * mask_f).astype(jnp.bfloat16)
    sig = jax.nn.sigmoid(pre)
    dpre = (dact * sig * (1.0 + pre * (1.0 - sig))).astype(jnp.bfloat16)
    cond_back = jnp.dot(cot_sum, cond_weight.astype(jnp.float32).T, precision=lax.Precision.HIGHEST)
    dpre_rows = row_halo(dpre)
    dpre_pad = jnp.pad(dpre_rows, ((0, 0), (0, 0), (0, 0), (1, 1), (0, 0)))
    dmasked = spatial_sum(dpre_pad, spatial_weight, True)
    is_first = (frame_ids == 0).astype(jnp.float32)[None, :, None, None, None]
    grad_latents = (
        (cot.astype(jnp.float32) + dmasked + is_first * cond_back[:, None]) * mask_f
    ).astype(jnp.bfloat16)
    dims = (((0, 1, 2, 3), (0, 1, 2, 3)), ((), ()))
    spatial_terms = []
    for row_off in range(3):
        for col_off in range(3):
            piece = padded[:, :, row_off : row_off + rows, col_off : col_off + cols]
            spatial_terms.append(
                lax.dot_general(piece, dpre, dims, preferred_element_type=jnp.float32)
            )
    spatial_terms = jnp.stack(spatial_terms)
    cond_terms = lax.dot_general(
        first.astype(jnp.float32),
        cot_local,
        (((0, 1, 2), (0, 1, 2)), ((), ())),
        precision=lax.Precision.HIGHEST,
    )
    taps_s = spatial_terms.shape[0]
    taps_t = temporal_terms.shape[0]
    flat = jnp.concatenate(
        [
            spatial_terms.reshape(-1, chans),
            temporal_terms.reshape(-1, chans),
            cond_terms.reshape(-1, chans),
        ],
        axis=0,
    )
    scale = (clips * frames * rows * cols * lax.axis_size("space") * lax.axis_size("tm")) ** (-0.5)
    summed = all_sum_rounded(flat, scale)
    n_s = taps_s * chans
    n_t = taps_t * chans
    grad_spatial, grad_temporal, grad_cond = split_rows(
        summed, [(0, n_s), (n_s, n_s + n_t), (n_s + n_t, n_s + n_t + chans)]
    )
    grad_spatial = grad_spatial.reshape(taps_s, chans, chans)
    grad_temporal = grad_temporal.reshape(taps_t, chans, chans)
    return (output, grad_latents, grad_spatial, grad_temporal, grad_cond)


def solution(mesh):
    return jax.shard_map(
        on_device,
        mesh=mesh,
        in_specs=(
            P("groups", "space", "tm", None, None),
            P("groups", "space", "tm", None, None),
            P("groups"),
            P(),
            P(),
            P(),
        ),
        out_specs=(
            P("groups", "space", "tm", None, None),
            P("groups", "space", "tm", None, None),
            P("groups", None, None),
            P("groups", None, None),
            P("groups", None),
        ),
        check_vma=False,
    )
```

```python
import jax
import jax.numpy as jnp
from jax import lax
from jax.sharding import PartitionSpec as P


def shifted(value, axis, by):
    count = lax.axis_size(axis)
    pairs = [(i, i + by) for i in range(count) if 0 <= i + by < count]
    return lax.ppermute(value, axis, pairs)


def tree_broadcast(value, axis):
    count = lax.axis_size(axis)
    me = lax.axis_index(axis)
    step = 1
    while step * 2 < count:
        step *= 2
    while step >= 1 and count > 1:
        pairs = [(i, i + step) for i in range(0, count, 2 * step) if i + step < count]
        got = lax.ppermute(value, axis, pairs)
        value = jnp.where(me % (2 * step) == step, got, value)
        step //= 2
    return value


def tree_reduce(value, axis, step=1):
    count = lax.axis_size(axis)
    while step < count:
        pairs = [(i + step, i) for i in range(0, count, 2 * step) if i + step < count]
        value = value + lax.ppermute(value, axis, pairs)
        step *= 2
    return value


def two_column_sum(pair, local, axis):
    count = lax.axis_size(axis)
    me = lax.axis_index(axis)
    half = pair.shape[0] // 2
    odd = me % 2 == 1
    value = jnp.where(odd, pair[half:], pair[:half])
    n = count // 2
    step = 1
    while step < n:
        pairs = []
        for i in range(0, n, 2 * step):
            if i + step < n:
                pairs.append((2 * (i + step), 2 * i))
                if 2 * (i + step) + 1 < count:
                    pairs.append((2 * (i + step) + 1, 2 * i + 1))
        value = value + lax.ppermute(value, axis, pairs)
        step *= 2
    got = lax.ppermute(value, axis, [(1, 0)])
    return jnp.concatenate([value, got + local[half:]], axis=0)


def xor_halving(flat, axis, steps):
    me = lax.axis_index(axis)
    count = lax.axis_size(axis)
    for step in steps:
        half = flat.shape[0] // 2
        upper = (me // step) % 2
        keep = lax.dynamic_slice_in_dim(flat, upper * half, half, 0)
        send = lax.dynamic_slice_in_dim(flat, (1 - upper) * half, half, 0)
        pairs = [(i, i ^ step) for i in range(count)]
        flat = keep + lax.ppermute(send, axis, pairs)
    return flat


def xor_doubling(piece, axis, steps):
    me = lax.axis_index(axis)
    count = lax.axis_size(axis)
    for step in reversed(steps):
        got = lax.ppermute(piece, axis, [(i, i ^ step) for i in range(count)])
        upper = (me // step) % 2 == 1
        piece = jnp.where(
            upper, jnp.concatenate([got, piece], 0), jnp.concatenate([piece, got], 0)
        )
    return piece


def direct_scatter(flat, axis, low, high):
    me = lax.axis_index(axis)
    j = me // low
    blk = flat.shape[0] // high
    total = lax.dynamic_slice_in_dim(flat, j * blk, blk, 0)
    for d in range(1, high):
        send = lax.dynamic_slice_in_dim(flat, ((j + d) % high) * blk, blk, 0)
        pairs = [
            (a * low + b, ((a + d) % high) * low + b) for a in range(high) for b in range(low)
        ]
        total = total + lax.ppermute(send, axis, pairs)
    return total


def direct_gather(piece, axis, low, high):
    me = lax.axis_index(axis)
    j = me // low
    out = jnp.zeros((high,) + piece.shape, piece.dtype)
    out = lax.dynamic_update_index_in_dim(out, piece, j, 0)
    for d in range(1, high):
        pairs = [
            (a * low + b, ((a + d) % high) * low + b) for a in range(high) for b in range(low)
        ]
        got = lax.ppermute(piece, axis, pairs)
        out = lax.dynamic_update_index_in_dim(out, got, (j - d) % high, 0)
    return out.reshape((-1,) + piece.shape[1:])


def is_pow2(n):
    return n >= 1 and (n & (n - 1)) == 0


def all_sum_rounded(flat, scale):
    n_tm = lax.axis_size("tm")
    n_sp = lax.axis_size("space")
    if not (is_pow2(n_tm) and is_pow2(n_sp)):
        return (lax.psum(flat, ("tm", "space")) * scale).astype(jnp.bfloat16), [], flat.shape[0]
    high = min(4, n_sp)
    low = n_sp // high
    tm_steps = []
    s = 1
    while s < n_tm:
        tm_steps.append(s)
        s *= 2
    sp_steps = []
    s = 1
    while s < low:
        sp_steps.append(s)
        s *= 2
    rows = flat.shape[0]
    unit = n_tm * n_sp * 8
    padded_rows = -(-rows // unit) * unit
    if padded_rows != rows:
        flat = jnp.pad(flat, ((0, padded_rows - rows), (0, 0)))
    flat = xor_halving(flat, "tm", tm_steps)
    flat = xor_halving(flat, "space", sp_steps)
    flat = direct_scatter(flat, "space", low, high)
    piece = (flat * scale).astype(jnp.bfloat16)
    piece = direct_gather(piece, "space", low, high)
    piece = xor_doubling(piece, "space", sp_steps)
    return piece, tm_steps, rows


def split_rows(gathered, cuts):
    piece, tm_steps, rows = gathered
    if len(tm_steps) != 1:
        whole = xor_doubling(piece, "tm", tm_steps)
        return [whole[a:b] for a, b in cuts]
    me = lax.axis_index("tm")
    got = lax.ppermute(piece, "tm", [(0, 1), (1, 0)])
    lower = jnp.where(me == 0, piece, got)
    upper = jnp.where(me == 0, got, piece)
    half = piece.shape[0]
    outs = []
    for a, b in cuts:
        parts = []
        if a < half:
            parts.append(lower[a : min(b, half)])
        if b > half:
            parts.append(upper[max(a, half) - half : b - half])
        outs.append(parts[0] if len(parts) == 1 else jnp.concatenate(parts, 0))
    return outs


def spatial_sum(padded, weights, flip):
    rows = padded.shape[2] - 2
    cols = padded.shape[3] - 2
    total = jnp.zeros(padded.shape[:2] + (rows, cols, weights.shape[2]), jnp.float32)
    for row_off in range(3):
        for col_off in range(3):
            if flip:
                piece = padded[
                    :, :, 2 - row_off : 2 - row_off + rows, 2 - col_off : 2 - col_off + cols
                ]
                kernel = weights[3 * row_off + col_off].T
            else:
                piece = padded[:, :, row_off : row_off + rows, col_off : col_off + cols]
                kernel = weights[3 * row_off + col_off]
            total = total + jnp.dot(piece, kernel, preferred_element_type=jnp.float32)
    return total


def lag_forward(padded_act, weights, count):
    total = 0.0
    for lag in range(3):
        total = total + jnp.dot(
            padded_act[:, 2 - lag : 2 - lag + count],
            weights[lag],
            preferred_element_type=jnp.float32,
        )
    return total


def lag_backward(padded_cot, weights, count):
    total = 0.0
    for lag in range(3):
        total = total + jnp.dot(
            padded_cot[:, lag : lag + count], weights[lag].T, preferred_element_type=jnp.float32
        )
    return total


def lag_grads(act, padded_cot, count):
    dims = (((0, 1, 2, 3), (0, 1, 2, 3)), ((), ()))
    terms = []
    for lag in range(3):
        terms.append(
            lax.dot_general(
                act,
                padded_cot[:, lag : lag + count],
                dims,
                preferred_element_type=jnp.float32,
            )
        )
    return jnp.stack(terms)


def row_halo(x):
    if lax.axis_size("tm") == 2:
        me = lax.axis_index("tm")
        edge = jnp.where(me == 0, x[:, :, -1:], x[:, :, :1])
        got = lax.ppermute(edge, "tm", [(0, 1), (1, 0)])
        zero = jnp.zeros_like(got)
        above = jnp.where(me == 1, got, zero)
        below = jnp.where(me == 0, got, zero)
        return jnp.concatenate([above, x, below], axis=2)
    above = shifted(x[:, :, -1:], "tm", 1)
    below = shifted(x[:, :, :1], "tm", -1)
    return jnp.concatenate([above, x, below], axis=2)


def on_device(latents, cotangent, valid_frames, spatial_weight, temporal_weight, cond_weight):
    clips, frames, rows, cols, chans = latents.shape
    slab = lax.axis_index("space")
    frame_ids = slab * frames + jnp.arange(frames, dtype=jnp.int32)
    mask = (frame_ids[None, :] < valid_frames[:, None]).astype(jnp.bfloat16)[:, :, None, None, None]
    mask_f = mask.astype(jnp.float32)
    masked = latents * mask
    cot = cotangent * mask
    first = tree_broadcast(masked[:, 0], "space")
    cot_local = jnp.sum(cot, axis=1, dtype=jnp.float32)
    later = shifted(cot, "space", -1)
    if lax.axis_size("space") % 2 == 0:
        cot_pair = cot_local + jnp.sum(later, axis=1, dtype=jnp.float32)
        if clips % 2 == 0 and lax.axis_size("space") >= 4:
            cot_sum = two_column_sum(cot_pair, cot_local, "space")
        else:
            cot_sum = tree_reduce(cot_pair, "space", 2)
    else:
        cot_sum = tree_reduce(cot_local, "space")
    rows_pad = row_halo(masked)
    padded = jnp.pad(rows_pad, ((0, 0), (0, 0), (0, 0), (1, 1), (0, 0)))
    pre = spatial_sum(padded, spatial_weight, False)
    act = jax.nn.silu(pre).astype(jnp.bfloat16)
    earlier = shifted(act, "space", 1)
    act_pad = jnp.concatenate([earlier, act], axis=1)
    mixed = lag_forward(act_pad, temporal_weight, frames)
    cot_pad = jnp.concatenate([cot, later], axis=1)
    dact = lag_backward(cot_pad, temporal_weight, frames)
    temporal_terms = lag_grads(act, cot_pad, frames)
    cond = jnp.dot(first, cond_weight, preferred_element_type=jnp.float32)
    output = ((masked.astype(jnp.float32) + mixed + cond[:, None]) * mask_f).astype(jnp.bfloat16)
    sig = jax.nn.sigmoid(pre)
    dpre = (dact * sig * (1.0 + pre * (1.0 - sig))).astype(jnp.bfloat16)
    cond_back = jnp.dot(cot_sum, cond_weight.astype(jnp.float32).T, precision=lax.Precision.HIGHEST)
    dpre_rows = row_halo(dpre)
    dpre_pad = jnp.pad(dpre_rows, ((0, 0), (0, 0), (0, 0), (1, 1), (0, 0)))
    dmasked = spatial_sum(dpre_pad, spatial_weight, True)
    is_first = (frame_ids == 0).astype(jnp.float32)[None, :, None, None, None]
    grad_latents = (
        (cot.astype(jnp.float32) + dmasked + is_first * cond_back[:, None]) * mask_f
    ).astype(jnp.bfloat16)
    dims = (((0, 1, 2, 3), (0, 1, 2, 3)), ((), ()))
    spatial_terms = []
    for row_off in range(3):
        for col_off in range(3):
            piece = padded[:, :, row_off : row_off + rows, col_off : col_off + cols]
            spatial_terms.append(
                lax.dot_general(piece, dpre, dims, preferred_element_type=jnp.float32)
            )
    spatial_terms = jnp.stack(spatial_terms)
    cond_terms = lax.dot_general(
        first.astype(jnp.float32),
        cot_local,
        (((0, 1, 2), (0, 1, 2)), ((), ())),
        precision=lax.Precision.HIGHEST,
    )
    taps_s = spatial_terms.shape[0]
    taps_t = temporal_terms.shape[0]
    flat = jnp.concatenate(
        [
            spatial_terms.reshape(-1, chans),
            temporal_terms.reshape(-1, chans),
            cond_terms.reshape(-1, chans),
        ],
        axis=0,
    )
    scale = (clips * frames * rows * cols * lax.axis_size("space") * lax.axis_size("tm")) ** (-0.5)
    summed = all_sum_rounded(flat, scale)
    n_s = taps_s * chans
    n_t = taps_t * chans
    grad_spatial, grad_temporal, grad_cond = split_rows(
        summed, [(0, n_s), (n_s, n_s + n_t), (n_s + n_t, n_s + n_t + chans)]
    )
    grad_spatial = grad_spatial.reshape(taps_s, chans, chans)
    grad_temporal = grad_temporal.reshape(taps_t, chans, chans)
    return (output, grad_latents, grad_spatial, grad_temporal, grad_cond)


def solution(mesh):
    return jax.shard_map(
        on_device,
        mesh=mesh,
        in_specs=(
            P("groups", "space", "tm", None, None),
            P("groups", "space", "tm", None, None),
            P("groups"),
            P(),
            P(),
            P(),
        ),
        out_specs=(
            P("groups", "space", "tm", None, None),
            P("groups", "space", "tm", None, None),
            P("groups", None, None),
            P("groups", None, None),
            P("groups", None),
        ),
        check_vma=False,
    )
```

```python
import jax
import jax.numpy as jnp
from jax import lax
from jax.sharding import PartitionSpec as P


def shifted(value, axis, by):
    count = lax.axis_size(axis)
    pairs = [(i, i + by) for i in range(count) if 0 <= i + by < count]
    return lax.ppermute(value, axis, pairs)


def tree_broadcast(value, axis):
    count = lax.axis_size(axis)
    me = lax.axis_index(axis)
    step = 1
    while step * 2 < count:
        step *= 2
    while step >= 1 and count > 1:
        pairs = [(i, i + step) for i in range(0, count, 2 * step) if i + step < count]
        got = lax.ppermute(value, axis, pairs)
        value = jnp.where(me % (2 * step) == step, got, value)
        step //= 2
    return value


def tree_reduce(value, axis, step=1):
    count = lax.axis_size(axis)
    while step < count:
        pairs = [(i + step, i) for i in range(0, count, 2 * step) if i + step < count]
        value = value + lax.ppermute(value, axis, pairs)
        step *= 2
    return value


def two_column_sum(pair, local, axis):
    count = lax.axis_size(axis)
    me = lax.axis_index(axis)
    half = pair.shape[0] // 2
    odd = me % 2 == 1
    value = jnp.where(odd, pair[half:], pair[:half])
    n = count // 2
    step = 1
    while step * 2 < n:
        step *= 2
    while step >= 1:
        pairs = []
        for i in range(n):
            if i < step and i + step < n:
                pairs.append((2 * (i + step), 2 * i))
                if 2 * (i + step) + 1 < count:
                    pairs.append((2 * (i + step) + 1, 2 * i + 1))
        value = value + lax.ppermute(value, axis, pairs)
        step //= 2
    got = lax.ppermute(value, axis, [(1, 0)])
    return jnp.concatenate([value, got + local[half:]], axis=0)


def xor_halving(flat, axis, steps):
    me = lax.axis_index(axis)
    count = lax.axis_size(axis)
    for step in steps:
        half = flat.shape[0] // 2
        upper = (me // step) % 2
        keep = lax.dynamic_slice_in_dim(flat, upper * half, half, 0)
        send = lax.dynamic_slice_in_dim(flat, (1 - upper) * half, half, 0)
        pairs = [(i, i ^ step) for i in range(count)]
        flat = keep + lax.ppermute(send, axis, pairs)
    return flat


def xor_doubling(piece, axis, steps):
    me = lax.axis_index(axis)
    count = lax.axis_size(axis)
    for step in reversed(steps):
        got = lax.ppermute(piece, axis, [(i, i ^ step) for i in range(count)])
        upper = (me // step) % 2 == 1
        piece = jnp.where(
            upper, jnp.concatenate([got, piece], 0), jnp.concatenate([piece, got], 0)
        )
    return piece


def direct_scatter(flat, axis, low, high):
    me = lax.axis_index(axis)
    j = me // low
    blk = flat.shape[0] // high
    total = lax.dynamic_slice_in_dim(flat, j * blk, blk, 0)
    for d in range(1, high):
        send = lax.dynamic_slice_in_dim(flat, ((j + d) % high) * blk, blk, 0)
        pairs = [
            (a * low + b, ((a + d) % high) * low + b) for a in range(high) for b in range(low)
        ]
        total = total + lax.ppermute(send, axis, pairs)
    return total


def direct_gather(piece, axis, low, high):
    me = lax.axis_index(axis)
    j = me // low
    out = jnp.zeros((high,) + piece.shape, piece.dtype)
    out = lax.dynamic_update_index_in_dim(out, piece, j, 0)
    for d in range(1, high):
        pairs = [
            (a * low + b, ((a + d) % high) * low + b) for a in range(high) for b in range(low)
        ]
        got = lax.ppermute(piece, axis, pairs)
        out = lax.dynamic_update_index_in_dim(out, got, (j - d) % high, 0)
    return out.reshape((-1,) + piece.shape[1:])


def is_pow2(n):
    return n >= 1 and (n & (n - 1)) == 0


def all_sum_rounded(flat, scale):
    n_tm = lax.axis_size("tm")
    n_sp = lax.axis_size("space")
    if not (is_pow2(n_tm) and is_pow2(n_sp)):
        return (lax.psum(flat, ("tm", "space")) * scale).astype(jnp.bfloat16), [], flat.shape[0]
    high = min(4, n_sp)
    low = n_sp // high
    tm_steps = []
    s = 1
    while s < n_tm:
        tm_steps.append(s)
        s *= 2
    sp_steps = []
    s = 1
    while s < low:
        sp_steps.append(s)
        s *= 2
    rows = flat.shape[0]
    unit = n_tm * n_sp * 8
    padded_rows = -(-rows // unit) * unit
    if padded_rows != rows:
        flat = jnp.pad(flat, ((0, padded_rows - rows), (0, 0)))
    flat = xor_halving(flat, "tm", tm_steps)
    flat = xor_halving(flat, "space", sp_steps)
    flat = direct_scatter(flat, "space", low, high)
    piece = (flat * scale).astype(jnp.bfloat16)
    piece = direct_gather(piece, "space", low, high)
    piece = xor_doubling(piece, "space", sp_steps)
    return piece, tm_steps, rows


def split_rows(gathered, cuts):
    piece, tm_steps, rows = gathered
    if len(tm_steps) != 1:
        whole = xor_doubling(piece, "tm", tm_steps)
        return [whole[a:b] for a, b in cuts]
    me = lax.axis_index("tm")
    got = lax.ppermute(piece, "tm", [(0, 1), (1, 0)])
    lower = jnp.where(me == 0, piece, got)
    upper = jnp.where(me == 0, got, piece)
    half = piece.shape[0]
    outs = []
    for a, b in cuts:
        parts = []
        if a < half:
            parts.append(lower[a : min(b, half)])
        if b > half:
            parts.append(upper[max(a, half) - half : b - half])
        outs.append(parts[0] if len(parts) == 1 else jnp.concatenate(parts, 0))
    return outs


def spatial_sum(padded, weights, flip):
    rows = padded.shape[2] - 2
    cols = padded.shape[3] - 2
    total = jnp.zeros(padded.shape[:2] + (rows, cols, weights.shape[2]), jnp.float32)
    for row_off in range(3):
        for col_off in range(3):
            if flip:
                piece = padded[
                    :, :, 2 - row_off : 2 - row_off + rows, 2 - col_off : 2 - col_off + cols
                ]
                kernel = weights[3 * row_off + col_off].T
            else:
                piece = padded[:, :, row_off : row_off + rows, col_off : col_off + cols]
                kernel = weights[3 * row_off + col_off]
            total = total + jnp.dot(piece, kernel, preferred_element_type=jnp.float32)
    return total


def lag_forward(padded_act, weights, count):
    total = 0.0
    for lag in range(3):
        total = total + jnp.dot(
            padded_act[:, 2 - lag : 2 - lag + count],
            weights[lag],
            preferred_element_type=jnp.float32,
        )
    return total


def lag_backward(padded_cot, weights, count):
    total = 0.0
    for lag in range(3):
        total = total + jnp.dot(
            padded_cot[:, lag : lag + count], weights[lag].T, preferred_element_type=jnp.float32
        )
    return total


def lag_grads(act, padded_cot, count):
    dims = (((0, 1, 2, 3), (0, 1, 2, 3)), ((), ()))
    terms = []
    for lag in range(3):
        terms.append(
            lax.dot_general(
                act,
                padded_cot[:, lag : lag + count],
                dims,
                preferred_element_type=jnp.float32,
            )
        )
    return jnp.stack(terms)


def row_halo(x):
    if lax.axis_size("tm") == 2:
        me = lax.axis_index("tm")
        edge = jnp.where(me == 0, x[:, :, -1:], x[:, :, :1])
        got = lax.ppermute(edge, "tm", [(0, 1), (1, 0)])
        zero = jnp.zeros_like(got)
        above = jnp.where(me == 1, got, zero)
        below = jnp.where(me == 0, got, zero)
        return jnp.concatenate([above, x, below], axis=2)
    above = shifted(x[:, :, -1:], "tm", 1)
    below = shifted(x[:, :, :1], "tm", -1)
    return jnp.concatenate([above, x, below], axis=2)


def on_device(latents, cotangent, valid_frames, spatial_weight, temporal_weight, cond_weight):
    clips, frames, rows, cols, chans = latents.shape
    slab = lax.axis_index("space")
    frame_ids = slab * frames + jnp.arange(frames, dtype=jnp.int32)
    mask = (frame_ids[None, :] < valid_frames[:, None]).astype(jnp.bfloat16)[:, :, None, None, None]
    mask_f = mask.astype(jnp.float32)
    masked = latents * mask
    cot = cotangent * mask
    first = tree_broadcast(masked[:, 0], "space")
    cot_local = jnp.sum(cot, axis=1, dtype=jnp.float32)
    later = shifted(cot, "space", -1)
    if lax.axis_size("space") % 2 == 0:
        cot_pair = cot_local + jnp.sum(later, axis=1, dtype=jnp.float32)
        if clips % 2 == 0 and lax.axis_size("space") >= 4:
            cot_sum = two_column_sum(cot_pair, cot_local, "space")
        else:
            cot_sum = tree_reduce(cot_pair, "space", 2)
    else:
        cot_sum = tree_reduce(cot_local, "space")
    rows_pad = row_halo(masked)
    padded = jnp.pad(rows_pad, ((0, 0), (0, 0), (0, 0), (1, 1), (0, 0)))
    pre = spatial_sum(padded, spatial_weight, False)
    act = jax.nn.silu(pre).astype(jnp.bfloat16)
    earlier = shifted(act, "space", 1)
    act_pad = jnp.concatenate([earlier, act], axis=1)
    mixed = lag_forward(act_pad, temporal_weight, frames)
    cot_pad = jnp.concatenate([cot, later], axis=1)
    dact = lag_backward(cot_pad, temporal_weight, frames)
    temporal_terms = lag_grads(act, cot_pad, frames)
    cond = jnp.dot(first, cond_weight, preferred_element_type=jnp.float32)
    output = ((masked.astype(jnp.float32) + mixed + cond[:, None]) * mask_f).astype(jnp.bfloat16)
    sig = jax.nn.sigmoid(pre)
    dpre = (dact * sig * (1.0 + pre * (1.0 - sig))).astype(jnp.bfloat16)
    cond_back = jnp.dot(cot_sum, cond_weight.astype(jnp.float32).T, precision=lax.Precision.HIGHEST)
    dpre_rows = row_halo(dpre)
    dpre_pad = jnp.pad(dpre_rows, ((0, 0), (0, 0), (0, 0), (1, 1), (0, 0)))
    dmasked = spatial_sum(dpre_pad, spatial_weight, True)
    is_first = (frame_ids == 0).astype(jnp.float32)[None, :, None, None, None]
    grad_latents = (
        (cot.astype(jnp.float32) + dmasked + is_first * cond_back[:, None]) * mask_f
    ).astype(jnp.bfloat16)
    dims = (((0, 1, 2, 3), (0, 1, 2, 3)), ((), ()))
    spatial_terms = []
    for row_off in range(3):
        for col_off in range(3):
            piece = padded[:, :, row_off : row_off + rows, col_off : col_off + cols]
            spatial_terms.append(
                lax.dot_general(piece, dpre, dims, preferred_element_type=jnp.float32)
            )
    spatial_terms = jnp.stack(spatial_terms)
    cond_terms = lax.dot_general(
        first.astype(jnp.float32),
        cot_local,
        (((0, 1, 2), (0, 1, 2)), ((), ())),
        precision=lax.Precision.HIGHEST,
    )
    taps_s = spatial_terms.shape[0]
    taps_t = temporal_terms.shape[0]
    flat = jnp.concatenate(
        [
            spatial_terms.reshape(-1, chans),
            temporal_terms.reshape(-1, chans),
            cond_terms.reshape(-1, chans),
        ],
        axis=0,
    )
    scale = (clips * frames * rows * cols * lax.axis_size("space") * lax.axis_size("tm")) ** (-0.5)
    summed = all_sum_rounded(flat, scale)
    n_s = taps_s * chans
    n_t = taps_t * chans
    grad_spatial, grad_temporal, grad_cond = split_rows(
        summed, [(0, n_s), (n_s, n_s + n_t), (n_s + n_t, n_s + n_t + chans)]
    )
    grad_spatial = grad_spatial.reshape(taps_s, chans, chans)
    grad_temporal = grad_temporal.reshape(taps_t, chans, chans)
    return (output, grad_latents, grad_spatial, grad_temporal, grad_cond)


def solution(mesh):
    return jax.shard_map(
        on_device,
        mesh=mesh,
        in_specs=(
            P("groups", "space", "tm", None, None),
            P("groups", "space", "tm", None, None),
            P("groups"),
            P(),
            P(),
            P(),
        ),
        out_specs=(
            P("groups", "space", "tm", None, None),
            P("groups", "space", "tm", None, None),
            P("groups", None, None),
            P("groups", None, None),
            P("groups", None),
        ),
        check_vma=False,
    )
```

```python
import jax
import jax.numpy as jnp
from jax import lax
from jax.sharding import PartitionSpec as P


def shifted(value, axis, by):
    count = lax.axis_size(axis)
    pairs = [(i, i + by) for i in range(count) if 0 <= i + by < count]
    return lax.ppermute(value, axis, pairs)


def tree_broadcast(value, axis):
    count = lax.axis_size(axis)
    me = lax.axis_index(axis)
    step = 1
    while step * 2 < count:
        step *= 2
    while step >= 1 and count > 1:
        pairs = [(i, i + step) for i in range(0, count, 2 * step) if i + step < count]
        got = lax.ppermute(value, axis, pairs)
        value = jnp.where(me % (2 * step) == step, got, value)
        step //= 2
    return value


def tree_broadcast_from(value, axis, unit):
    count = lax.axis_size(axis)
    me = lax.axis_index(axis)
    step = unit
    while step * 2 < count:
        step *= 2
    while step >= unit:
        pairs = [(i, i + step) for i in range(0, count, 2 * step) if i + step < count]
        got = lax.ppermute(value, axis, pairs)
        value = jnp.where(me % (2 * step) == step, got, value)
        step //= 2
    return value


def tree_reduce(value, axis, step=1):
    count = lax.axis_size(axis)
    while step < count:
        pairs = [(i + step, i) for i in range(0, count, 2 * step) if i + step < count]
        value = value + lax.ppermute(value, axis, pairs)
        step *= 2
    return value


def two_column_sum(pair, local, axis):
    count = lax.axis_size(axis)
    me = lax.axis_index(axis)
    half = pair.shape[0] // 2
    odd = me % 2 == 1
    value = jnp.where(odd, pair[half:], pair[:half])
    n = count // 2
    step = 1
    while step * 2 < n:
        step *= 2
    while step >= 1:
        pairs = []
        for i in range(n):
            if i < step and i + step < n:
                pairs.append((2 * (i + step), 2 * i))
                if 2 * (i + step) + 1 < count:
                    pairs.append((2 * (i + step) + 1, 2 * i + 1))
        value = value + lax.ppermute(value, axis, pairs)
        step //= 2
    got = lax.ppermute(value, axis, [(1, 0)])
    return jnp.concatenate([value, got + local[half:]], axis=0)


def xor_halving(flat, axis, steps):
    me = lax.axis_index(axis)
    count = lax.axis_size(axis)
    for step in steps:
        half = flat.shape[0] // 2
        upper = (me // step) % 2
        keep = lax.dynamic_slice_in_dim(flat, upper * half, half, 0)
        send = lax.dynamic_slice_in_dim(flat, (1 - upper) * half, half, 0)
        pairs = [(i, i ^ step) for i in range(count)]
        flat = keep + lax.ppermute(send, axis, pairs)
    return flat


def xor_doubling(piece, axis, steps):
    me = lax.axis_index(axis)
    count = lax.axis_size(axis)
    for step in reversed(steps):
        got = lax.ppermute(piece, axis, [(i, i ^ step) for i in range(count)])
        upper = (me // step) % 2 == 1
        piece = jnp.where(
            upper, jnp.concatenate([got, piece], 0), jnp.concatenate([piece, got], 0)
        )
    return piece


def direct_scatter(flat, axis, low, high):
    me = lax.axis_index(axis)
    j = me // low
    blk = flat.shape[0] // high
    total = lax.dynamic_slice_in_dim(flat, j * blk, blk, 0)
    for d in range(1, high):
        send = lax.dynamic_slice_in_dim(flat, ((j + d) % high) * blk, blk, 0)
        pairs = [
            (a * low + b, ((a + d) % high) * low + b) for a in range(high) for b in range(low)
        ]
        total = total + lax.ppermute(send, axis, pairs)
    return total


def direct_gather(piece, axis, low, high):
    me = lax.axis_index(axis)
    j = me // low
    out = jnp.zeros((high,) + piece.shape, piece.dtype)
    out = lax.dynamic_update_index_in_dim(out, piece, j, 0)
    for d in range(1, high):
        pairs = [
            (a * low + b, ((a + d) % high) * low + b) for a in range(high) for b in range(low)
        ]
        got = lax.ppermute(piece, axis, pairs)
        out = lax.dynamic_update_index_in_dim(out, got, (j - d) % high, 0)
    return out.reshape((-1,) + piece.shape[1:])


def is_pow2(n):
    return n >= 1 and (n & (n - 1)) == 0


def all_sum_rounded(flat, scale):
    n_tm = lax.axis_size("tm")
    n_sp = lax.axis_size("space")
    if not (is_pow2(n_tm) and is_pow2(n_sp)):
        return (lax.psum(flat, ("tm", "space")) * scale).astype(jnp.bfloat16), [], flat.shape[0]
    high = min(4, n_sp)
    low = n_sp // high
    tm_steps = []
    s = 1
    while s < n_tm:
        tm_steps.append(s)
        s *= 2
    sp_steps = []
    s = 1
    while s < low:
        sp_steps.append(s)
        s *= 2
    rows = flat.shape[0]
    unit = n_tm * n_sp * 8
    padded_rows = -(-rows // unit) * unit
    if padded_rows != rows:
        flat = jnp.pad(flat, ((0, padded_rows - rows), (0, 0)))
    flat = xor_halving(flat, "tm", tm_steps)
    flat = xor_halving(flat, "space", sp_steps)
    flat = direct_scatter(flat, "space", low, high)
    piece = (flat * scale).astype(jnp.bfloat16)
    piece = direct_gather(piece, "space", low, high)
    piece = xor_doubling(piece, "space", sp_steps)
    return piece, tm_steps, rows


def split_rows(gathered, cuts):
    piece, tm_steps, rows = gathered
    if len(tm_steps) != 1:
        whole = xor_doubling(piece, "tm", tm_steps)
        return [whole[a:b] for a, b in cuts]
    me = lax.axis_index("tm")
    got = lax.ppermute(piece, "tm", [(0, 1), (1, 0)])
    lower = jnp.where(me == 0, piece, got)
    upper = jnp.where(me == 0, got, piece)
    half = piece.shape[0]
    outs = []
    for a, b in cuts:
        parts = []
        if a < half:
            parts.append(lower[a : min(b, half)])
        if b > half:
            parts.append(upper[max(a, half) - half : b - half])
        outs.append(parts[0] if len(parts) == 1 else jnp.concatenate(parts, 0))
    return outs


def spatial_sum(padded, weights, flip):
    rows = padded.shape[2] - 2
    cols = padded.shape[3] - 2
    total = jnp.zeros(padded.shape[:2] + (rows, cols, weights.shape[2]), jnp.float32)
    for row_off in range(3):
        for col_off in range(3):
            if flip:
                piece = padded[
                    :, :, 2 - row_off : 2 - row_off + rows, 2 - col_off : 2 - col_off + cols
                ]
                kernel = weights[3 * row_off + col_off].T
            else:
                piece = padded[:, :, row_off : row_off + rows, col_off : col_off + cols]
                kernel = weights[3 * row_off + col_off]
            total = total + jnp.dot(piece, kernel, preferred_element_type=jnp.float32)
    return total


def lag_forward(padded_act, weights, count):
    total = 0.0
    for lag in range(3):
        total = total + jnp.dot(
            padded_act[:, 2 - lag : 2 - lag + count],
            weights[lag],
            preferred_element_type=jnp.float32,
        )
    return total


def lag_backward(padded_cot, weights, count):
    total = 0.0
    for lag in range(3):
        total = total + jnp.dot(
            padded_cot[:, lag : lag + count], weights[lag].T, preferred_element_type=jnp.float32
        )
    return total


def lag_grads(act, padded_cot, count):
    dims = (((0, 1, 2, 3), (0, 1, 2, 3)), ((), ()))
    terms = []
    for lag in range(3):
        terms.append(
            lax.dot_general(
                act,
                padded_cot[:, lag : lag + count],
                dims,
                preferred_element_type=jnp.float32,
            )
        )
    return jnp.stack(terms)


def row_halo(x):
    if lax.axis_size("tm") == 2:
        me = lax.axis_index("tm")
        edge = jnp.where(me == 0, x[:, :, -1:], x[:, :, :1])
        got = lax.ppermute(edge, "tm", [(0, 1), (1, 0)])
        zero = jnp.zeros_like(got)
        above = jnp.where(me == 1, got, zero)
        below = jnp.where(me == 0, got, zero)
        return jnp.concatenate([above, x, below], axis=2)
    above = shifted(x[:, :, -1:], "tm", 1)
    below = shifted(x[:, :, :1], "tm", -1)
    return jnp.concatenate([above, x, below], axis=2)


def on_device(latents, cotangent, valid_frames, spatial_weight, temporal_weight, cond_weight):
    clips, frames, rows, cols, chans = latents.shape
    slab = lax.axis_index("space")
    frame_ids = slab * frames + jnp.arange(frames, dtype=jnp.int32)
    mask = (frame_ids[None, :] < valid_frames[:, None]).astype(jnp.bfloat16)[:, :, None, None, None]
    mask_f = mask.astype(jnp.float32)
    masked = latents * mask
    cot = cotangent * mask
    paired = lax.axis_size("space") % 2 == 0
    if paired:
        first_even = tree_broadcast_from(masked[:, 0], "space", 2)
        hop = lax.ppermute(
            first_even, "space", [(i, i + 1) for i in range(0, lax.axis_size("space"), 2)]
        )
        first = jnp.where(slab % 2 == 1, hop, first_even)
    else:
        first = tree_broadcast(masked[:, 0], "space")
    cot_local = jnp.sum(cot, axis=1, dtype=jnp.float32)
    later = shifted(cot, "space", -1)
    if lax.axis_size("space") % 2 == 0:
        cot_pair = cot_local + jnp.sum(later, axis=1, dtype=jnp.float32)
        if clips % 2 == 0 and lax.axis_size("space") >= 4:
            cot_sum = two_column_sum(cot_pair, cot_local, "space")
        else:
            cot_sum = tree_reduce(cot_pair, "space", 2)
    else:
        cot_sum = tree_reduce(cot_local, "space")
    rows_pad = row_halo(masked)
    padded = jnp.pad(rows_pad, ((0, 0), (0, 0), (0, 0), (1, 1), (0, 0)))
    pre = spatial_sum(padded, spatial_weight, False)
    act = jax.nn.silu(pre).astype(jnp.bfloat16)
    earlier = shifted(act, "space", 1)
    act_pad = jnp.concatenate([earlier, act], axis=1)
    mixed = lag_forward(act_pad, temporal_weight, frames)
    cot_pad = jnp.concatenate([cot, later], axis=1)
    dact = lag_backward(cot_pad, temporal_weight, frames)
    temporal_terms = lag_grads(act, cot_pad, frames)
    cond = jnp.dot(first, cond_weight, preferred_element_type=jnp.float32)
    output = ((masked.astype(jnp.float32) + mixed + cond[:, None]) * mask_f).astype(jnp.bfloat16)
    sig = jax.nn.sigmoid(pre)
    dpre = (dact * sig * (1.0 + pre * (1.0 - sig))).astype(jnp.bfloat16)
    cond_back = jnp.dot(cot_sum, cond_weight.astype(jnp.float32).T, precision=lax.Precision.HIGHEST)
    dpre_rows = row_halo(dpre)
    dpre_pad = jnp.pad(dpre_rows, ((0, 0), (0, 0), (0, 0), (1, 1), (0, 0)))
    dmasked = spatial_sum(dpre_pad, spatial_weight, True)
    is_first = (frame_ids == 0).astype(jnp.float32)[None, :, None, None, None]
    grad_latents = (
        (cot.astype(jnp.float32) + dmasked + is_first * cond_back[:, None]) * mask_f
    ).astype(jnp.bfloat16)
    dims = (((0, 1, 2, 3), (0, 1, 2, 3)), ((), ()))
    spatial_terms = []
    for row_off in range(3):
        for col_off in range(3):
            piece = padded[:, :, row_off : row_off + rows, col_off : col_off + cols]
            spatial_terms.append(
                lax.dot_general(piece, dpre, dims, preferred_element_type=jnp.float32)
            )
    spatial_terms = jnp.stack(spatial_terms)
    if paired:
        cond_lhs = first_even.astype(jnp.float32)
        cond_rhs = cot_pair * (slab % 2 == 0).astype(jnp.float32)
    else:
        cond_lhs = first.astype(jnp.float32)
        cond_rhs = cot_local
    cond_terms = lax.dot_general(
        cond_lhs,
        cond_rhs,
        (((0, 1, 2), (0, 1, 2)), ((), ())),
        precision=lax.Precision.HIGHEST,
    )
    taps_s = spatial_terms.shape[0]
    taps_t = temporal_terms.shape[0]
    flat = jnp.concatenate(
        [
            spatial_terms.reshape(-1, chans),
            temporal_terms.reshape(-1, chans),
            cond_terms.reshape(-1, chans),
        ],
        axis=0,
    )
    scale = (clips * frames * rows * cols * lax.axis_size("space") * lax.axis_size("tm")) ** (-0.5)
    summed = all_sum_rounded(flat, scale)
    n_s = taps_s * chans
    n_t = taps_t * chans
    grad_spatial, grad_temporal, grad_cond = split_rows(
        summed, [(0, n_s), (n_s, n_s + n_t), (n_s + n_t, n_s + n_t + chans)]
    )
    grad_spatial = grad_spatial.reshape(taps_s, chans, chans)
    grad_temporal = grad_temporal.reshape(taps_t, chans, chans)
    return (output, grad_latents, grad_spatial, grad_temporal, grad_cond)


def solution(mesh):
    return jax.shard_map(
        on_device,
        mesh=mesh,
        in_specs=(
            P("groups", "space", "tm", None, None),
            P("groups", "space", "tm", None, None),
            P("groups"),
            P(),
            P(),
            P(),
        ),
        out_specs=(
            P("groups", "space", "tm", None, None),
            P("groups", "space", "tm", None, None),
            P("groups", None, None),
            P("groups", None, None),
            P("groups", None),
        ),
        check_vma=False,
    )
```

```python
import jax
import jax.numpy as jnp
from jax import lax
from jax.sharding import PartitionSpec as P


def shifted(value, axis, by):
    count = lax.axis_size(axis)
    pairs = [(i, i + by) for i in range(count) if 0 <= i + by < count]
    return lax.ppermute(value, axis, pairs)


def tree_broadcast(value, axis):
    count = lax.axis_size(axis)
    me = lax.axis_index(axis)
    step = 1
    while step * 2 < count:
        step *= 2
    while step >= 1 and count > 1:
        pairs = [(i, i + step) for i in range(0, count, 2 * step) if i + step < count]
        got = lax.ppermute(value, axis, pairs)
        value = jnp.where(me % (2 * step) == step, got, value)
        step //= 2
    return value


def even_first_broadcast(value, axis):
    count = lax.axis_size(axis)
    me = lax.axis_index(axis)
    step = 2
    while step < count:
        pairs = [(i, i + step) for i in range(0, step, 2) if i + step < count]
        got = lax.ppermute(value, axis, pairs)
        value = jnp.where((me >= step) & (me < 2 * step) & (me % 2 == 0), got, value)
        step *= 2
    got = lax.ppermute(value, axis, [(i, i + 1) for i in range(0, count, 2)])
    return jnp.where(me % 2 == 1, got, value)


def tree_reduce(value, axis, step=1):
    count = lax.axis_size(axis)
    while step < count:
        pairs = [(i + step, i) for i in range(0, count, 2 * step) if i + step < count]
        value = value + lax.ppermute(value, axis, pairs)
        step *= 2
    return value


def two_column_sum(pair, local, axis):
    count = lax.axis_size(axis)
    me = lax.axis_index(axis)
    half = pair.shape[0] // 2
    odd = me % 2 == 1
    value = jnp.where(odd, pair[half:], pair[:half])
    n = count // 2
    step = 1
    while step * 2 < n:
        step *= 2
    while step >= 1:
        pairs = []
        for i in range(n):
            if i < step and i + step < n:
                pairs.append((2 * (i + step), 2 * i))
                if 2 * (i + step) + 1 < count:
                    pairs.append((2 * (i + step) + 1, 2 * i + 1))
        value = value + lax.ppermute(value, axis, pairs)
        step //= 2
    got = lax.ppermute(value, axis, [(1, 0)])
    return jnp.concatenate([value, got + local[half:]], axis=0)


def xor_halving(flat, axis, steps):
    me = lax.axis_index(axis)
    count = lax.axis_size(axis)
    for step in steps:
        half = flat.shape[0] // 2
        upper = (me // step) % 2
        keep = lax.dynamic_slice_in_dim(flat, upper * half, half, 0)
        send = lax.dynamic_slice_in_dim(flat, (1 - upper) * half, half, 0)
        pairs = [(i, i ^ step) for i in range(count)]
        flat = keep + lax.ppermute(send, axis, pairs)
    return flat


def xor_doubling(piece, axis, steps):
    me = lax.axis_index(axis)
    count = lax.axis_size(axis)
    for step in reversed(steps):
        got = lax.ppermute(piece, axis, [(i, i ^ step) for i in range(count)])
        upper = (me // step) % 2 == 1
        piece = jnp.where(
            upper, jnp.concatenate([got, piece], 0), jnp.concatenate([piece, got], 0)
        )
    return piece


def direct_scatter(flat, axis, low, high):
    me = lax.axis_index(axis)
    j = me // low
    blk = flat.shape[0] // high
    total = lax.dynamic_slice_in_dim(flat, j * blk, blk, 0)
    for d in range(1, high):
        send = lax.dynamic_slice_in_dim(flat, ((j + d) % high) * blk, blk, 0)
        pairs = [
            (a * low + b, ((a + d) % high) * low + b) for a in range(high) for b in range(low)
        ]
        total = total + lax.ppermute(send, axis, pairs)
    return total


def direct_gather(piece, axis, low, high):
    me = lax.axis_index(axis)
    j = me // low
    out = jnp.zeros((high,) + piece.shape, piece.dtype)
    out = lax.dynamic_update_index_in_dim(out, piece, j, 0)
    for d in range(1, high):
        pairs = [
            (a * low + b, ((a + d) % high) * low + b) for a in range(high) for b in range(low)
        ]
        got = lax.ppermute(piece, axis, pairs)
        out = lax.dynamic_update_index_in_dim(out, got, (j - d) % high, 0)
    return out.reshape((-1,) + piece.shape[1:])


def is_pow2(n):
    return n >= 1 and (n & (n - 1)) == 0


def all_sum_rounded(flat, scale):
    n_tm = lax.axis_size("tm")
    n_sp = lax.axis_size("space")
    if not (is_pow2(n_tm) and is_pow2(n_sp)):
        return (lax.psum(flat, ("tm", "space")) * scale).astype(jnp.bfloat16), [], flat.shape[0]
    high = min(4, n_sp)
    low = n_sp // high
    tm_steps = []
    s = 1
    while s < n_tm:
        tm_steps.append(s)
        s *= 2
    sp_steps = []
    s = 1
    while s < low:
        sp_steps.append(s)
        s *= 2
    rows = flat.shape[0]
    unit = n_tm * n_sp * 8
    padded_rows = -(-rows // unit) * unit
    if padded_rows != rows:
        flat = jnp.pad(flat, ((0, padded_rows - rows), (0, 0)))
    flat = xor_halving(flat, "tm", tm_steps)
    flat = xor_halving(flat, "space", sp_steps)
    flat = direct_scatter(flat, "space", low, high)
    piece = (flat * scale).astype(jnp.bfloat16)
    piece = direct_gather(piece, "space", low, high)
    piece = xor_doubling(piece, "space", sp_steps)
    return piece, tm_steps, rows


def split_rows(gathered, cuts):
    piece, tm_steps, rows = gathered
    if len(tm_steps) != 1:
        whole = xor_doubling(piece, "tm", tm_steps)
        return [whole[a:b] for a, b in cuts]
    me = lax.axis_index("tm")
    got = lax.ppermute(piece, "tm", [(0, 1), (1, 0)])
    lower = jnp.where(me == 0, piece, got)
    upper = jnp.where(me == 0, got, piece)
    half = piece.shape[0]
    outs = []
    for a, b in cuts:
        parts = []
        if a < half:
            parts.append(lower[a : min(b, half)])
        if b > half:
            parts.append(upper[max(a, half) - half : b - half])
        outs.append(parts[0] if len(parts) == 1 else jnp.concatenate(parts, 0))
    return outs


def spatial_sum(padded, weights, flip):
    rows = padded.shape[2] - 2
    cols = padded.shape[3] - 2
    total = jnp.zeros(padded.shape[:2] + (rows, cols, weights.shape[2]), jnp.float32)
    for row_off in range(3):
        for col_off in range(3):
            if flip:
                piece = padded[
                    :, :, 2 - row_off : 2 - row_off + rows, 2 - col_off : 2 - col_off + cols
                ]
                kernel = weights[3 * row_off + col_off].T
            else:
                piece = padded[:, :, row_off : row_off + rows, col_off : col_off + cols]
                kernel = weights[3 * row_off + col_off]
            total = total + jnp.dot(piece, kernel, preferred_element_type=jnp.float32)
    return total


def lag_forward(padded_act, weights, count):
    total = 0.0
    for lag in range(3):
        total = total + jnp.dot(
            padded_act[:, 2 - lag : 2 - lag + count],
            weights[lag],
            preferred_element_type=jnp.float32,
        )
    return total


def lag_backward(padded_cot, weights, count):
    total = 0.0
    for lag in range(3):
        total = total + jnp.dot(
            padded_cot[:, lag : lag + count], weights[lag].T, preferred_element_type=jnp.float32
        )
    return total


def lag_grads(act, padded_cot, count):
    dims = (((0, 1, 2, 3), (0, 1, 2, 3)), ((), ()))
    terms = []
    for lag in range(3):
        terms.append(
            lax.dot_general(
                act,
                padded_cot[:, lag : lag + count],
                dims,
                preferred_element_type=jnp.float32,
            )
        )
    return jnp.stack(terms)


def row_halo(x):
    if lax.axis_size("tm") == 2:
        me = lax.axis_index("tm")
        edge = jnp.where(me == 0, x[:, :, -1:], x[:, :, :1])
        got = lax.ppermute(edge, "tm", [(0, 1), (1, 0)])
        zero = jnp.zeros_like(got)
        above = jnp.where(me == 1, got, zero)
        below = jnp.where(me == 0, got, zero)
        return jnp.concatenate([above, x, below], axis=2)
    above = shifted(x[:, :, -1:], "tm", 1)
    below = shifted(x[:, :, :1], "tm", -1)
    return jnp.concatenate([above, x, below], axis=2)


def on_device(latents, cotangent, valid_frames, spatial_weight, temporal_weight, cond_weight):
    clips, frames, rows, cols, chans = latents.shape
    slab = lax.axis_index("space")
    frame_ids = slab * frames + jnp.arange(frames, dtype=jnp.int32)
    mask = (frame_ids[None, :] < valid_frames[:, None]).astype(jnp.bfloat16)[:, :, None, None, None]
    mask_f = mask.astype(jnp.float32)
    masked = latents * mask
    cot = cotangent * mask
    if lax.axis_size("space") % 2 == 0:
        first = even_first_broadcast(masked[:, 0], "space")
    else:
        first = tree_broadcast(masked[:, 0], "space")
    cot_local = jnp.sum(cot, axis=1, dtype=jnp.float32)
    later = shifted(cot, "space", -1)
    if lax.axis_size("space") % 2 == 0:
        cot_pair = cot_local + jnp.sum(later, axis=1, dtype=jnp.float32)
        if clips % 2 == 0 and lax.axis_size("space") >= 4:
            cot_sum = two_column_sum(cot_pair, cot_local, "space")
        else:
            cot_sum = tree_reduce(cot_pair, "space", 2)
    else:
        cot_sum = tree_reduce(cot_local, "space")
    rows_pad = row_halo(masked)
    padded = jnp.pad(rows_pad, ((0, 0), (0, 0), (0, 0), (1, 1), (0, 0)))
    pre = spatial_sum(padded, spatial_weight, False)
    act = jax.nn.silu(pre).astype(jnp.bfloat16)
    earlier = shifted(act, "space", 1)
    act_pad = jnp.concatenate([earlier, act], axis=1)
    mixed = lag_forward(act_pad, temporal_weight, frames)
    cot_pad = jnp.concatenate([cot, later], axis=1)
    dact = lag_backward(cot_pad, temporal_weight, frames)
    temporal_terms = lag_grads(act, cot_pad, frames)
    cond = jnp.dot(first, cond_weight, preferred_element_type=jnp.float32)
    output = ((masked.astype(jnp.float32) + mixed + cond[:, None]) * mask_f).astype(jnp.bfloat16)
    sig = jax.nn.sigmoid(pre)
    dpre = (dact * sig * (1.0 + pre * (1.0 - sig))).astype(jnp.bfloat16)
    cond_back = jnp.dot(cot_sum, cond_weight.astype(jnp.float32).T, precision=lax.Precision.HIGHEST)
    dpre_rows = row_halo(dpre)
    dpre_pad = jnp.pad(dpre_rows, ((0, 0), (0, 0), (0, 0), (1, 1), (0, 0)))
    dmasked = spatial_sum(dpre_pad, spatial_weight, True)
    is_first = (frame_ids == 0).astype(jnp.float32)[None, :, None, None, None]
    grad_latents = (
        (cot.astype(jnp.float32) + dmasked + is_first * cond_back[:, None]) * mask_f
    ).astype(jnp.bfloat16)
    dims = (((0, 1, 2, 3), (0, 1, 2, 3)), ((), ()))
    spatial_terms = []
    for row_off in range(3):
        for col_off in range(3):
            piece = padded[:, :, row_off : row_off + rows, col_off : col_off + cols]
            spatial_terms.append(
                lax.dot_general(piece, dpre, dims, preferred_element_type=jnp.float32)
            )
    spatial_terms = jnp.stack(spatial_terms)
    cond_terms = lax.dot_general(
        first.astype(jnp.float32),
        cot_local,
        (((0, 1, 2), (0, 1, 2)), ((), ())),
        precision=lax.Precision.HIGHEST,
    )
    taps_s = spatial_terms.shape[0]
    taps_t = temporal_terms.shape[0]
    flat = jnp.concatenate(
        [
            spatial_terms.reshape(-1, chans),
            temporal_terms.reshape(-1, chans),
            cond_terms.reshape(-1, chans),
        ],
        axis=0,
    )
    scale = (clips * frames * rows * cols * lax.axis_size("space") * lax.axis_size("tm")) ** (-0.5)
    summed = all_sum_rounded(flat, scale)
    n_s = taps_s * chans
    n_t = taps_t * chans
    grad_spatial, grad_temporal, grad_cond = split_rows(
        summed, [(0, n_s), (n_s, n_s + n_t), (n_s + n_t, n_s + n_t + chans)]
    )
    grad_spatial = grad_spatial.reshape(taps_s, chans, chans)
    grad_temporal = grad_temporal.reshape(taps_t, chans, chans)
    return (output, grad_latents, grad_spatial, grad_temporal, grad_cond)


def solution(mesh):
    return jax.shard_map(
        on_device,
        mesh=mesh,
        in_specs=(
            P("groups", "space", "tm", None, None),
            P("groups", "space", "tm", None, None),
            P("groups"),
            P(),
            P(),
            P(),
        ),
        out_specs=(
            P("groups", "space", "tm", None, None),
            P("groups", "space", "tm", None, None),
            P("groups", None, None),
            P("groups", None, None),
            P("groups", None),
        ),
        check_vma=False,
    )
```

```python
import jax
import jax.numpy as jnp
from jax import lax
from jax.sharding import PartitionSpec as P


def shifted(value, axis, by):
    count = lax.axis_size(axis)
    pairs = [(i, i + by) for i in range(count) if 0 <= i + by < count]
    return lax.ppermute(value, axis, pairs)


def tree_broadcast(value, axis):
    count = lax.axis_size(axis)
    me = lax.axis_index(axis)
    step = 1
    while step * 2 < count:
        step *= 2
    while step >= 1 and count > 1:
        pairs = [(i, i + step) for i in range(0, count, 2 * step) if i + step < count]
        got = lax.ppermute(value, axis, pairs)
        value = jnp.where(me % (2 * step) == step, got, value)
        step //= 2
    return value


def tree_reduce(value, axis, step=1):
    count = lax.axis_size(axis)
    while step < count:
        pairs = [(i + step, i) for i in range(0, count, 2 * step) if i + step < count]
        value = value + lax.ppermute(value, axis, pairs)
        step *= 2
    return value


def two_column_sum(pair, local, axis):
    count = lax.axis_size(axis)
    me = lax.axis_index(axis)
    half = pair.shape[0] // 2
    odd = me % 2 == 1
    value = jnp.where(odd, pair[half:], pair[:half])
    n = count // 2
    step = 1
    while step * 2 < n:
        step *= 2
    while step >= 1:
        pairs = []
        for i in range(n):
            if i < step and i + step < n:
                pairs.append((2 * (i + step), 2 * i))
                if 2 * (i + step) + 1 < count:
                    pairs.append((2 * (i + step) + 1, 2 * i + 1))
        value = value + lax.ppermute(value, axis, pairs)
        step //= 2
    got = lax.ppermute(value, axis, [(1, 0)])
    return jnp.concatenate([value, got + local[half:]], axis=0)


def xor_halving(flat, axis, steps):
    me = lax.axis_index(axis)
    count = lax.axis_size(axis)
    for step in steps:
        half = flat.shape[0] // 2
        upper = (me // step) % 2
        keep = lax.dynamic_slice_in_dim(flat, upper * half, half, 0)
        send = lax.dynamic_slice_in_dim(flat, (1 - upper) * half, half, 0)
        pairs = [(i, i ^ step) for i in range(count)]
        flat = keep + lax.ppermute(send, axis, pairs)
    return flat


def xor_doubling(piece, axis, steps):
    me = lax.axis_index(axis)
    count = lax.axis_size(axis)
    for step in reversed(steps):
        got = lax.ppermute(piece, axis, [(i, i ^ step) for i in range(count)])
        upper = (me // step) % 2 == 1
        piece = jnp.where(
            upper, jnp.concatenate([got, piece], 0), jnp.concatenate([piece, got], 0)
        )
    return piece


def direct_scatter(flat, axis, low, high):
    me = lax.axis_index(axis)
    j = me // low
    blk = flat.shape[0] // high
    total = lax.dynamic_slice_in_dim(flat, j * blk, blk, 0)
    for d in sorted(range(1, high), key=lambda d: -min(d, high - d)):
        send = lax.dynamic_slice_in_dim(flat, ((j + d) % high) * blk, blk, 0)
        pairs = [
            (a * low + b, ((a + d) % high) * low + b) for a in range(high) for b in range(low)
        ]
        total = total + lax.ppermute(send, axis, pairs)
    return total


def direct_gather(piece, axis, low, high):
    me = lax.axis_index(axis)
    j = me // low
    out = jnp.zeros((high,) + piece.shape, piece.dtype)
    out = lax.dynamic_update_index_in_dim(out, piece, j, 0)
    for d in sorted(range(1, high), key=lambda d: -min(d, high - d)):
        pairs = [
            (a * low + b, ((a + d) % high) * low + b) for a in range(high) for b in range(low)
        ]
        got = lax.ppermute(piece, axis, pairs)
        out = lax.dynamic_update_index_in_dim(out, got, (j - d) % high, 0)
    return out.reshape((-1,) + piece.shape[1:])


def is_pow2(n):
    return n >= 1 and (n & (n - 1)) == 0


def all_sum_rounded(flat, scale):
    n_tm = lax.axis_size("tm")
    n_sp = lax.axis_size("space")
    if not (is_pow2(n_tm) and is_pow2(n_sp)):
        return (lax.psum(flat, ("tm", "space")) * scale).astype(jnp.bfloat16), [], flat.shape[0]
    high = min(4, n_sp)
    low = n_sp // high
    tm_steps = []
    s = 1
    while s < n_tm:
        tm_steps.append(s)
        s *= 2
    sp_steps = []
    s = 1
    while s < low:
        sp_steps.append(s)
        s *= 2
    rows = flat.shape[0]
    unit = n_tm * n_sp * 8
    padded_rows = -(-rows // unit) * unit
    if padded_rows != rows:
        flat = jnp.pad(flat, ((0, padded_rows - rows), (0, 0)))
    flat = xor_halving(flat, "tm", tm_steps)
    flat = xor_halving(flat, "space", sp_steps)
    flat = direct_scatter(flat, "space", low, high)
    piece = (flat * scale).astype(jnp.bfloat16)
    piece = direct_gather(piece, "space", low, high)
    piece = xor_doubling(piece, "space", sp_steps)
    return piece, tm_steps, rows


def split_rows(gathered, cuts):
    piece, tm_steps, rows = gathered
    if len(tm_steps) != 1:
        whole = xor_doubling(piece, "tm", tm_steps)
        return [whole[a:b] for a, b in cuts]
    me = lax.axis_index("tm")
    got = lax.ppermute(piece, "tm", [(0, 1), (1, 0)])
    lower = jnp.where(me == 0, piece, got)
    upper = jnp.where(me == 0, got, piece)
    half = piece.shape[0]
    outs = []
    for a, b in cuts:
        parts = []
        if a < half:
            parts.append(lower[a : min(b, half)])
        if b > half:
            parts.append(upper[max(a, half) - half : b - half])
        outs.append(parts[0] if len(parts) == 1 else jnp.concatenate(parts, 0))
    return outs


def spatial_sum(padded, weights, flip):
    rows = padded.shape[2] - 2
    cols = padded.shape[3] - 2
    total = jnp.zeros(padded.shape[:2] + (rows, cols, weights.shape[2]), jnp.float32)
    for row_off in range(3):
        for col_off in range(3):
            if flip:
                piece = padded[
                    :, :, 2 - row_off : 2 - row_off + rows, 2 - col_off : 2 - col_off + cols
                ]
                kernel = weights[3 * row_off + col_off].T
            else:
                piece = padded[:, :, row_off : row_off + rows, col_off : col_off + cols]
                kernel = weights[3 * row_off + col_off]
            total = total + jnp.dot(piece, kernel, preferred_element_type=jnp.float32)
    return total


def lag_forward(padded_act, weights, count):
    total = 0.0
    for lag in range(3):
        total = total + jnp.dot(
            padded_act[:, 2 - lag : 2 - lag + count],
            weights[lag],
            preferred_element_type=jnp.float32,
        )
    return total


def lag_backward(padded_cot, weights, count):
    total = 0.0
    for lag in range(3):
        total = total + jnp.dot(
            padded_cot[:, lag : lag + count], weights[lag].T, preferred_element_type=jnp.float32
        )
    return total


def lag_grads(act, padded_cot, count):
    dims = (((0, 1, 2, 3), (0, 1, 2, 3)), ((), ()))
    terms = []
    for lag in range(3):
        terms.append(
            lax.dot_general(
                act,
                padded_cot[:, lag : lag + count],
                dims,
                preferred_element_type=jnp.float32,
            )
        )
    return jnp.stack(terms)


def row_halo(x):
    if lax.axis_size("tm") == 2:
        me = lax.axis_index("tm")
        edge = jnp.where(me == 0, x[:, :, -1:], x[:, :, :1])
        got = lax.ppermute(edge, "tm", [(0, 1), (1, 0)])
        zero = jnp.zeros_like(got)
        above = jnp.where(me == 1, got, zero)
        below = jnp.where(me == 0, got, zero)
        return jnp.concatenate([above, x, below], axis=2)
    above = shifted(x[:, :, -1:], "tm", 1)
    below = shifted(x[:, :, :1], "tm", -1)
    return jnp.concatenate([above, x, below], axis=2)


def on_device(latents, cotangent, valid_frames, spatial_weight, temporal_weight, cond_weight):
    clips, frames, rows, cols, chans = latents.shape
    slab = lax.axis_index("space")
    frame_ids = slab * frames + jnp.arange(frames, dtype=jnp.int32)
    mask = (frame_ids[None, :] < valid_frames[:, None]).astype(jnp.bfloat16)[:, :, None, None, None]
    mask_f = mask.astype(jnp.float32)
    masked = latents * mask
    cot = cotangent * mask
    first = tree_broadcast(masked[:, 0], "space")
    cot_local = jnp.sum(cot, axis=1, dtype=jnp.float32)
    later = shifted(cot, "space", -1)
    if lax.axis_size("space") % 2 == 0:
        cot_pair = cot_local + jnp.sum(later, axis=1, dtype=jnp.float32)
        if clips % 2 == 0 and lax.axis_size("space") >= 4:
            cot_sum = two_column_sum(cot_pair, cot_local, "space")
        else:
            cot_sum = tree_reduce(cot_pair, "space", 2)
    else:
        cot_sum = tree_reduce(cot_local, "space")
    rows_pad = row_halo(masked)
    padded = jnp.pad(rows_pad, ((0, 0), (0, 0), (0, 0), (1, 1), (0, 0)))
    pre = spatial_sum(padded, spatial_weight, False)
    act = jax.nn.silu(pre).astype(jnp.bfloat16)
    earlier = shifted(act, "space", 1)
    act_pad = jnp.concatenate([earlier, act], axis=1)
    mixed = lag_forward(act_pad, temporal_weight, frames)
    cot_pad = jnp.concatenate([cot, later], axis=1)
    dact = lag_backward(cot_pad, temporal_weight, frames)
    temporal_terms = lag_grads(act, cot_pad, frames)
    cond = jnp.dot(first, cond_weight, preferred_element_type=jnp.float32)
    output = ((masked.astype(jnp.float32) + mixed + cond[:, None]) * mask_f).astype(jnp.bfloat16)
    sig = jax.nn.sigmoid(pre)
    dpre = (dact * sig * (1.0 + pre * (1.0 - sig))).astype(jnp.bfloat16)
    cond_back = jnp.dot(cot_sum, cond_weight.astype(jnp.float32).T, precision=lax.Precision.HIGHEST)
    dpre_rows = row_halo(dpre)
    dpre_pad = jnp.pad(dpre_rows, ((0, 0), (0, 0), (0, 0), (1, 1), (0, 0)))
    dmasked = spatial_sum(dpre_pad, spatial_weight, True)
    is_first = (frame_ids == 0).astype(jnp.float32)[None, :, None, None, None]
    grad_latents = (
        (cot.astype(jnp.float32) + dmasked + is_first * cond_back[:, None]) * mask_f
    ).astype(jnp.bfloat16)
    dims = (((0, 1, 2, 3), (0, 1, 2, 3)), ((), ()))
    spatial_terms = []
    for row_off in range(3):
        for col_off in range(3):
            piece = padded[:, :, row_off : row_off + rows, col_off : col_off + cols]
            spatial_terms.append(
                lax.dot_general(piece, dpre, dims, preferred_element_type=jnp.float32)
            )
    spatial_terms = jnp.stack(spatial_terms)
    cond_terms = lax.dot_general(
        first.astype(jnp.float32),
        cot_local,
        (((0, 1, 2), (0, 1, 2)), ((), ())),
        precision=lax.Precision.HIGHEST,
    )
    taps_s = spatial_terms.shape[0]
    taps_t = temporal_terms.shape[0]
    flat = jnp.concatenate(
        [
            spatial_terms.reshape(-1, chans),
            temporal_terms.reshape(-1, chans),
            cond_terms.reshape(-1, chans),
        ],
        axis=0,
    )
    scale = (clips * frames * rows * cols * lax.axis_size("space") * lax.axis_size("tm")) ** (-0.5)
    summed = all_sum_rounded(flat, scale)
    n_s = taps_s * chans
    n_t = taps_t * chans
    grad_spatial, grad_temporal, grad_cond = split_rows(
        summed, [(0, n_s), (n_s, n_s + n_t), (n_s + n_t, n_s + n_t + chans)]
    )
    grad_spatial = grad_spatial.reshape(taps_s, chans, chans)
    grad_temporal = grad_temporal.reshape(taps_t, chans, chans)
    return (output, grad_latents, grad_spatial, grad_temporal, grad_cond)


def solution(mesh):
    return jax.shard_map(
        on_device,
        mesh=mesh,
        in_specs=(
            P("groups", "space", "tm", None, None),
            P("groups", "space", "tm", None, None),
            P("groups"),
            P(),
            P(),
            P(),
        ),
        out_specs=(
            P("groups", "space", "tm", None, None),
            P("groups", "space", "tm", None, None),
            P("groups", None, None),
            P("groups", None, None),
            P("groups", None),
        ),
        check_vma=False,
    )
```
